32 devices in a mesh: probe: 2 (over x), space: 16 (over z, y, core).
Axes of the slice: x: 2, y: 2, z: 4, core: 2. Of those that a mesh axis runs over, the one named last changes fastest.
Arguments:
- cos_polar: float32 [4, 64, 128], P(None, 'space', 'probe'), may hold values from -1 to 1
- azimuth: float32 [4, 64, 128], P(None, 'space', 'probe'), may hold values from -3.140625 to 3.140625
- bond_class: int32 [3, 4, 64, 128], P(None, None, 'space', 'probe'), may hold values from 0 to 7
- exchange: float32 [8], replicated, may hold values from -1 to 1
- probe_wave: int32 [16, 3], P('probe'), may hold values from 0 to 63
Outputs:
- relaxed: float32 [3, 4, 64, 128], P(None, None, 'space', 'probe')
- cheb_last: bfloat16 [16, 2, 3, 4, 64, 128], P('probe', None, None, None, 'space')
- moments: float32 [16, 4], P('probe')
The draws below stay inside these ranges and needn't reach their ends.
All inputs are finite; a program needn't handle non-finite values.
Results may differ from the reference program's by a relative error of at most 0.001.
Values sent between devices are 32-bit elements; how exact they have to be, the bound alone decides.
No kernel may reach another device: no remote copies, remote signals or barrier semaphores. Data moves between devices by JAX's collectives and lax.ppermute only.
A program may use at most 128 MiB of HBM per device.

```python
import math
import jax
import jax.numpy as jnp
from jax import lax

LZ = 4
NCLASS = 8
SWEEPS = 2
CHEB = 4
LX = 64
LY = 128
PROBES = 16


def draw_bond_class(key, part):
    rows = jnp.arange(LX, dtype=jnp.int32)[None, None, :, None]
    region = rows * NCLASS // LX
    jitter = jax.random.randint(key, (3, LZ, LX, LY), 0, 3, dtype=jnp.int32)
    return (region + jitter) % NCLASS


def touch_ends(array, stream_key, low, largest):
    spot = [jax.random.randint(jax.random.fold_in(stream_key, axis), (), 0, length) for axis, length in enumerate(array.shape)]
    widest = array.shape.index(max(array.shape))
    neighbour = spot[:widest] + [(spot[widest] + 1) % array.shape[widest]] + spot[widest + 1:]
    return array.at[tuple(spot)].set(low).at[tuple(neighbour)].set(largest)


def steps_of(rng, shape, shards, low, high):
    level, own = 1.0, jax.random.fold_in(rng, 6)
    for axis_at, shards_of in shards:
        heights = jnp.exp(jax.random.uniform(jax.random.fold_in(own, axis_at), (shards_of,), jnp.float32, low / len(shards), high / len(shards)))
        level = level * jnp.repeat(heights, shape[axis_at] // shards_of).reshape([-1 if axis == axis_at else 1 for axis in range(len(shape))])
    return level


def setup_inputs(seed: int = 0) -> dict:
    seeds = jax.random.split(jax.random.key(seed), 6)
    cos_polar = jnp.clip(jax.random.uniform(seeds[0], (LZ, LX, LY), jnp.float32, -1.0, 1.0) * steps_of(seeds[0], (LZ, LX, LY), ((1, 16), (2, 2)), -0.4, 0.0), -1.0, 1.0)
    azimuth = jnp.clip(jax.random.uniform(seeds[1], (LZ, LX, LY), jnp.float32, -3.140625, 3.140625), -3.140625, 3.140625)
    bond_class = draw_bond_class(jax.random.fold_in(seeds[5], 71), 0)
    exchange = jnp.clip(jax.random.uniform(seeds[3], (NCLASS,), jnp.float32, -1.0, 1.0), -1.0, 1.0)
    probe_wave = touch_ends(jax.random.randint(seeds[4], (PROBES, 3), 0, min(LX, LY)), jax.random.fold_in(seeds[4], 1), 0, (min(LX, LY)) - 1).astype(jnp.int32)
    return dict(cos_polar=cos_polar, azimuth=azimuth, bond_class=bond_class, exchange=exchange, probe_wave=probe_wave)


relax_rate = 0.15
precess_scale = 1.0 / 6.0

def spin_field(cos_polar, azimuth):
    radial = jnp.sqrt(1.0 - cos_polar * cos_polar)
    return jnp.stack([radial * jnp.cos(azimuth), radial * jnp.sin(azimuth), cos_polar], 0)

def bond_strengths(bond_class, exchange):
    strengths = jnp.zeros(bond_class.shape, exchange.dtype)
    for class_index in range(exchange.shape[0]):
        strengths = strengths + jnp.where(bond_class == class_index, exchange[class_index], 0.0)
    return strengths

def cross_product(spin_core, vector):
    spin_a, spin_b, spin_c = (spin_core[0], spin_core[1], spin_core[2])
    vec_a = vector[..., 0, :, :, :]
    vec_b = vector[..., 1, :, :, :]
    vec_c = vector[..., 2, :, :, :]
    return jnp.stack([spin_b * vec_c - spin_c * vec_b, spin_c * vec_a - spin_a * vec_c, spin_a * vec_b - spin_b * vec_a], axis=-4)

def neighbour_sum(vector, bonds):
    along_x, along_y, along_z = (bonds[0], bonds[1], bonds[2])
    total = along_x * jnp.roll(vector, -1, -2) + jnp.roll(along_x, 1, -2) * jnp.roll(vector, 1, -2)
    total = total + along_y * jnp.roll(vector, -1, -1) + jnp.roll(along_y, 1, -1) * jnp.roll(vector, 1, -1)
    total = total + along_z * jnp.roll(vector, -1, -3) + jnp.roll(along_z, 1, -3) * jnp.roll(vector, 1, -3)
    return total

def relax_update(spins, field):
    turned = cross_product(spins, field)
    twice = cross_product(spins, turned)
    moved = spins - relax_rate * twice
    length = jnp.sqrt(lax.optimization_barrier(jnp.sum(moved * moved, axis=0)))
    return moved / length

def make_probes(probe_wave, probe_ids, x_coords, total_x, total_y, depth_z):
    wave_x = probe_wave[:, 0][:, None]
    wave_y = probe_wave[:, 1][:, None]
    wave_z = probe_wave[:, 2][:, None]
    phase_x = wave_x * x_coords[None, :] % total_x
    phase_y = wave_y * jnp.arange(total_y, dtype=jnp.int32)[None, :] % total_y
    phase_z = wave_z * jnp.arange(depth_z, dtype=jnp.int32)[None, :] % depth_z
    fraction = phase_z[:, :, None, None].astype(jnp.float32) / depth_z + phase_x[:, None, :, None].astype(jnp.float32) / total_x + phase_y[:, None, None, :].astype(jnp.float32) / total_y
    angle = 2.0 * math.pi * fraction
    ramp = jnp.sqrt(1.0 + 2.0 * x_coords.astype(jnp.float32) / total_x)[None, None, :, None]
    waves = jnp.stack([jnp.cos(angle) * ramp, jnp.sin(angle) * ramp], 1)
    polar = ((probe_ids % 3)[:, None] == jnp.arange(3, dtype=jnp.int32)[None, :]).astype(jnp.float32)
    return waves[:, :, None] * polar[:, None, :, None, None, None]

def reference(cos_polar, azimuth, bond_class, exchange, probe_wave):
    spins = spin_field(cos_polar, azimuth)
    bonds = bond_strengths(bond_class, exchange)
    for sweep_index in range(SWEEPS):
        spins = relax_update(spins, neighbour_sum(spins, bonds))
    site_count = LX * LY * LZ

    def precess(vector):
        return cross_product(spins, neighbour_sum(vector, bonds)) * -precess_scale

    def one_probe(operands):
        wave, ident = operands
        start = make_probes(wave[None, :], ident[None], jnp.arange(LX, dtype=jnp.int32), LX, LY, LZ)
        previous = start
        current = precess(start)
        found = [jnp.sum(current * current) / site_count]
        for order in range(1, CHEB):
            advanced = 2.0 * precess(current) - previous
            previous, current = (current, advanced)
            found.append(jnp.sum(current * current) / site_count)
        return (current[0].astype(jnp.bfloat16), jnp.stack(found))
    last_vectors, moment_rows = lax.map(one_probe, (probe_wave, jnp.arange(PROBES, dtype=jnp.int32)))
    return (spins, last_vectors, moment_rows)
```

```python
import math

import jax
import jax.numpy as jnp
from jax import lax
from jax.sharding import PartitionSpec as P

LZ = 4
SWEEPS = 2
CHEB = 4
HALO_SLABS = 2


relax_rate = 0.15
precess_scale = 1.0 / 6.0


def shifted(array, axis, shift):
    size = lax.axis_size(axis)
    if shift % size == 0:
        return array
    return lax.ppermute(array, axis, [(i, (i - shift) % size) for i in range(size)])


def bond_strengths(bond_class, exchange):
    strengths = jnp.zeros(bond_class.shape, exchange.dtype)
    for class_index in range(exchange.shape[0]):
        strengths = strengths + jnp.where(bond_class == class_index, exchange[class_index], 0.0)
    return strengths


def cross_product(spin_core, vector):
    spin_a, spin_b, spin_c = (spin_core[0], spin_core[1], spin_core[2])
    vec_a = vector[..., 0, :, :, :]
    vec_b = vector[..., 1, :, :, :]
    vec_c = vector[..., 2, :, :, :]
    return jnp.stack(
        [
            spin_b * vec_c - spin_c * vec_b,
            spin_c * vec_a - spin_a * vec_c,
            spin_a * vec_b - spin_b * vec_a,
        ],
        axis=-4,
    )


def rows(array, start, stop):
    return lax.slice_in_dim(array, start, stop, axis=array.ndim - 2)


def neighbour_window(vector, bonds):
    n = vector.shape[-2]
    along_x, along_y, along_z = (bonds[0], bonds[1], bonds[2])
    total = rows(along_x, 1, n - 1) * rows(vector, 2, n) + rows(along_x, 0, n - 2) * rows(vector, 0, n - 2)
    centre = rows(vector, 1, n - 1)
    bond_y = rows(along_y, 1, n - 1)
    total = total + bond_y * jnp.roll(centre, -1, -1) + jnp.roll(bond_y, 1, -1) * jnp.roll(centre, 1, -1)
    bond_z = rows(along_z, 1, n - 1)
    total = total + bond_z * jnp.roll(centre, -1, -3) + jnp.roll(bond_z, 1, -3) * jnp.roll(centre, 1, -3)
    return total


def relax_update(spins, field):
    turned = cross_product(spins, field)
    twice = cross_product(spins, turned)
    moved = spins - relax_rate * twice
    length = jnp.sqrt(jnp.sum(moved * moved, axis=0))
    return moved / length


def make_probes(probe_wave, probe_ids, x_coords, y_coords, total_x, total_y, depth_z):
    wave_x = probe_wave[:, 0][:, None]
    wave_y = probe_wave[:, 1][:, None]
    wave_z = probe_wave[:, 2][:, None]
    phase_x = wave_x * x_coords[None, :] % total_x
    phase_y = wave_y * y_coords[None, :] % total_y
    phase_z = wave_z * jnp.arange(depth_z, dtype=jnp.int32)[None, :] % depth_z
    fraction = (
        phase_z[:, :, None, None].astype(jnp.float32) / depth_z
        + phase_x[:, None, :, None].astype(jnp.float32) / total_x
        + phase_y[:, None, None, :].astype(jnp.float32) / total_y
    )
    angle = 2.0 * math.pi * fraction
    ramp = jnp.sqrt(1.0 + 2.0 * x_coords.astype(jnp.float32) / total_x)[None, None, :, None]
    waves = jnp.stack([jnp.cos(angle) * ramp, jnp.sin(angle) * ramp], 1)
    polar = ((probe_ids % 3)[:, None] == jnp.arange(3, dtype=jnp.int32)[None, :]).astype(
        jnp.float32
    )
    return waves[:, :, None] * polar[:, None, :, None, None, None]


def butterfly_sum(value, axis):
    size = lax.axis_size(axis)
    if size & (size - 1):
        return lax.psum(value, axis)
    step = 1
    while step < size:
        value = value + lax.ppermute(value, axis, [(i, i ^ step) for i in range(size)])
        step *= 2
    return value


def shards(cos_polar, azimuth, bond_class, exchange, probe_wave):
    groups = lax.axis_size("probe")
    slabs = lax.axis_size("space")
    group = lax.axis_index("probe")
    slab = lax.axis_index("space")
    slab_rows = cos_polar.shape[1]
    block_y = cos_polar.shape[2]
    total_x = slab_rows * slabs
    total_y = block_y * groups
    site_count = total_x * total_y * LZ

    bonds = bond_strengths(bond_class, exchange)
    local = jnp.concatenate([cos_polar[None], azimuth[None], bonds], 0)

    pieces = [shifted(local, "probe", k) for k in range(groups)]
    rotated = jnp.concatenate(pieces, -1)
    full_y = jnp.roll(rotated, group * block_y, -1) if groups > 1 else rotated

    window = jnp.concatenate(
        [shifted(full_y, "space", k) for k in range(-HALO_SLABS, HALO_SLABS + 1)], -2
    )
    halo = HALO_SLABS * slab_rows
    cos_w, az_w, bonds_w = window[0], window[1], window[2:]

    radial = jnp.sqrt(1.0 - cos_w * cos_w)
    spins = jnp.stack([radial * jnp.cos(az_w), radial * jnp.sin(az_w), cos_w], 0)
    sweep_bonds = bonds_w
    for sweep_index in range(SWEEPS):
        n = spins.shape[-2]
        field = neighbour_window(spins, sweep_bonds)
        spins = relax_update(rows(spins, 1, n - 1), field)
        sweep_bonds = rows(sweep_bonds, 1, n - 1)
    own = halo - SWEEPS
    relaxed_own = lax.dynamic_slice_in_dim(rows(spins, own, own + slab_rows), group * block_y, block_y, -1)

    reach = CHEB
    first = halo - reach
    width = slab_rows + 2 * reach
    x_coords = (slab * slab_rows - reach + jnp.arange(width, dtype=jnp.int32)) % total_x
    y_coords = jnp.arange(total_y, dtype=jnp.int32)
    group_size = probe_wave.shape[0]
    probe_ids = group * group_size + jnp.arange(group_size, dtype=jnp.int32)
    start = make_probes(probe_wave, probe_ids, x_coords, y_coords, total_x, total_y, LZ)

    def precess(vector, lo):
        n = vector.shape[-2]
        field = neighbour_window(vector, rows(bonds_w, lo, lo + n))
        spin_rows = rows(spins, lo + 1 - SWEEPS, lo + n - 1 - SWEEPS)
        return cross_product(spin_rows, field) * -precess_scale

    terms = []
    previous, current, lo = start, start, first
    for order in range(CHEB):
        advanced = precess(current, lo)
        n = current.shape[-2]
        if order > 0:
            advanced = 2.0 * advanced - rows(previous, 2, n)
        previous, current, lo = current, advanced, lo + 1
        keep = halo - lo
        mine = rows(current, keep, keep + slab_rows)
        terms.append(jnp.sum(mine * mine, axis=(1, 2, 3, 4, 5)))
    moment_rows = butterfly_sum(jnp.stack(terms, 1), "space") / site_count
    return (relaxed_own, current.astype(jnp.bfloat16), moment_rows)


def solution(mesh):
    return jax.shard_map(
        shards,
        mesh=mesh,
        in_specs=(
            P(None, "space", "probe"),
            P(None, "space", "probe"),
            P(None, None, "space", "probe"),
            P(),
            P("probe", None),
        ),
        out_specs=(
            P(None, None, "space", "probe"),
            P("probe", None, None, None, "space", None),
            P("probe", None),
        ),
        check_vma=False,
    )
```

```python
import math

import jax
import jax.numpy as jnp
from jax import lax
from jax.sharding import PartitionSpec as P

LZ = 4
SWEEPS = 2
CHEB = 4
HALO_SLABS = 2


relax_rate = 0.15
precess_scale = 1.0 / 6.0


def shifted(array, axis, shift):
    size = lax.axis_size(axis)
    if shift % size == 0:
        return array
    return lax.ppermute(array, axis, [(i, (i - shift) % size) for i in range(size)])


def bond_strengths(bond_class, exchange):
    classes = jnp.arange(exchange.shape[0], dtype=bond_class.dtype)
    picked = jnp.where(bond_class[..., None] == classes, exchange, 0.0)
    return jnp.sum(picked, axis=-1)


def cross_product(spin_core, vector):
    spin_a, spin_b, spin_c = (spin_core[0], spin_core[1], spin_core[2])
    vec_a = vector[..., 0, :, :, :]
    vec_b = vector[..., 1, :, :, :]
    vec_c = vector[..., 2, :, :, :]
    return jnp.stack(
        [
            spin_b * vec_c - spin_c * vec_b,
            spin_c * vec_a - spin_a * vec_c,
            spin_a * vec_b - spin_b * vec_a,
        ],
        axis=-4,
    )


def rows(array, start, stop):
    return lax.slice_in_dim(array, start, stop, axis=array.ndim - 2)


def neighbour_window(vector, bonds):
    n = vector.shape[-2]
    along_x, along_y, along_z = (bonds[0], bonds[1], bonds[2])
    total = rows(along_x, 1, n - 1) * rows(vector, 2, n) + rows(along_x, 0, n - 2) * rows(vector, 0, n - 2)
    centre = rows(vector, 1, n - 1)
    bond_y = rows(along_y, 1, n - 1)
    total = total + bond_y * jnp.roll(centre, -1, -1) + jnp.roll(bond_y, 1, -1) * jnp.roll(centre, 1, -1)
    bond_z = rows(along_z, 1, n - 1)
    total = total + bond_z * jnp.roll(centre, -1, -3) + jnp.roll(bond_z, 1, -3) * jnp.roll(centre, 1, -3)
    return total


def relax_update(spins, field):
    turned = cross_product(spins, field)
    twice = cross_product(spins, turned)
    moved = spins - relax_rate * twice
    length = jnp.sqrt(jnp.sum(moved * moved, axis=0))
    return moved / length


def make_probes(probe_wave, probe_ids, x_coords, y_coords, total_x, total_y, depth_z):
    wave_x = probe_wave[:, 0][:, None]
    wave_y = probe_wave[:, 1][:, None]
    wave_z = probe_wave[:, 2][:, None]
    phase_x = wave_x * x_coords[None, :] % total_x
    phase_y = wave_y * y_coords[None, :] % total_y
    phase_z = wave_z * jnp.arange(depth_z, dtype=jnp.int32)[None, :] % depth_z
    fraction = (
        phase_z[:, :, None, None].astype(jnp.float32) / depth_z
        + phase_x[:, None, :, None].astype(jnp.float32) / total_x
        + phase_y[:, None, None, :].astype(jnp.float32) / total_y
    )
    angle = 2.0 * math.pi * fraction
    ramp = jnp.sqrt(1.0 + 2.0 * x_coords.astype(jnp.float32) / total_x)[None, None, :, None]
    waves = jnp.stack([jnp.cos(angle) * ramp, jnp.sin(angle) * ramp], 1)
    polar = ((probe_ids % 3)[:, None] == jnp.arange(3, dtype=jnp.int32)[None, :]).astype(
        jnp.float32
    )
    return waves[:, :, None] * polar[:, None, :, None, None, None]


def butterfly_sum(value, axis):
    size = lax.axis_size(axis)
    if size & (size - 1):
        return lax.psum(value, axis)
    step = 1
    while step < size:
        value = value + lax.ppermute(value, axis, [(i, i ^ step) for i in range(size)])
        step *= 2
    return value


def shards(cos_polar, azimuth, bond_class, exchange, probe_wave):
    groups = lax.axis_size("probe")
    slabs = lax.axis_size("space")
    group = lax.axis_index("probe")
    slab = lax.axis_index("space")
    slab_rows = cos_polar.shape[1]
    block_y = cos_polar.shape[2]
    total_x = slab_rows * slabs
    total_y = block_y * groups
    site_count = total_x * total_y * LZ

    bonds = bond_strengths(bond_class, exchange)
    local = jnp.concatenate([cos_polar[None], azimuth[None], bonds], 0)

    pieces = [shifted(local, "probe", k) for k in range(groups)]
    rotated = jnp.concatenate(pieces, -1)
    full_y = jnp.roll(rotated, group * block_y, -1) if groups > 1 else rotated

    window = jnp.concatenate(
        [shifted(full_y, "space", k) for k in range(-HALO_SLABS, HALO_SLABS + 1)], -2
    )
    halo = HALO_SLABS * slab_rows
    cos_w, az_w, bonds_w = window[0], window[1], window[2:]

    radial = jnp.sqrt(1.0 - cos_w * cos_w)
    spins = jnp.stack([radial * jnp.cos(az_w), radial * jnp.sin(az_w), cos_w], 0)
    sweep_bonds = bonds_w
    for sweep_index in range(SWEEPS):
        n = spins.shape[-2]
        field = neighbour_window(spins, sweep_bonds)
        spins = relax_update(rows(spins, 1, n - 1), field)
        sweep_bonds = rows(sweep_bonds, 1, n - 1)
    own = halo - SWEEPS
    relaxed_own = lax.dynamic_slice_in_dim(rows(spins, own, own + slab_rows), group * block_y, block_y, -1)

    reach = CHEB
    first = halo - reach
    width = slab_rows + 2 * reach
    x_coords = (slab * slab_rows - reach + jnp.arange(width, dtype=jnp.int32)) % total_x
    y_coords = jnp.arange(total_y, dtype=jnp.int32)
    group_size = probe_wave.shape[0]
    probe_ids = group * group_size + jnp.arange(group_size, dtype=jnp.int32)
    start = make_probes(probe_wave, probe_ids, x_coords, y_coords, total_x, total_y, LZ)

    def precess(vector, lo):
        n = vector.shape[-2]
        field = neighbour_window(vector, rows(bonds_w, lo, lo + n))
        spin_rows = rows(spins, lo + 1 - SWEEPS, lo + n - 1 - SWEEPS)
        return cross_product(spin_rows, field) * -precess_scale

    terms = []
    previous, current, lo = start, start, first
    for order in range(CHEB):
        advanced = precess(current, lo)
        n = current.shape[-2]
        if order > 0:
            advanced = 2.0 * advanced - rows(previous, 2, n)
        previous, current, lo = current, advanced, lo + 1
        keep = halo - lo
        mine = rows(current, keep, keep + slab_rows)
        terms.append(jnp.sum(mine * mine, axis=(1, 2, 3, 4, 5)))
    moment_rows = butterfly_sum(jnp.stack(terms, 1), "space") / site_count
    return (relaxed_own, current.astype(jnp.bfloat16), moment_rows)


def solution(mesh):
    return jax.shard_map(
        shards,
        mesh=mesh,
        in_specs=(
            P(None, "space", "probe"),
            P(None, "space", "probe"),
            P(None, None, "space", "probe"),
            P(),
            P("probe", None),
        ),
        out_specs=(
            P(None, None, "space", "probe"),
            P("probe", None, None, None, "space", None),
            P("probe", None),
        ),
        check_vma=False,
    )
```

```python
import math

import jax
import jax.numpy as jnp
from jax import lax
from jax.experimental import pallas as pl
from jax.experimental.pallas import tpu as pltpu
from jax.sharding import PartitionSpec as P

LZ = 4
SWEEPS = 2
CHEB = 4
HALO_SLABS = 2


relax_rate = 0.15
precess_scale = 1.0 / 6.0


def shifted(array, axis, shift):
    size = lax.axis_size(axis)
    if shift % size == 0:
        return array
    return lax.ppermute(array, axis, [(i, (i - shift) % size) for i in range(size)])


def bond_strengths(bond_class, exchange):
    classes = jnp.arange(exchange.shape[0], dtype=bond_class.dtype)
    picked = jnp.where(bond_class[..., None] == classes, exchange, 0.0)
    return jnp.sum(picked, axis=-1)


def cross_product(spin_core, vector):
    spin_a, spin_b, spin_c = (spin_core[0], spin_core[1], spin_core[2])
    vec_a = vector[..., 0, :, :, :]
    vec_b = vector[..., 1, :, :, :]
    vec_c = vector[..., 2, :, :, :]
    return jnp.stack(
        [
            spin_b * vec_c - spin_c * vec_b,
            spin_c * vec_a - spin_a * vec_c,
            spin_a * vec_b - spin_b * vec_a,
        ],
        axis=-4,
    )


def rows(array, start, stop):
    return lax.slice_in_dim(array, start, stop, axis=array.ndim - 2)


def neighbour_window(vector, bonds):
    n = vector.shape[-2]
    along_x, along_y, along_z = (bonds[0], bonds[1], bonds[2])
    total = rows(along_x, 1, n - 1) * rows(vector, 2, n) + rows(along_x, 0, n - 2) * rows(vector, 0, n - 2)
    centre = rows(vector, 1, n - 1)
    bond_y = rows(along_y, 1, n - 1)
    total = total + bond_y * jnp.roll(centre, -1, -1) + jnp.roll(bond_y, 1, -1) * jnp.roll(centre, 1, -1)
    bond_z = rows(along_z, 1, n - 1)
    total = total + bond_z * jnp.roll(centre, -1, -3) + jnp.roll(bond_z, 1, -3) * jnp.roll(centre, 1, -3)
    return total


def relax_update(spins, field):
    turned = cross_product(spins, field)
    twice = cross_product(spins, turned)
    moved = spins - relax_rate * twice
    length = jnp.sqrt(jnp.sum(moved * moved, axis=0))
    return moved / length


def make_probes(probe_wave, probe_ids, x_coords, y_coords, total_x, total_y, depth_z):
    wave_x = probe_wave[:, 0][:, None]
    wave_y = probe_wave[:, 1][:, None]
    wave_z = probe_wave[:, 2][:, None]
    phase_x = wave_x * x_coords[None, :] % total_x
    phase_y = wave_y * y_coords[None, :] % total_y
    phase_z = wave_z * jnp.arange(depth_z, dtype=jnp.int32)[None, :] % depth_z
    fraction = (
        phase_z[:, :, None, None].astype(jnp.float32) / depth_z
        + phase_x[:, None, :, None].astype(jnp.float32) / total_x
        + phase_y[:, None, None, :].astype(jnp.float32) / total_y
    )
    angle = 2.0 * math.pi * fraction
    ramp = jnp.sqrt(1.0 + 2.0 * x_coords.astype(jnp.float32) / total_x)[None, None, :, None]
    waves = jnp.stack([jnp.cos(angle) * ramp, jnp.sin(angle) * ramp], 1)
    polar = ((probe_ids % 3)[:, None] == jnp.arange(3, dtype=jnp.int32)[None, :]).astype(
        jnp.float32
    )
    return waves[:, :, None] * polar[:, None, :, None, None, None]


def butterfly_sum(value, axis):
    size = lax.axis_size(axis)
    if size & (size - 1):
        return lax.psum(value, axis)
    step = 1
    while step < size:
        value = value + lax.ppermute(value, axis, [(i, i ^ step) for i in range(size)])
        step *= 2
    return value


def y_roll(x, shift):
    return pltpu.roll(x, shift % x.shape[-1], x.ndim - 1)


def z_roll(x, shift):
    axis = x.ndim - 3
    n = x.shape[axis]
    s = shift % n
    if s == 0:
        return x
    return jnp.concatenate(
        [lax.slice_in_dim(x, n - s, n, axis=axis), lax.slice_in_dim(x, 0, n - s, axis=axis)], axis
    )


def field_rows(vector, bond, lo, n):
    up = vector(lo + 2, lo + n)
    down = vector(lo, lo + n - 2)
    centre = vector(lo + 1, lo + n - 1)
    total = bond(0, lo + 1, lo + n - 1) * up + bond(0, lo, lo + n - 2) * down
    bond_y = bond(1, lo + 1, lo + n - 1)
    total = total + bond_y * y_roll(centre, -1) + y_roll(bond_y, 1) * y_roll(centre, 1)
    bond_z = bond(2, lo + 1, lo + n - 1)
    total = total + bond_z * z_roll(centre, -1) + z_roll(bond_z, 1) * z_roll(centre, 1)
    return total


def local_kernel(halo, slab_rows, win_ref, start_ref, relaxed_ref, last_ref, sq_ref, sweep_a, sweep_b, t_refs):
    width = win_ref.shape[2]

    def bond(d, a, b):
        return win_ref[3 + d, :, a:b, :]

    def from_window(a, b):
        return win_ref[0:3, :, a:b, :]

    def from_a(a, b):
        return sweep_a[:, :, a - 1:b - 1, :]

    rows_a = width - 2
    sweep_a[:, :, 0:rows_a, :] = relax_update(win_ref[0:3, :, 1:width - 1, :], field_rows(from_window, bond, 0, width))
    rows_b = width - 4
    sweep_b[:, :, 0:rows_b, :] = relax_update(sweep_a[:, :, 1:rows_a - 1, :], field_rows(from_a, bond, 1, width - 2))
    relaxed_ref[...] = sweep_b[:, :, halo - SWEEPS:halo - SWEEPS + slab_rows, :]

    first = halo - CHEB
    n_start = slab_rows + 2 * CHEB

    def one_vector(q, carry):
        def from_start(a, b):
            return start_ref[q, :, :, a - first:b - first, :]

        loaders = [from_start]
        for order in range(CHEB):
            lo = first + order
            n = n_start - 2 * order
            spin_rows = sweep_b[:, :, lo + 1 - SWEEPS:lo + n - 1 - SWEEPS, :]
            advanced = cross_product(spin_rows, field_rows(loaders[-1], bond, lo, n)) * -precess_scale
            if order > 0:
                advanced = 2.0 * advanced - loaders[-2](lo + 1, lo + n - 1)
            mine = advanced[:, :, halo - lo - 1:halo - lo - 1 + slab_rows, :]
            squares = mine * mine
            total = squares[0] + squares[1] + squares[2]
            sq_ref[order, q] = total[0] + total[1] + total[2] + total[3]
            if order == CHEB - 1:
                last_ref[q] = advanced
            else:
                t_ref = t_refs[order]
                t_ref[:, :, 0:n - 2, :] = advanced

                def from_t(a, b, t_ref=t_ref, base=lo + 1):
                    return t_ref[:, :, a - base:b - base, :]

                loaders.append(from_t)
        return carry

    lax.fori_loop(0, start_ref.shape[0], one_vector, 0)


def run_local(window, start, halo, slab_rows):
    width = window.shape[2]
    vectors = start.shape[0]
    depth, lanes = window.shape[1], window.shape[3]
    spin_shape = (3, depth, width, lanes)
    vector_rows = start.shape[3]

    def body(win_ref, start_ref, relaxed_ref, last_ref, sq_ref, sweep_a, sweep_b, t1, t2, t3):
        local_kernel(halo, slab_rows, win_ref, start_ref, relaxed_ref, last_ref, sq_ref, sweep_a, sweep_b, (t1, t2, t3))

    sites = vectors * 3 * depth * vector_rows * lanes
    return pl.pallas_call(
        body,
        out_shape=(
            jax.ShapeDtypeStruct((3, depth, slab_rows, lanes), jnp.float32),
            jax.ShapeDtypeStruct((vectors, 3, depth, slab_rows, lanes), jnp.float32),
            jax.ShapeDtypeStruct((CHEB, vectors, slab_rows, lanes), jnp.float32),
        ),
        in_specs=[pl.BlockSpec(memory_space=pltpu.VMEM)] * 2,
        out_specs=[pl.BlockSpec(memory_space=pltpu.VMEM)] * 3,
        scratch_shapes=[pltpu.VMEM(spin_shape, jnp.float32)] * 2
        + [pltpu.VMEM((3, depth, vector_rows, lanes), jnp.float32)] * (CHEB - 1),
        cost_estimate=pl.CostEstimate(
            flops=40 * CHEB * sites + 200 * 3 * depth * width * lanes,
            transcendentals=0,
            bytes_accessed=4 * (window.size + start.size + sites // 2),
        ),
    )(window, start)


def shards(cos_polar, azimuth, bond_class, exchange, probe_wave):
    groups = lax.axis_size("probe")
    slabs = lax.axis_size("space")
    group = lax.axis_index("probe")
    slab = lax.axis_index("space")
    slab_rows = cos_polar.shape[1]
    block_y = cos_polar.shape[2]
    total_x = slab_rows * slabs
    total_y = block_y * groups
    site_count = total_x * total_y * LZ

    bonds = bond_strengths(bond_class, exchange)
    radial = jnp.sqrt(1.0 - cos_polar * cos_polar)
    spins0 = jnp.stack([radial * jnp.cos(azimuth), radial * jnp.sin(azimuth), cos_polar], 0)
    local = jnp.concatenate([spins0, bonds], 0)

    pieces = [shifted(local, "probe", k) for k in range(groups)]
    rotated = jnp.concatenate(pieces, -1)
    full_y = jnp.roll(rotated, group * block_y, -1) if groups > 1 else rotated

    window = jnp.concatenate(
        [shifted(full_y, "space", k) for k in range(-HALO_SLABS, HALO_SLABS + 1)], -2
    )
    halo = HALO_SLABS * slab_rows

    width = slab_rows + 2 * CHEB
    x_coords = (slab * slab_rows - CHEB + jnp.arange(width, dtype=jnp.int32)) % total_x
    y_coords = jnp.arange(total_y, dtype=jnp.int32)
    group_size = probe_wave.shape[0]
    probe_ids = group * group_size + jnp.arange(group_size, dtype=jnp.int32)
    start = make_probes(probe_wave, probe_ids, x_coords, y_coords, total_x, total_y, LZ)
    start = start.reshape((group_size * 2,) + start.shape[2:])

    relaxed, last, squares = run_local(window, start, halo, slab_rows)
    relaxed_own = lax.dynamic_slice_in_dim(relaxed, group * block_y, block_y, -1)
    last = last.reshape((group_size, 2) + last.shape[1:]).astype(jnp.bfloat16)
    terms = squares.reshape((CHEB, group_size, 2 * slab_rows * total_y)).sum(-1)
    moment_rows = butterfly_sum(terms.T, "space") / site_count
    return (relaxed_own, last, moment_rows)


def solution(mesh):
    return jax.shard_map(
        shards,
        mesh=mesh,
        in_specs=(
            P(None, "space", "probe"),
            P(None, "space", "probe"),
            P(None, None, "space", "probe"),
            P(),
            P("probe", None),
        ),
        out_specs=(
            P(None, None, "space", "probe"),
            P("probe", None, None, None, "space", None),
            P("probe", None),
        ),
        check_vma=False,
    )
```

```python
import math

import jax
import jax.numpy as jnp
from jax import lax
from jax.experimental import pallas as pl
from jax.experimental.pallas import tpu as pltpu
from jax.sharding import PartitionSpec as P

LZ = 4
SWEEPS = 2
CHEB = 4
HALO_SLABS = 2


relax_rate = 0.15
precess_scale = 1.0 / 6.0


def shifted(array, axis, shift):
    size = lax.axis_size(axis)
    if shift % size == 0:
        return array
    return lax.ppermute(array, axis, [(i, (i - shift) % size) for i in range(size)])


def bond_strengths(bond_class, exchange):
    classes = jnp.arange(exchange.shape[0], dtype=bond_class.dtype)
    picked = jnp.where(bond_class[..., None] == classes, exchange, 0.0)
    return jnp.sum(picked, axis=-1)


def cross_product(spin_core, vector):
    spin_a, spin_b, spin_c = (spin_core[0], spin_core[1], spin_core[2])
    vec_a = vector[..., 0, :, :, :]
    vec_b = vector[..., 1, :, :, :]
    vec_c = vector[..., 2, :, :, :]
    return jnp.stack(
        [
            spin_b * vec_c - spin_c * vec_b,
            spin_c * vec_a - spin_a * vec_c,
            spin_a * vec_b - spin_b * vec_a,
        ],
        axis=-4,
    )


def rows(array, start, stop):
    return lax.slice_in_dim(array, start, stop, axis=array.ndim - 2)


def neighbour_window(vector, bonds):
    n = vector.shape[-2]
    along_x, along_y, along_z = (bonds[0], bonds[1], bonds[2])
    total = rows(along_x, 1, n - 1) * rows(vector, 2, n) + rows(along_x, 0, n - 2) * rows(vector, 0, n - 2)
    centre = rows(vector, 1, n - 1)
    bond_y = rows(along_y, 1, n - 1)
    total = total + bond_y * jnp.roll(centre, -1, -1) + jnp.roll(bond_y, 1, -1) * jnp.roll(centre, 1, -1)
    bond_z = rows(along_z, 1, n - 1)
    total = total + bond_z * jnp.roll(centre, -1, -3) + jnp.roll(bond_z, 1, -3) * jnp.roll(centre, 1, -3)
    return total


def relax_update(spins, field):
    turned = cross_product(spins, field)
    twice = cross_product(spins, turned)
    moved = spins - relax_rate * twice
    length = jnp.sqrt(jnp.sum(moved * moved, axis=0))
    return moved / length


def make_probes(probe_wave, probe_ids, x_coords, y_coords, total_x, total_y, depth_z):
    wave_x = probe_wave[:, 0][:, None]
    wave_y = probe_wave[:, 1][:, None]
    wave_z = probe_wave[:, 2][:, None]
    phase_x = wave_x * x_coords[None, :] % total_x
    phase_y = wave_y * y_coords[None, :] % total_y
    phase_z = wave_z * jnp.arange(depth_z, dtype=jnp.int32)[None, :] % depth_z
    fraction = (
        phase_z[:, :, None, None].astype(jnp.float32) / depth_z
        + phase_x[:, None, :, None].astype(jnp.float32) / total_x
        + phase_y[:, None, None, :].astype(jnp.float32) / total_y
    )
    angle = 2.0 * math.pi * fraction
    ramp = jnp.sqrt(1.0 + 2.0 * x_coords.astype(jnp.float32) / total_x)[None, None, :, None]
    waves = jnp.stack([jnp.cos(angle) * ramp, jnp.sin(angle) * ramp], 1)
    polar = ((probe_ids % 3)[:, None] == jnp.arange(3, dtype=jnp.int32)[None, :]).astype(
        jnp.float32
    )
    return waves[:, :, None] * polar[:, None, :, None, None, None]


def butterfly_sum(value, axis):
    size = lax.axis_size(axis)
    if size & (size - 1):
        return lax.psum(value, axis)
    step = 1
    while step < size:
        value = value + lax.ppermute(value, axis, [(i, i ^ step) for i in range(size)])
        step *= 2
    return value


def y_roll(x, shift):
    return pltpu.roll(x, shift % x.shape[-1], x.ndim - 1)


def z_roll(x, shift):
    axis = x.ndim - 3
    n = x.shape[axis]
    s = shift % n
    if s == 0:
        return x
    return jnp.concatenate(
        [lax.slice_in_dim(x, n - s, n, axis=axis), lax.slice_in_dim(x, 0, n - s, axis=axis)], axis
    )


def field_rows(vector, bond, lo, n):
    up = vector(lo + 2, lo + n)
    down = vector(lo, lo + n - 2)
    centre = vector(lo + 1, lo + n - 1)
    total = bond(0, lo + 1, lo + n - 1) * up + bond(0, lo, lo + n - 2) * down
    bond_y = bond(1, lo + 1, lo + n - 1)
    total = total + bond_y * y_roll(centre, -1) + y_roll(bond_y, 1) * y_roll(centre, 1)
    bond_z = bond(2, lo + 1, lo + n - 1)
    total = total + bond_z * z_roll(centre, -1) + z_roll(bond_z, 1) * z_roll(centre, 1)
    return total


def local_kernel(halo, slab_rows, *refs):
    slab_refs = refs[:2 * HALO_SLABS + 1]
    start_ref, relaxed_ref, last_ref, sums_ref, win, sweep_a, sweep_b, bonds_b, bonds_yr, bonds_zr, spins_b, t1, t2, t3 = refs[2 * HALO_SLABS + 1:]
    for k, slab_ref in enumerate(slab_refs):
        win[:, :, k * slab_rows:(k + 1) * slab_rows, :] = slab_ref[...]
    width = len(slab_refs) * slab_rows

    def bond(d, a, b):
        return win[3 + d, :, a:b, :]

    def from_window(a, b):
        return win[0:3, :, a:b, :]

    def from_a(a, b):
        return sweep_a[:, :, a - 1:b - 1, :]

    rows_a = width - 2
    sweep_a[:, :, 0:rows_a, :] = relax_update(win[0:3, :, 1:width - 1, :], field_rows(from_window, bond, 0, width))
    rows_b = width - 4
    sweep_b[:, :, 0:rows_b, :] = relax_update(sweep_a[:, :, 1:rows_a - 1, :], field_rows(from_a, bond, 1, width - 2))
    relaxed_ref[...] = sweep_b[:, :, halo - SWEEPS:halo - SWEEPS + slab_rows, :]

    first = halo - CHEB
    n_start = slab_rows + 2 * CHEB
    lanes = win.shape[3]
    depth = win.shape[1]
    probes = start_ref.shape[4]
    for xr in range(n_start):
        w = first + xr
        site = jnp.broadcast_to(win[3:6, :, w:w + 1, :], (3, depth, probes, lanes))
        bonds_b[xr] = site
        bonds_yr[xr] = y_roll(site[1], 1)
        bonds_zr[xr] = z_roll(site[2], 1)
    for xr in range(n_start - 2):
        w = first + 1 + xr
        spins_b[xr] = jnp.broadcast_to(sweep_b[:, :, w - SWEEPS:w - SWEEPS + 1, :], (3, depth, probes, lanes))

    t_refs = (start_ref, t1, t2, t3, last_ref)
    sums = []
    for order in range(CHEB):
        lo = first + order
        n = n_start - 2 * order
        source = t_refs[order]
        target = t_refs[order + 1]
        acc = None
        for i in range(n - 2):
            w = lo + 1 + i
            b = w - first
            up = source[i + 2]
            down = source[i]
            centre = source[i + 1]
            total = bonds_b[b, 0] * up + bonds_b[b - 1, 0] * down
            total = total + bonds_b[b, 1] * y_roll(centre, -1) + bonds_yr[b] * y_roll(centre, 1)
            total = total + bonds_b[b, 2] * z_roll(centre, -1) + bonds_zr[b] * z_roll(centre, 1)
            advanced = cross_product(spins_b[b - 1], total) * -precess_scale
            if order > 0:
                advanced = 2.0 * advanced - t_refs[order - 1][i + 2]
            target[i] = advanced
            if halo <= w < halo + slab_rows:
                squares = advanced * advanced
                part = squares[0] + squares[1]
                part = part[0] + part[1] + part[2]
                part = part[0] + part[1] + part[2] + part[3]
                acc = part if acc is None else acc + part
        sums.append(jnp.sum(acc, axis=-1, keepdims=True))
    lane = lax.broadcasted_iota(jnp.int32, sums_ref.shape, 1)
    out = jnp.zeros(sums_ref.shape, jnp.float32)
    for order in range(CHEB):
        out = jnp.where(lane == order, sums[order], out)
    sums_ref[...] = out


def run_local(slab_blocks, start, halo, slab_rows):
    depth, lanes = slab_blocks[0].shape[1], slab_blocks[0].shape[3]
    width = len(slab_blocks) * slab_rows
    n_start, probes = start.shape[0], start.shape[4]
    vec_shape = start.shape[1:]

    def body(*refs):
        local_kernel(halo, slab_rows, *refs)

    sites = n_start * start[0].size
    return pl.pallas_call(
        body,
        out_shape=(
            jax.ShapeDtypeStruct((3, depth, slab_rows, lanes), jnp.float32),
            jax.ShapeDtypeStruct((slab_rows,) + vec_shape, jnp.float32),
            jax.ShapeDtypeStruct((probes, 128), jnp.float32),
        ),
        in_specs=[pl.BlockSpec(memory_space=pltpu.VMEM)] * (len(slab_blocks) + 1),
        out_specs=[pl.BlockSpec(memory_space=pltpu.VMEM)] * 3,
        scratch_shapes=[
            pltpu.VMEM((6, depth, width, lanes), jnp.float32),
            pltpu.VMEM((3, depth, width, lanes), jnp.float32),
            pltpu.VMEM((3, depth, width, lanes), jnp.float32),
            pltpu.VMEM((n_start, 3, depth, probes, lanes), jnp.float32),
            pltpu.VMEM((n_start, depth, probes, lanes), jnp.float32),
            pltpu.VMEM((n_start, depth, probes, lanes), jnp.float32),
            pltpu.VMEM((n_start, 3, depth, probes, lanes), jnp.float32),
        ]
        + [pltpu.VMEM((n_start - 2 * k,) + vec_shape, jnp.float32) for k in range(1, CHEB)],
        cost_estimate=pl.CostEstimate(
            flops=30 * sites + 200 * 3 * depth * width * lanes,
            transcendentals=0,
            bytes_accessed=4 * (6 * depth * width * lanes + start.size + start.size // 3),
        ),
    )(*slab_blocks, start)


def shards(cos_polar, azimuth, bond_class, exchange, probe_wave):
    groups = lax.axis_size("probe")
    slabs = lax.axis_size("space")
    group = lax.axis_index("probe")
    slab = lax.axis_index("space")
    slab_rows = cos_polar.shape[1]
    block_y = cos_polar.shape[2]
    total_x = slab_rows * slabs
    total_y = block_y * groups
    site_count = total_x * total_y * LZ

    bonds = bond_strengths(bond_class, exchange)
    radial = jnp.sqrt(1.0 - cos_polar * cos_polar)
    spins0 = jnp.stack([radial * jnp.cos(azimuth), radial * jnp.sin(azimuth), cos_polar], 0)
    local = jnp.concatenate([spins0, bonds], 0)

    pieces = [shifted(local, "probe", k) for k in range(groups)]
    rotated = jnp.concatenate(pieces, -1)
    full_y = jnp.roll(rotated, group * block_y, -1) if groups > 1 else rotated

    slab_blocks = [shifted(full_y, "space", k) for k in range(-HALO_SLABS, HALO_SLABS + 1)]
    halo = HALO_SLABS * slab_rows

    width = slab_rows + 2 * CHEB
    x_coords = (slab * slab_rows - CHEB + jnp.arange(width, dtype=jnp.int32)) % total_x
    y_coords = jnp.arange(total_y, dtype=jnp.int32)
    group_size = probe_wave.shape[0]
    probe_ids = group * group_size + jnp.arange(group_size, dtype=jnp.int32)
    start = make_probes(probe_wave, probe_ids, x_coords, y_coords, total_x, total_y, LZ)
    start = jnp.transpose(start, (4, 1, 2, 3, 0, 5))

    relaxed, last, sums = run_local(slab_blocks, start, halo, slab_rows)
    relaxed_own = lax.dynamic_slice_in_dim(relaxed, group * block_y, block_y, -1)
    last = jnp.transpose(last, (4, 1, 2, 3, 0, 5)).astype(jnp.bfloat16)
    moment_rows = butterfly_sum(sums[:, :CHEB], "space") / site_count
    return (relaxed_own, last, moment_rows)


def solution(mesh):
    return jax.shard_map(
        shards,
        mesh=mesh,
        in_specs=(
            P(None, "space", "probe"),
            P(None, "space", "probe"),
            P(None, None, "space", "probe"),
            P(),
            P("probe", None),
        ),
        out_specs=(
            P(None, None, "space", "probe"),
            P("probe", None, None, None, "space", None),
            P("probe", None),
        ),
        check_vma=False,
    )
```

```python
import math

import jax
import jax.numpy as jnp
from jax import lax
from jax.experimental import pallas as pl
from jax.experimental.pallas import tpu as pltpu
from jax.sharding import PartitionSpec as P

LZ = 4
SWEEPS = 2
CHEB = 4
HALO_SLABS = 2
NCLASS = 8


relax_rate = 0.15
precess_scale = 1.0 / 6.0


def shifted(array, axis, shift):
    size = lax.axis_size(axis)
    if shift % size == 0:
        return array
    return lax.ppermute(array, axis, [(i, (i - shift) % size) for i in range(size)])


def cross_product(spin_core, vector):
    spin_a, spin_b, spin_c = (spin_core[0], spin_core[1], spin_core[2])
    vec_a = vector[..., 0, :, :, :]
    vec_b = vector[..., 1, :, :, :]
    vec_c = vector[..., 2, :, :, :]
    return jnp.stack(
        [
            spin_b * vec_c - spin_c * vec_b,
            spin_c * vec_a - spin_a * vec_c,
            spin_a * vec_b - spin_b * vec_a,
        ],
        axis=-4,
    )


def rows(array, start, stop):
    return lax.slice_in_dim(array, start, stop, axis=array.ndim - 2)


def neighbour_window(vector, bonds):
    n = vector.shape[-2]
    along_x, along_y, along_z = (bonds[0], bonds[1], bonds[2])
    total = rows(along_x, 1, n - 1) * rows(vector, 2, n) + rows(along_x, 0, n - 2) * rows(vector, 0, n - 2)
    centre = rows(vector, 1, n - 1)
    bond_y = rows(along_y, 1, n - 1)
    total = total + bond_y * jnp.roll(centre, -1, -1) + jnp.roll(bond_y, 1, -1) * jnp.roll(centre, 1, -1)
    bond_z = rows(along_z, 1, n - 1)
    total = total + bond_z * jnp.roll(centre, -1, -3) + jnp.roll(bond_z, 1, -3) * jnp.roll(centre, 1, -3)
    return total


def relax_update(spins, field):
    turned = cross_product(spins, field)
    twice = cross_product(spins, turned)
    moved = spins - relax_rate * twice
    length = jnp.sqrt(jnp.sum(moved * moved, axis=0))
    return moved / length


def make_probes(probe_wave, probe_ids, x_coords, y_coords, total_x, total_y, depth_z):
    wave_x = probe_wave[:, 0][:, None]
    wave_y = probe_wave[:, 1][:, None]
    wave_z = probe_wave[:, 2][:, None]
    phase_x = wave_x * x_coords[None, :] % total_x
    phase_y = wave_y * y_coords[None, :] % total_y
    phase_z = wave_z * jnp.arange(depth_z, dtype=jnp.int32)[None, :] % depth_z
    fraction = (
        phase_z[:, :, None, None].astype(jnp.float32) / depth_z
        + phase_x[:, None, :, None].astype(jnp.float32) / total_x
        + phase_y[:, None, None, :].astype(jnp.float32) / total_y
    )
    angle = 2.0 * math.pi * fraction
    ramp = jnp.sqrt(1.0 + 2.0 * x_coords.astype(jnp.float32) / total_x)[None, None, :, None]
    waves = jnp.stack([jnp.cos(angle) * ramp, jnp.sin(angle) * ramp], 1)
    polar = ((probe_ids % 3)[:, None] == jnp.arange(3, dtype=jnp.int32)[None, :]).astype(
        jnp.float32
    )
    return waves[:, :, None] * polar[:, None, :, None, None, None]


def butterfly_sum(value, axis):
    size = lax.axis_size(axis)
    if size & (size - 1):
        return lax.psum(value, axis)
    step = 1
    while step < size:
        value = value + lax.ppermute(value, axis, [(i, i ^ step) for i in range(size)])
        step *= 2
    return value


def y_roll(x, shift):
    return pltpu.roll(x, shift % x.shape[-1], x.ndim - 1)


def z_roll(x, shift):
    axis = x.ndim - 3
    n = x.shape[axis]
    s = shift % n
    if s == 0:
        return x
    return jnp.concatenate(
        [lax.slice_in_dim(x, n - s, n, axis=axis), lax.slice_in_dim(x, 0, n - s, axis=axis)], axis
    )


def field_rows(vector, bond, lo, n):
    up = vector(lo + 2, lo + n)
    down = vector(lo, lo + n - 2)
    centre = vector(lo + 1, lo + n - 1)
    total = bond(0, lo + 1, lo + n - 1) * up + bond(0, lo, lo + n - 2) * down
    bond_y = bond(1, lo + 1, lo + n - 1)
    total = total + bond_y * y_roll(centre, -1) + y_roll(bond_y, 1) * y_roll(centre, 1)
    bond_z = bond(2, lo + 1, lo + n - 1)
    total = total + bond_z * z_roll(centre, -1) + z_roll(bond_z, 1) * z_roll(centre, 1)
    return total


def local_kernel(halo, slab_rows, *refs):
    slab_refs = refs[:2 * HALO_SLABS + 1]
    start_ref, exchange_ref, relaxed_ref, last_ref, sums_ref, win, sweep_a, sweep_b, bonds_b, bonds_yr, bonds_zr, spins_b, t1, t2, t3 = refs[2 * HALO_SLABS + 1:]
    for k, slab_ref in enumerate(slab_refs):
        block = slab_ref[...]
        cos_polar, azimuth, bond_class = block[0], block[1], block[2:5]
        radial = jnp.sqrt(1.0 - cos_polar * cos_polar)
        strengths = jnp.zeros(bond_class.shape, jnp.float32)
        for class_index in range(NCLASS):
            strengths = jnp.where(bond_class == class_index, exchange_ref[class_index], strengths)
        site = jnp.stack([radial * jnp.cos(azimuth), radial * jnp.sin(azimuth), cos_polar], 0)
        win[:, :, k * slab_rows:(k + 1) * slab_rows, :] = jnp.concatenate([site, strengths], 0)
    width = len(slab_refs) * slab_rows

    def bond(d, a, b):
        return win[3 + d, :, a:b, :]

    def from_window(a, b):
        return win[0:3, :, a:b, :]

    def from_a(a, b):
        return sweep_a[:, :, a - 1:b - 1, :]

    rows_a = width - 2
    sweep_a[:, :, 0:rows_a, :] = relax_update(win[0:3, :, 1:width - 1, :], field_rows(from_window, bond, 0, width))
    rows_b = width - 4
    sweep_b[:, :, 0:rows_b, :] = relax_update(sweep_a[:, :, 1:rows_a - 1, :], field_rows(from_a, bond, 1, width - 2))
    relaxed_ref[...] = sweep_b[:, :, halo - SWEEPS:halo - SWEEPS + slab_rows, :]

    first = halo - CHEB
    n_start = slab_rows + 2 * CHEB
    lanes = win.shape[3]
    depth = win.shape[1]
    probes = start_ref.shape[4]
    for xr in range(n_start):
        w = first + xr
        site = jnp.broadcast_to(win[3:6, :, w:w + 1, :], (3, depth, probes, lanes))
        bonds_b[xr] = site
        bonds_yr[xr] = y_roll(site[1], 1)
        bonds_zr[xr] = z_roll(site[2], 1)
    for xr in range(n_start - 2):
        w = first + 1 + xr
        spins_b[xr] = jnp.broadcast_to(sweep_b[:, :, w - SWEEPS:w - SWEEPS + 1, :], (3, depth, probes, lanes))

    t_refs = (start_ref, t1, t2, t3, last_ref)
    for order in range(CHEB):
        lo = first + order
        n = n_start - 2 * order
        source = t_refs[order]
        target = t_refs[order + 1]
        acc = None
        for i in range(n - 2):
            w = lo + 1 + i
            b = w - first
            up = source[i + 2]
            down = source[i]
            centre = source[i + 1]
            total = bonds_b[b, 0] * up + bonds_b[b - 1, 0] * down
            total = total + bonds_b[b, 1] * y_roll(centre, -1) + bonds_yr[b] * y_roll(centre, 1)
            total = total + bonds_b[b, 2] * z_roll(centre, -1) + bonds_zr[b] * z_roll(centre, 1)
            advanced = cross_product(spins_b[b - 1], total) * -precess_scale
            if order > 0:
                advanced = 2.0 * advanced - t_refs[order - 1][i + 2]
            target[i] = advanced
            if halo <= w < halo + slab_rows:
                squares = advanced * advanced
                part = squares[0] + squares[1]
                part = part[0] + part[1] + part[2]
                part = part[0] + part[1] + part[2] + part[3]
                acc = part if acc is None else acc + part
        sums_ref[order:order + 1, :] = jnp.sum(acc.T, axis=0, keepdims=True)


def run_local(slab_blocks, start, exchange, halo, slab_rows):
    depth, lanes = slab_blocks[0].shape[1], slab_blocks[0].shape[3]
    width = len(slab_blocks) * slab_rows
    n_start, probes = start.shape[0], start.shape[4]
    vec_shape = start.shape[1:]

    def body(*refs):
        local_kernel(halo, slab_rows, *refs)

    sites = n_start * start[0].size
    return pl.pallas_call(
        body,
        out_shape=(
            jax.ShapeDtypeStruct((3, depth, slab_rows, lanes), jnp.float32),
            jax.ShapeDtypeStruct((slab_rows,) + vec_shape, jnp.float32),
            jax.ShapeDtypeStruct((CHEB, probes), jnp.float32),
        ),
        in_specs=[pl.BlockSpec(memory_space=pltpu.VMEM)] * (len(slab_blocks) + 1)
        + [pl.BlockSpec(memory_space=pltpu.SMEM)],
        out_specs=[pl.BlockSpec(memory_space=pltpu.VMEM)] * 3,
        scratch_shapes=[
            pltpu.VMEM((6, depth, width, lanes), jnp.float32),
            pltpu.VMEM((3, depth, width, lanes), jnp.float32),
            pltpu.VMEM((3, depth, width, lanes), jnp.float32),
            pltpu.VMEM((n_start, 3, depth, probes, lanes), jnp.float32),
            pltpu.VMEM((n_start, depth, probes, lanes), jnp.float32),
            pltpu.VMEM((n_start, depth, probes, lanes), jnp.float32),
            pltpu.VMEM((n_start, 3, depth, probes, lanes), jnp.float32),
        ]
        + [pltpu.VMEM((n_start - 2 * k,) + vec_shape, jnp.float32) for k in range(1, CHEB)],
        cost_estimate=pl.CostEstimate(
            flops=30 * sites + 200 * 3 * depth * width * lanes,
            transcendentals=0,
            bytes_accessed=4 * (6 * depth * width * lanes + start.size + start.size // 3),
        ),
    )(*slab_blocks, start, exchange)


def shards(cos_polar, azimuth, bond_class, exchange, probe_wave):
    groups = lax.axis_size("probe")
    slabs = lax.axis_size("space")
    group = lax.axis_index("probe")
    slab = lax.axis_index("space")
    slab_rows = cos_polar.shape[1]
    block_y = cos_polar.shape[2]
    total_x = slab_rows * slabs
    total_y = block_y * groups
    site_count = total_x * total_y * LZ

    local = jnp.concatenate([cos_polar[None], azimuth[None], bond_class.astype(jnp.float32)], 0)

    pieces = [shifted(local, "probe", k) for k in range(groups)]
    rotated = jnp.concatenate(pieces, -1)
    full_y = jnp.roll(rotated, group * block_y, -1) if groups > 1 else rotated

    slab_blocks = [shifted(full_y, "space", k) for k in range(-HALO_SLABS, HALO_SLABS + 1)]
    halo = HALO_SLABS * slab_rows

    width = slab_rows + 2 * CHEB
    x_coords = (slab * slab_rows - CHEB + jnp.arange(width, dtype=jnp.int32)) % total_x
    y_coords = jnp.arange(total_y, dtype=jnp.int32)
    group_size = probe_wave.shape[0]
    probe_ids = group * group_size + jnp.arange(group_size, dtype=jnp.int32)
    start = make_probes(probe_wave, probe_ids, x_coords, y_coords, total_x, total_y, LZ)
    start = jnp.transpose(start, (4, 1, 2, 3, 0, 5))

    relaxed, last, sums = run_local(slab_blocks, start, exchange, halo, slab_rows)
    relaxed_own = lax.dynamic_slice_in_dim(relaxed, group * block_y, block_y, -1)
    last = jnp.transpose(last, (4, 1, 2, 3, 0, 5)).astype(jnp.bfloat16)
    moment_rows = butterfly_sum(sums, "space") / site_count
    return (relaxed_own, last, moment_rows.T)


def solution(mesh):
    return jax.shard_map(
        shards,
        mesh=mesh,
        in_specs=(
            P(None, "space", "probe"),
            P(None, "space", "probe"),
            P(None, None, "space", "probe"),
            P(),
            P("probe", None),
        ),
        out_specs=(
            P(None, None, "space", "probe"),
            P("probe", None, None, None, "space", None),
            P("probe", None),
        ),
        check_vma=False,
    )
```

```python
import math

import jax
import jax.numpy as jnp
from jax import lax
from jax.experimental import pallas as pl
from jax.experimental.pallas import tpu as pltpu
from jax.sharding import PartitionSpec as P

LZ = 4
SWEEPS = 2
CHEB = 4
NCLASS = 8


relax_rate = 0.15
precess_scale = 1.0 / 6.0


def shifted(array, axis, shift):
    size = lax.axis_size(axis)
    if shift % size == 0:
        return array
    return lax.ppermute(array, axis, [(i, (i - shift) % size) for i in range(size)])


def cross_product(spin_core, vector):
    spin_a, spin_b, spin_c = (spin_core[0], spin_core[1], spin_core[2])
    vec_a = vector[..., 0, :, :, :]
    vec_b = vector[..., 1, :, :, :]
    vec_c = vector[..., 2, :, :, :]
    return jnp.stack(
        [
            spin_b * vec_c - spin_c * vec_b,
            spin_c * vec_a - spin_a * vec_c,
            spin_a * vec_b - spin_b * vec_a,
        ],
        axis=-4,
    )


def rows(array, start, stop):
    return lax.slice_in_dim(array, start, stop, axis=array.ndim - 2)


def neighbour_window(vector, bonds):
    n = vector.shape[-2]
    along_x, along_y, along_z = (bonds[0], bonds[1], bonds[2])
    total = rows(along_x, 1, n - 1) * rows(vector, 2, n) + rows(along_x, 0, n - 2) * rows(vector, 0, n - 2)
    centre = rows(vector, 1, n - 1)
    bond_y = rows(along_y, 1, n - 1)
    total = total + bond_y * jnp.roll(centre, -1, -1) + jnp.roll(bond_y, 1, -1) * jnp.roll(centre, 1, -1)
    bond_z = rows(along_z, 1, n - 1)
    total = total + bond_z * jnp.roll(centre, -1, -3) + jnp.roll(bond_z, 1, -3) * jnp.roll(centre, 1, -3)
    return total


def relax_update(spins, field):
    turned = cross_product(spins, field)
    twice = cross_product(spins, turned)
    moved = spins - relax_rate * twice
    length = jnp.sqrt(jnp.sum(moved * moved, axis=0))
    return moved / length


def make_probes(probe_wave, probe_ids, x_coords, y_coords, total_x, total_y, depth_z):
    wave_x = probe_wave[:, 0][:, None]
    wave_y = probe_wave[:, 1][:, None]
    wave_z = probe_wave[:, 2][:, None]
    phase_x = wave_x * x_coords[None, :] % total_x
    phase_y = wave_y * y_coords[None, :] % total_y
    phase_z = wave_z * jnp.arange(depth_z, dtype=jnp.int32)[None, :] % depth_z
    fraction = (
        phase_z[:, :, None, None].astype(jnp.float32) / depth_z
        + phase_x[:, None, :, None].astype(jnp.float32) / total_x
        + phase_y[:, None, None, :].astype(jnp.float32) / total_y
    )
    angle = 2.0 * math.pi * fraction
    ramp = jnp.sqrt(1.0 + 2.0 * x_coords.astype(jnp.float32) / total_x)[None, None, :, None]
    waves = jnp.stack([jnp.cos(angle) * ramp, jnp.sin(angle) * ramp], 1)
    polar = ((probe_ids % 3)[:, None] == jnp.arange(3, dtype=jnp.int32)[None, :]).astype(
        jnp.float32
    )
    return waves[:, :, None] * polar[:, None, :, None, None, None]


def butterfly_sum(value, axis):
    size = lax.axis_size(axis)
    if size & (size - 1):
        return lax.psum(value, axis)
    step = 1
    while step < size:
        value = value + lax.ppermute(value, axis, [(i, i ^ step) for i in range(size)])
        step *= 2
    return value


def y_roll(x, shift):
    return pltpu.roll(x, shift % x.shape[-1], x.ndim - 1)


def z_roll(x, shift):
    axis = x.ndim - 3
    n = x.shape[axis]
    s = shift % n
    if s == 0:
        return x
    return jnp.concatenate(
        [lax.slice_in_dim(x, n - s, n, axis=axis), lax.slice_in_dim(x, 0, n - s, axis=axis)], axis
    )


def field_rows(vector, bond, lo, n):
    up = vector(lo + 2, lo + n)
    down = vector(lo, lo + n - 2)
    centre = vector(lo + 1, lo + n - 1)
    total = bond(0, lo + 1, lo + n - 1) * up + bond(0, lo, lo + n - 2) * down
    bond_y = bond(1, lo + 1, lo + n - 1)
    total = total + bond_y * y_roll(centre, -1) + y_roll(bond_y, 1) * y_roll(centre, 1)
    bond_z = bond(2, lo + 1, lo + n - 1)
    total = total + bond_z * z_roll(centre, -1) + z_roll(bond_z, 1) * z_roll(centre, 1)
    return total


def local_kernel(halo, slab_rows, scale, n_blocks, *refs):
    slab_refs = refs[:n_blocks]
    start_ref, exchange_ref, relaxed_ref, last_ref, sums_ref, win, sweep_a, sweep_b, bonds_b, bonds_yr, bonds_zr, spins_b, t1, t2, t3 = refs[n_blocks:]
    offset = 0
    for slab_ref in slab_refs:
        count = slab_ref.shape[2]
        block = slab_ref[...]
        cos_polar, azimuth, bond_class = block[0], block[1], block[2:5]
        radial = jnp.sqrt(1.0 - cos_polar * cos_polar)
        strengths = jnp.zeros(bond_class.shape, jnp.float32)
        for class_index in range(NCLASS):
            strengths = jnp.where(bond_class == class_index, exchange_ref[class_index], strengths)
        site = jnp.stack([radial * jnp.cos(azimuth), radial * jnp.sin(azimuth), cos_polar], 0)
        win[:, :, offset:offset + count, :] = jnp.concatenate([site, strengths], 0)
        offset += count
    width = offset

    def bond(d, a, b):
        return win[3 + d, :, a:b, :]

    def from_window(a, b):
        return win[0:3, :, a:b, :]

    def from_a(a, b):
        return sweep_a[:, :, a - 1:b - 1, :]

    rows_a = width - 2
    sweep_a[:, :, 0:rows_a, :] = relax_update(win[0:3, :, 1:width - 1, :], field_rows(from_window, bond, 0, width))
    rows_b = width - 4
    sweep_b[:, :, 0:rows_b, :] = relax_update(sweep_a[:, :, 1:rows_a - 1, :], field_rows(from_a, bond, 1, width - 2))
    relaxed_ref[...] = sweep_b[:, :, halo - SWEEPS:halo - SWEEPS + slab_rows, :]

    first = halo - CHEB
    n_start = slab_rows + 2 * CHEB
    lanes = win.shape[3]
    depth = win.shape[1]
    probes = start_ref.shape[4]
    for xr in range(n_start):
        w = first + xr
        site = jnp.broadcast_to(win[3:6, :, w:w + 1, :], (3, depth, probes, lanes))
        bonds_b[xr] = site
        bonds_yr[xr] = y_roll(site[1], 1)
        bonds_zr[xr] = z_roll(site[2], 1)
    for xr in range(n_start - 2):
        w = first + 1 + xr
        spins_b[xr] = jnp.broadcast_to(sweep_b[:, :, w - SWEEPS:w - SWEEPS + 1, :], (3, depth, probes, lanes))

    t_refs = (start_ref, t1, t2, t3, last_ref)
    for order in range(CHEB):
        lo = first + order
        n = n_start - 2 * order
        source = t_refs[order]
        target = t_refs[order + 1]
        acc = None
        for i in range(n - 2):
            w = lo + 1 + i
            b = w - first
            up = source[i + 2]
            down = source[i]
            centre = source[i + 1]
            total = bonds_b[b, 0] * up + bonds_b[b - 1, 0] * down
            total = total + bonds_b[b, 1] * y_roll(centre, -1) + bonds_yr[b] * y_roll(centre, 1)
            total = total + bonds_b[b, 2] * z_roll(centre, -1) + bonds_zr[b] * z_roll(centre, 1)
            advanced = cross_product(spins_b[b - 1], total) * -precess_scale
            if order > 0:
                advanced = 2.0 * advanced - t_refs[order - 1][i + 2]
            target[i] = advanced
            if halo <= w < halo + slab_rows:
                squares = advanced * advanced
                part = squares[0] + squares[1]
                part = part[0] + part[1] + part[2]
                part = part[0] + part[1] + part[2] + part[3]
                acc = part if acc is None else acc + part
        sums_ref[order:order + 1, :] = jnp.sum(acc.T, axis=0, keepdims=True) * scale


def run_local(slab_blocks, start, exchange, halo, slab_rows, site_count):
    depth, lanes = slab_blocks[0].shape[1], slab_blocks[0].shape[3]
    width = sum(block.shape[2] for block in slab_blocks)
    n_start, probes = start.shape[0], start.shape[4]
    vec_shape = start.shape[1:]

    def body(*refs):
        local_kernel(halo, slab_rows, 1.0 / site_count, len(slab_blocks), *refs)

    sites = n_start * start[0].size
    return pl.pallas_call(
        body,
        out_shape=(
            jax.ShapeDtypeStruct((3, depth, slab_rows, lanes), jnp.float32),
            jax.ShapeDtypeStruct((slab_rows,) + vec_shape, jnp.float32),
            jax.ShapeDtypeStruct((CHEB, probes), jnp.float32),
        ),
        in_specs=[pl.BlockSpec(memory_space=pltpu.VMEM)] * (len(slab_blocks) + 1)
        + [pl.BlockSpec(memory_space=pltpu.SMEM)],
        out_specs=[pl.BlockSpec(memory_space=pltpu.VMEM)] * 3,
        scratch_shapes=[
            pltpu.VMEM((6, depth, width, lanes), jnp.float32),
            pltpu.VMEM((3, depth, width, lanes), jnp.float32),
            pltpu.VMEM((3, depth, width, lanes), jnp.float32),
            pltpu.VMEM((n_start, 3, depth, probes, lanes), jnp.float32),
            pltpu.VMEM((n_start, depth, probes, lanes), jnp.float32),
            pltpu.VMEM((n_start, depth, probes, lanes), jnp.float32),
            pltpu.VMEM((n_start, 3, depth, probes, lanes), jnp.float32),
        ]
        + [pltpu.VMEM((n_start - 2 * k,) + vec_shape, jnp.float32) for k in range(1, CHEB)],
        cost_estimate=pl.CostEstimate(
            flops=30 * sites + 200 * 3 * depth * width * lanes,
            transcendentals=0,
            bytes_accessed=4 * (6 * depth * width * lanes + start.size + start.size // 3),
        ),
    )(*slab_blocks, start, exchange)


def shards(cos_polar, azimuth, bond_class, exchange, probe_wave):
    groups = lax.axis_size("probe")
    slabs = lax.axis_size("space")
    group = lax.axis_index("probe")
    slab = lax.axis_index("space")
    slab_rows = cos_polar.shape[1]
    block_y = cos_polar.shape[2]
    total_x = slab_rows * slabs
    total_y = block_y * groups
    site_count = total_x * total_y * LZ

    local = jnp.concatenate([cos_polar[None], azimuth[None], bond_class.astype(jnp.float32)], 0)

    pieces = [shifted(local, "probe", k) for k in range(groups)]
    rotated = jnp.concatenate(pieces, -1)
    full_y = jnp.roll(rotated, group * block_y, -1) if groups > 1 else rotated

    halo = SWEEPS + CHEB - 1
    reach = -(-halo // slab_rows)
    slab_blocks = []
    for k in range(-reach, reach + 1):
        low = max(k * slab_rows, -halo) - k * slab_rows
        high = min((k + 1) * slab_rows, slab_rows + halo) - k * slab_rows
        slab_blocks.append(shifted(full_y[:, :, low:high, :], "space", k))

    width = slab_rows + 2 * CHEB
    x_coords = (slab * slab_rows - CHEB + jnp.arange(width, dtype=jnp.int32)) % total_x
    y_coords = jnp.arange(total_y, dtype=jnp.int32)
    group_size = probe_wave.shape[0]
    probe_ids = group * group_size + jnp.arange(group_size, dtype=jnp.int32)
    start = make_probes(probe_wave, probe_ids, x_coords, y_coords, total_x, total_y, LZ)
    start = jnp.transpose(start, (4, 1, 2, 3, 0, 5))

    relaxed, last, sums = run_local(slab_blocks, start, exchange, halo, slab_rows, site_count)
    relaxed_own = lax.dynamic_slice_in_dim(relaxed, group * block_y, block_y, -1)
    last = jnp.transpose(last, (4, 1, 2, 3, 0, 5)).astype(jnp.bfloat16)
    moment_rows = butterfly_sum(sums, "space")
    return (relaxed_own, last, moment_rows.T)


def solution(mesh):
    return jax.shard_map(
        shards,
        mesh=mesh,
        in_specs=(
            P(None, "space", "probe"),
            P(None, "space", "probe"),
            P(None, None, "space", "probe"),
            P(),
            P("probe", None),
        ),
        out_specs=(
            P(None, None, "space", "probe"),
            P("probe", None, None, None, "space", None),
            P("probe", None),
        ),
        check_vma=False,
    )
```

```python
import math

import jax
import jax.numpy as jnp
from jax import lax
from jax.experimental import pallas as pl
from jax.experimental.pallas import tpu as pltpu
from jax.sharding import PartitionSpec as P

LZ = 4
SWEEPS = 2
CHEB = 4
HALO_SLABS = 2
NCLASS = 8


relax_rate = 0.15
precess_scale = 1.0 / 6.0


def shifted(array, axis, shift):
    size = lax.axis_size(axis)
    if shift % size == 0:
        return array
    return lax.ppermute(array, axis, [(i, (i - shift) % size) for i in range(size)])


def cross_product(spin_core, vector):
    spin_a, spin_b, spin_c = (spin_core[0], spin_core[1], spin_core[2])
    vec_a = vector[..., 0, :, :, :]
    vec_b = vector[..., 1, :, :, :]
    vec_c = vector[..., 2, :, :, :]
    return jnp.stack(
        [
            spin_b * vec_c - spin_c * vec_b,
            spin_c * vec_a - spin_a * vec_c,
            spin_a * vec_b - spin_b * vec_a,
        ],
        axis=-4,
    )


def rows(array, start, stop):
    return lax.slice_in_dim(array, start, stop, axis=array.ndim - 2)


def neighbour_window(vector, bonds):
    n = vector.shape[-2]
    along_x, along_y, along_z = (bonds[0], bonds[1], bonds[2])
    total = rows(along_x, 1, n - 1) * rows(vector, 2, n) + rows(along_x, 0, n - 2) * rows(vector, 0, n - 2)
    centre = rows(vector, 1, n - 1)
    bond_y = rows(along_y, 1, n - 1)
    total = total + bond_y * jnp.roll(centre, -1, -1) + jnp.roll(bond_y, 1, -1) * jnp.roll(centre, 1, -1)
    bond_z = rows(along_z, 1, n - 1)
    total = total + bond_z * jnp.roll(centre, -1, -3) + jnp.roll(bond_z, 1, -3) * jnp.roll(centre, 1, -3)
    return total


def relax_update(spins, field):
    turned = cross_product(spins, field)
    twice = cross_product(spins, turned)
    moved = spins - relax_rate * twice
    length = jnp.sqrt(jnp.sum(moved * moved, axis=0))
    return moved / length


def make_probes(probe_wave, probe_ids, x_coords, y_coords, total_x, total_y, depth_z):
    wave_x = probe_wave[:, 0][:, None]
    wave_y = probe_wave[:, 1][:, None]
    wave_z = probe_wave[:, 2][:, None]
    phase_x = wave_x * x_coords[None, :] % total_x
    phase_y = wave_y * y_coords[None, :] % total_y
    phase_z = wave_z * jnp.arange(depth_z, dtype=jnp.int32)[None, :] % depth_z
    fraction = (
        phase_z[:, :, None, None].astype(jnp.float32) / depth_z
        + phase_x[:, None, :, None].astype(jnp.float32) / total_x
        + phase_y[:, None, None, :].astype(jnp.float32) / total_y
    )
    angle = 2.0 * math.pi * fraction
    ramp = jnp.sqrt(1.0 + 2.0 * x_coords.astype(jnp.float32) / total_x)[None, None, :, None]
    waves = jnp.stack([jnp.cos(angle) * ramp, jnp.sin(angle) * ramp], 1)
    polar = ((probe_ids % 3)[:, None] == jnp.arange(3, dtype=jnp.int32)[None, :]).astype(
        jnp.float32
    )
    return waves[:, :, None] * polar[:, None, :, None, None, None]


def butterfly_sum(value, axis):
    size = lax.axis_size(axis)
    if size & (size - 1):
        return lax.psum(value, axis)
    step = 1
    while step < size:
        value = value + lax.ppermute(value, axis, [(i, i ^ step) for i in range(size)])
        step *= 2
    return value


def y_roll(x, shift):
    return pltpu.roll(x, shift % x.shape[-1], x.ndim - 1)


def z_roll(x, shift):
    axis = x.ndim - 3
    n = x.shape[axis]
    s = shift % n
    if s == 0:
        return x
    return jnp.concatenate(
        [lax.slice_in_dim(x, n - s, n, axis=axis), lax.slice_in_dim(x, 0, n - s, axis=axis)], axis
    )


def field_rows(vector, bond, lo, n):
    up = vector(lo + 2, lo + n)
    down = vector(lo, lo + n - 2)
    centre = vector(lo + 1, lo + n - 1)
    total = bond(0, lo + 1, lo + n - 1) * up + bond(0, lo, lo + n - 2) * down
    bond_y = bond(1, lo + 1, lo + n - 1)
    total = total + bond_y * y_roll(centre, -1) + y_roll(bond_y, 1) * y_roll(centre, 1)
    bond_z = bond(2, lo + 1, lo + n - 1)
    total = total + bond_z * z_roll(centre, -1) + z_roll(bond_z, 1) * z_roll(centre, 1)
    return total


def local_kernel(halo, slab_rows, raw_ref, start_ref, exchange_ref, relaxed_ref, last_ref, sums_ref, win, sweep_a, sweep_b, bonds_b, bonds_yr, bonds_zr, spins_b, t1, t2, t3):
    for k in range(2 * HALO_SLABS + 1):
        block = raw_ref[:, :, k * slab_rows:(k + 1) * slab_rows, :]
        cos_polar, azimuth, bond_class = block[0], block[1], block[2:5]
        radial = jnp.sqrt(1.0 - cos_polar * cos_polar)
        strengths = jnp.zeros(bond_class.shape, jnp.float32)
        for class_index in range(NCLASS):
            strengths = jnp.where(bond_class == class_index, exchange_ref[class_index], strengths)
        site = jnp.stack([radial * jnp.cos(azimuth), radial * jnp.sin(azimuth), cos_polar], 0)
        win[:, :, k * slab_rows:(k + 1) * slab_rows, :] = jnp.concatenate([site, strengths], 0)
    width = raw_ref.shape[2]

    def bond(d, a, b):
        return win[3 + d, :, a:b, :]

    def from_window(a, b):
        return win[0:3, :, a:b, :]

    def from_a(a, b):
        return sweep_a[:, :, a - 1:b - 1, :]

    rows_a = width - 2
    sweep_a[:, :, 0:rows_a, :] = relax_update(win[0:3, :, 1:width - 1, :], field_rows(from_window, bond, 0, width))
    rows_b = width - 4
    sweep_b[:, :, 0:rows_b, :] = relax_update(sweep_a[:, :, 1:rows_a - 1, :], field_rows(from_a, bond, 1, width - 2))
    relaxed_ref[...] = sweep_b[:, :, halo - SWEEPS:halo - SWEEPS + slab_rows, :]

    first = halo - CHEB
    n_start = slab_rows + 2 * CHEB
    lanes = win.shape[3]
    depth = win.shape[1]
    probes = start_ref.shape[4]
    for xr in range(n_start):
        w = first + xr
        site = jnp.broadcast_to(win[3:6, :, w:w + 1, :], (3, depth, probes, lanes))
        bonds_b[xr] = site
        bonds_yr[xr] = y_roll(site[1], 1)
        bonds_zr[xr] = z_roll(site[2], 1)
    for xr in range(n_start - 2):
        w = first + 1 + xr
        spins_b[xr] = jnp.broadcast_to(sweep_b[:, :, w - SWEEPS:w - SWEEPS + 1, :], (3, depth, probes, lanes))

    t_refs = (start_ref, t1, t2, t3, last_ref)
    for order in range(CHEB):
        lo = first + order
        n = n_start - 2 * order
        source = t_refs[order]
        target = t_refs[order + 1]
        acc = None
        for i in range(n - 2):
            w = lo + 1 + i
            b = w - first
            up = source[i + 2]
            down = source[i]
            centre = source[i + 1]
            total = bonds_b[b, 0] * up + bonds_b[b - 1, 0] * down
            total = total + bonds_b[b, 1] * y_roll(centre, -1) + bonds_yr[b] * y_roll(centre, 1)
            total = total + bonds_b[b, 2] * z_roll(centre, -1) + bonds_zr[b] * z_roll(centre, 1)
            advanced = cross_product(spins_b[b - 1], total) * -precess_scale
            if order > 0:
                advanced = 2.0 * advanced - t_refs[order - 1][i + 2]
            target[i] = advanced
            if halo <= w < halo + slab_rows:
                squares = advanced * advanced
                part = squares[0] + squares[1]
                part = part[0] + part[1] + part[2]
                part = part[0] + part[1] + part[2] + part[3]
                acc = part if acc is None else acc + part
        sums_ref[order:order + 1, :] = jnp.sum(acc.T, axis=0, keepdims=True)


def run_local(raw, start, exchange, halo, slab_rows):
    depth, width, lanes = raw.shape[1], raw.shape[2], raw.shape[3]
    n_start, probes = start.shape[0], start.shape[4]
    vec_shape = start.shape[1:]

    def body(*refs):
        local_kernel(halo, slab_rows, *refs)

    sites = n_start * start[0].size
    return pl.pallas_call(
        body,
        out_shape=(
            jax.ShapeDtypeStruct((3, depth, slab_rows, lanes), jnp.float32),
            jax.ShapeDtypeStruct((slab_rows,) + vec_shape, jnp.float32),
            jax.ShapeDtypeStruct((CHEB, probes), jnp.float32),
        ),
        in_specs=[pl.BlockSpec(memory_space=pltpu.VMEM)] * 2
        + [pl.BlockSpec(memory_space=pltpu.SMEM)],
        out_specs=[pl.BlockSpec(memory_space=pltpu.VMEM)] * 3,
        scratch_shapes=[
            pltpu.VMEM((6, depth, width, lanes), jnp.float32),
            pltpu.VMEM((3, depth, width, lanes), jnp.float32),
            pltpu.VMEM((3, depth, width, lanes), jnp.float32),
            pltpu.VMEM((n_start, 3, depth, probes, lanes), jnp.float32),
            pltpu.VMEM((n_start, depth, probes, lanes), jnp.float32),
            pltpu.VMEM((n_start, depth, probes, lanes), jnp.float32),
            pltpu.VMEM((n_start, 3, depth, probes, lanes), jnp.float32),
        ]
        + [pltpu.VMEM((n_start - 2 * k,) + vec_shape, jnp.float32) for k in range(1, CHEB)],
        cost_estimate=pl.CostEstimate(
            flops=30 * sites + 200 * 3 * depth * width * lanes,
            transcendentals=0,
            bytes_accessed=4 * (6 * depth * width * lanes + start.size + start.size // 3),
        ),
    )(raw, start, exchange)


def shards(cos_polar, azimuth, bond_class, exchange, probe_wave):
    groups = lax.axis_size("probe")
    slabs = lax.axis_size("space")
    group = lax.axis_index("probe")
    slab = lax.axis_index("space")
    slab_rows = cos_polar.shape[1]
    block_y = cos_polar.shape[2]
    total_x = slab_rows * slabs
    total_y = block_y * groups
    site_count = total_x * total_y * LZ

    local = jnp.concatenate([cos_polar[None], azimuth[None], bond_class.astype(jnp.float32)], 0)

    half = jnp.concatenate(
        [shifted(local, "space", k) for k in range(-HALO_SLABS, HALO_SLABS + 1)], 2
    )
    halo = HALO_SLABS * slab_rows
    raw = jnp.concatenate([shifted(half, "probe", k) for k in range(groups)], -1)

    width = slab_rows + 2 * CHEB
    x_coords = (slab * slab_rows - CHEB + jnp.arange(width, dtype=jnp.int32)) % total_x
    y_coords = (group * block_y + jnp.arange(total_y, dtype=jnp.int32)) % total_y
    group_size = probe_wave.shape[0]
    probe_ids = group * group_size + jnp.arange(group_size, dtype=jnp.int32)
    start = make_probes(probe_wave, probe_ids, x_coords, y_coords, total_x, total_y, LZ)
    start = jnp.transpose(start, (4, 1, 2, 3, 0, 5))

    relaxed, last, sums = run_local(raw, start, exchange, halo, slab_rows)
    relaxed_own = relaxed[..., :block_y]
    last = jnp.transpose(last, (4, 1, 2, 3, 0, 5)).astype(jnp.bfloat16)
    if groups > 1:
        last = jnp.roll(last, group * block_y, -1)
    moment_rows = butterfly_sum(sums, "space") / site_count
    return (relaxed_own, last, moment_rows.T)


def solution(mesh):
    return jax.shard_map(
        shards,
        mesh=mesh,
        in_specs=(
            P(None, "space", "probe"),
            P(None, "space", "probe"),
            P(None, None, "space", "probe"),
            P(),
            P("probe", None),
        ),
        out_specs=(
            P(None, None, "space", "probe"),
            P("probe", None, None, None, "space", None),
            P("probe", None),
        ),
        check_vma=False,
    )
```

```python
import math

import jax
import jax.numpy as jnp
from jax import lax
from jax.experimental import pallas as pl
from jax.experimental.pallas import tpu as pltpu
from jax.sharding import PartitionSpec as P

LZ = 4
SWEEPS = 2
CHEB = 4
NCLASS = 8


relax_rate = 0.15
precess_scale = 1.0 / 6.0


def shifted(array, axis, shift):
    size = lax.axis_size(axis)
    if shift % size == 0:
        return array
    return lax.ppermute(array, axis, [(i, (i - shift) % size) for i in range(size)])


def cross_product(spin_core, vector):
    spin_a, spin_b, spin_c = (spin_core[0], spin_core[1], spin_core[2])
    vec_a = vector[..., 0, :, :, :]
    vec_b = vector[..., 1, :, :, :]
    vec_c = vector[..., 2, :, :, :]
    return jnp.stack(
        [
            spin_b * vec_c - spin_c * vec_b,
            spin_c * vec_a - spin_a * vec_c,
            spin_a * vec_b - spin_b * vec_a,
        ],
        axis=-4,
    )


def rows(array, start, stop):
    return lax.slice_in_dim(array, start, stop, axis=array.ndim - 2)


def neighbour_window(vector, bonds):
    n = vector.shape[-2]
    along_x, along_y, along_z = (bonds[0], bonds[1], bonds[2])
    total = rows(along_x, 1, n - 1) * rows(vector, 2, n) + rows(along_x, 0, n - 2) * rows(vector, 0, n - 2)
    centre = rows(vector, 1, n - 1)
    bond_y = rows(along_y, 1, n - 1)
    total = total + bond_y * jnp.roll(centre, -1, -1) + jnp.roll(bond_y, 1, -1) * jnp.roll(centre, 1, -1)
    bond_z = rows(along_z, 1, n - 1)
    total = total + bond_z * jnp.roll(centre, -1, -3) + jnp.roll(bond_z, 1, -3) * jnp.roll(centre, 1, -3)
    return total


def relax_update(spins, field):
    turned = cross_product(spins, field)
    twice = cross_product(spins, turned)
    moved = spins - relax_rate * twice
    length = jnp.sqrt(jnp.sum(moved * moved, axis=0))
    return moved / length


def make_probes(probe_wave, probe_ids, x_coords, y_coords, total_x, total_y, depth_z):
    wave_x = probe_wave[:, 0][:, None]
    wave_y = probe_wave[:, 1][:, None]
    wave_z = probe_wave[:, 2][:, None]
    phase_x = wave_x * x_coords[None, :] % total_x
    phase_y = wave_y * y_coords[None, :] % total_y
    phase_z = wave_z * jnp.arange(depth_z, dtype=jnp.int32)[None, :] % depth_z
    fraction = (
        phase_z[:, :, None, None].astype(jnp.float32) / depth_z
        + phase_x[:, None, :, None].astype(jnp.float32) / total_x
        + phase_y[:, None, None, :].astype(jnp.float32) / total_y
    )
    angle = 2.0 * math.pi * fraction
    ramp = jnp.sqrt(1.0 + 2.0 * x_coords.astype(jnp.float32) / total_x)[None, None, :, None]
    waves = jnp.stack([jnp.cos(angle) * ramp, jnp.sin(angle) * ramp], 1)
    polar = ((probe_ids % 3)[:, None] == jnp.arange(3, dtype=jnp.int32)[None, :]).astype(
        jnp.float32
    )
    return waves[:, :, None] * polar[:, None, :, None, None, None]


def butterfly_sum(value, axis):
    size = lax.axis_size(axis)
    if size & (size - 1):
        return lax.psum(value, axis)
    step = 1
    while step < size:
        value = value + lax.ppermute(value, axis, [(i, i ^ step) for i in range(size)])
        step *= 2
    return value


def y_roll(x, shift):
    return pltpu.roll(x, shift % x.shape[-1], x.ndim - 1)


def z_roll(x, shift):
    axis = x.ndim - 3
    n = x.shape[axis]
    s = shift % n
    if s == 0:
        return x
    return jnp.concatenate(
        [lax.slice_in_dim(x, n - s, n, axis=axis), lax.slice_in_dim(x, 0, n - s, axis=axis)], axis
    )


def field_rows(vector, bond, lo, n):
    up = vector(lo + 2, lo + n)
    down = vector(lo, lo + n - 2)
    centre = vector(lo + 1, lo + n - 1)
    total = bond(0, lo + 1, lo + n - 1) * up + bond(0, lo, lo + n - 2) * down
    bond_y = bond(1, lo + 1, lo + n - 1)
    total = total + bond_y * y_roll(centre, -1) + y_roll(bond_y, 1) * y_roll(centre, 1)
    bond_z = bond(2, lo + 1, lo + n - 1)
    total = total + bond_z * z_roll(centre, -1) + z_roll(bond_z, 1) * z_roll(centre, 1)
    return total


def local_kernel(halo, slab_rows, raw_ref, start_ref, exchange_ref, relaxed_ref, last_ref, sums_ref, win, sweep_a, sweep_b, bonds_b, bonds_yr, bonds_zr, spins_b, t1, t2, t3):
    block = raw_ref[...]
    cos_polar, azimuth, bond_class = block[0], block[1], block[2:5]
    radial = jnp.sqrt(1.0 - cos_polar * cos_polar)
    strengths = jnp.zeros(bond_class.shape, jnp.float32)
    for class_index in range(NCLASS):
        strengths = jnp.where(bond_class == class_index, exchange_ref[class_index], strengths)
    site = jnp.stack([radial * jnp.cos(azimuth), radial * jnp.sin(azimuth), cos_polar], 0)
    win[...] = jnp.concatenate([site, strengths], 0)
    width = raw_ref.shape[2]

    def bond(d, a, b):
        return win[3 + d, :, a:b, :]

    def from_window(a, b):
        return win[0:3, :, a:b, :]

    def from_a(a, b):
        return sweep_a[:, :, a - 1:b - 1, :]

    rows_a = width - 2
    sweep_a[:, :, 0:rows_a, :] = relax_update(win[0:3, :, 1:width - 1, :], field_rows(from_window, bond, 0, width))
    rows_b = width - 4
    sweep_b[:, :, 0:rows_b, :] = relax_update(sweep_a[:, :, 1:rows_a - 1, :], field_rows(from_a, bond, 1, width - 2))
    relaxed_ref[...] = sweep_b[:, :, halo - SWEEPS:halo - SWEEPS + slab_rows, :]

    first = halo - CHEB
    n_start = slab_rows + 2 * CHEB
    lanes = win.shape[3]
    depth = win.shape[1]
    probes = start_ref.shape[4]
    for xr in range(n_start):
        w = first + xr
        site = jnp.broadcast_to(win[3:6, :, w:w + 1, :], (3, depth, probes, lanes))
        bonds_b[xr] = site
        bonds_yr[xr] = y_roll(site[1], 1)
        bonds_zr[xr] = z_roll(site[2], 1)
    for xr in range(n_start - 2):
        w = first + 1 + xr
        spins_b[xr] = jnp.broadcast_to(sweep_b[:, :, w - SWEEPS:w - SWEEPS + 1, :], (3, depth, probes, lanes))

    t_refs = (start_ref, t1, t2, t3, last_ref)
    for order in range(CHEB):
        lo = first + order
        n = n_start - 2 * order
        source = t_refs[order]
        target = t_refs[order + 1]
        acc = None
        for i in range(n - 2):
            w = lo + 1 + i
            b = w - first
            up = source[i + 2]
            down = source[i]
            centre = source[i + 1]
            total = bonds_b[b, 0] * up + bonds_b[b - 1, 0] * down
            total = total + bonds_b[b, 1] * y_roll(centre, -1) + bonds_yr[b] * y_roll(centre, 1)
            total = total + bonds_b[b, 2] * z_roll(centre, -1) + bonds_zr[b] * z_roll(centre, 1)
            advanced = cross_product(spins_b[b - 1], total) * -precess_scale
            if order > 0:
                advanced = 2.0 * advanced - t_refs[order - 1][i + 2]
            target[i] = advanced
            if halo <= w < halo + slab_rows:
                squares = advanced * advanced
                part = squares[0] + squares[1]
                part = part[0] + part[1] + part[2]
                part = part[0] + part[1] + part[2] + part[3]
                acc = part if acc is None else acc + part
        sums_ref[order:order + 1, :] = jnp.sum(acc.T, axis=0, keepdims=True)


def run_local(raw, start, exchange, halo, slab_rows):
    depth, width, lanes = raw.shape[1], raw.shape[2], raw.shape[3]
    n_start, probes = start.shape[0], start.shape[4]
    vec_shape = start.shape[1:]

    def body(*refs):
        local_kernel(halo, slab_rows, *refs)

    sites = n_start * start[0].size
    return pl.pallas_call(
        body,
        out_shape=(
            jax.ShapeDtypeStruct((3, depth, slab_rows, lanes), jnp.float32),
            jax.ShapeDtypeStruct((slab_rows,) + vec_shape, jnp.float32),
            jax.ShapeDtypeStruct((CHEB, probes), jnp.float32),
        ),
        in_specs=[pl.BlockSpec(memory_space=pltpu.VMEM)] * 2
        + [pl.BlockSpec(memory_space=pltpu.SMEM)],
        out_specs=[pl.BlockSpec(memory_space=pltpu.VMEM)] * 3,
        scratch_shapes=[
            pltpu.VMEM((6, depth, width, lanes), jnp.float32),
            pltpu.VMEM((3, depth, width, lanes), jnp.float32),
            pltpu.VMEM((3, depth, width, lanes), jnp.float32),
            pltpu.VMEM((n_start, 3, depth, probes, lanes), jnp.float32),
            pltpu.VMEM((n_start, depth, probes, lanes), jnp.float32),
            pltpu.VMEM((n_start, depth, probes, lanes), jnp.float32),
            pltpu.VMEM((n_start, 3, depth, probes, lanes), jnp.float32),
        ]
        + [pltpu.VMEM((n_start - 2 * k,) + vec_shape, jnp.float32) for k in range(1, CHEB)],
        cost_estimate=pl.CostEstimate(
            flops=30 * sites + 200 * 3 * depth * width * lanes,
            transcendentals=0,
            bytes_accessed=4 * (6 * depth * width * lanes + start.size + start.size // 3),
        ),
    )(raw, start, exchange)


def shards(cos_polar, azimuth, bond_class, exchange, probe_wave):
    groups = lax.axis_size("probe")
    slabs = lax.axis_size("space")
    group = lax.axis_index("probe")
    slab = lax.axis_index("space")
    slab_rows = cos_polar.shape[1]
    block_y = cos_polar.shape[2]
    total_x = slab_rows * slabs
    total_y = block_y * groups
    site_count = total_x * total_y * LZ

    local = jnp.concatenate([cos_polar[None], azimuth[None], bond_class.astype(jnp.float32)], 0)

    def pair_block(array, group_shift):
        pairs = []
        for g in range(groups):
            for i in range(slabs):
                pairs.append((((g + group_shift) % groups) * slabs + (i ^ 1), g * slabs + i))
        return lax.ppermute(array, ("probe", "space"), pairs)

    mine = jnp.concatenate([shifted(local, "probe", k) for k in range(groups)], -1)
    beside = jnp.concatenate([pair_block(local, k) for k in range(groups)], -1)
    odd = slab % 2 == 1
    chip = jnp.where(odd, jnp.concatenate([beside, mine], 2), jnp.concatenate([mine, beside], 2))
    halo = SWEEPS + CHEB - 1
    pair_rows = 2 * slab_rows
    edge = halo
    before = shifted(chip[:, :, pair_rows - edge:, :], "space", -2)
    after = shifted(chip[:, :, :edge, :], "space", 2)
    rows_all = jnp.concatenate([before, chip, after], 2)
    window_rows = slab_rows + 2 * halo
    raw = lax.dynamic_slice_in_dim(rows_all, odd.astype(jnp.int32) * slab_rows, window_rows, 2)

    width = slab_rows + 2 * CHEB
    x_coords = (slab * slab_rows - CHEB + jnp.arange(width, dtype=jnp.int32)) % total_x
    y_coords = (group * block_y + jnp.arange(total_y, dtype=jnp.int32)) % total_y
    group_size = probe_wave.shape[0]
    probe_ids = group * group_size + jnp.arange(group_size, dtype=jnp.int32)
    start = make_probes(probe_wave, probe_ids, x_coords, y_coords, total_x, total_y, LZ)
    start = jnp.transpose(start, (4, 1, 2, 3, 0, 5))

    relaxed, last, sums = run_local(raw, start, exchange, halo, slab_rows)
    relaxed_own = relaxed[..., :block_y]
    last = jnp.transpose(last, (4, 1, 2, 3, 0, 5)).astype(jnp.bfloat16)
    if groups > 1:
        last = jnp.roll(last, group * block_y, -1)
    moment_rows = butterfly_sum(sums, "space") / site_count
    return (relaxed_own, last, moment_rows.T)


def solution(mesh):
    return jax.shard_map(
        shards,
        mesh=mesh,
        in_specs=(
            P(None, "space", "probe"),
            P(None, "space", "probe"),
            P(None, None, "space", "probe"),
            P(),
            P("probe", None),
        ),
        out_specs=(
            P(None, None, "space", "probe"),
            P("probe", None, None, None, "space", None),
            P("probe", None),
        ),
        check_vma=False,
    )
```

```python
import math

import jax
import jax.numpy as jnp
from jax import lax
from jax.experimental import pallas as pl
from jax.experimental.pallas import tpu as pltpu
from jax.sharding import PartitionSpec as P

LZ = 4
SWEEPS = 2
CHEB = 4
HALO_SLABS = 2
NCLASS = 8


relax_rate = 0.15
precess_scale = 1.0 / 6.0


def shifted(array, axis, shift):
    size = lax.axis_size(axis)
    if shift % size == 0:
        return array
    return lax.ppermute(array, axis, [(i, (i - shift) % size) for i in range(size)])


def cross_product(spin_core, vector):
    spin_a, spin_b, spin_c = (spin_core[0], spin_core[1], spin_core[2])
    vec_a = vector[..., 0, :, :, :]
    vec_b = vector[..., 1, :, :, :]
    vec_c = vector[..., 2, :, :, :]
    return jnp.stack(
        [
            spin_b * vec_c - spin_c * vec_b,
            spin_c * vec_a - spin_a * vec_c,
            spin_a * vec_b - spin_b * vec_a,
        ],
        axis=-4,
    )


def rows(array, start, stop):
    return lax.slice_in_dim(array, start, stop, axis=array.ndim - 2)


def neighbour_window(vector, bonds):
    n = vector.shape[-2]
    along_x, along_y, along_z = (bonds[0], bonds[1], bonds[2])
    total = rows(along_x, 1, n - 1) * rows(vector, 2, n) + rows(along_x, 0, n - 2) * rows(vector, 0, n - 2)
    centre = rows(vector, 1, n - 1)
    bond_y = rows(along_y, 1, n - 1)
    total = total + bond_y * jnp.roll(centre, -1, -1) + jnp.roll(bond_y, 1, -1) * jnp.roll(centre, 1, -1)
    bond_z = rows(along_z, 1, n - 1)
    total = total + bond_z * jnp.roll(centre, -1, -3) + jnp.roll(bond_z, 1, -3) * jnp.roll(centre, 1, -3)
    return total


def relax_update(spins, field):
    turned = cross_product(spins, field)
    twice = cross_product(spins, turned)
    moved = spins - relax_rate * twice
    length = jnp.sqrt(jnp.sum(moved * moved, axis=0))
    return moved / length


def make_probes(probe_wave, probe_ids, x_coords, y_coords, total_x, total_y, depth_z):
    wave_x = probe_wave[:, 0][:, None]
    wave_y = probe_wave[:, 1][:, None]
    wave_z = probe_wave[:, 2][:, None]
    phase_x = wave_x * x_coords[None, :] % total_x
    phase_y = wave_y * y_coords[None, :] % total_y
    phase_z = wave_z * jnp.arange(depth_z, dtype=jnp.int32)[None, :] % depth_z
    fraction = (
        phase_z[:, :, None, None].astype(jnp.float32) / depth_z
        + phase_x[:, None, :, None].astype(jnp.float32) / total_x
        + phase_y[:, None, None, :].astype(jnp.float32) / total_y
    )
    angle = 2.0 * math.pi * fraction
    ramp = jnp.sqrt(1.0 + 2.0 * x_coords.astype(jnp.float32) / total_x)[None, None, :, None]
    waves = jnp.stack([jnp.cos(angle) * ramp, jnp.sin(angle) * ramp], 1)
    polar = ((probe_ids % 3)[:, None] == jnp.arange(3, dtype=jnp.int32)[None, :]).astype(
        jnp.float32
    )
    return waves[:, :, None] * polar[:, None, :, None, None, None]


def butterfly_sum(value, axis):
    size = lax.axis_size(axis)
    if size & (size - 1):
        return lax.psum(value, axis)
    step = 1
    while step < size:
        value = value + lax.ppermute(value, axis, [(i, i ^ step) for i in range(size)])
        step *= 2
    return value


def y_roll(x, shift):
    return pltpu.roll(x, shift % x.shape[-1], x.ndim - 1)


def z_roll(x, shift):
    axis = x.ndim - 3
    n = x.shape[axis]
    s = shift % n
    if s == 0:
        return x
    return jnp.concatenate(
        [lax.slice_in_dim(x, n - s, n, axis=axis), lax.slice_in_dim(x, 0, n - s, axis=axis)], axis
    )


def field_rows(vector, bond, lo, n):
    up = vector(lo + 2, lo + n)
    down = vector(lo, lo + n - 2)
    centre = vector(lo + 1, lo + n - 1)
    total = bond(0, lo + 1, lo + n - 1) * up + bond(0, lo, lo + n - 2) * down
    bond_y = bond(1, lo + 1, lo + n - 1)
    total = total + bond_y * y_roll(centre, -1) + y_roll(bond_y, 1) * y_roll(centre, 1)
    bond_z = bond(2, lo + 1, lo + n - 1)
    total = total + bond_z * z_roll(centre, -1) + z_roll(bond_z, 1) * z_roll(centre, 1)
    return total


def local_kernel(halo, slab_rows, *refs):
    slab_refs = refs[:2 * HALO_SLABS + 1]
    start_ref, exchange_ref, relaxed_ref, last_ref, sums_ref, win, sweep_a, sweep_b, bonds_b, bonds_yr, bonds_zr, spins_b, t1, t2, t3 = refs[2 * HALO_SLABS + 1:]
    for k, slab_ref in enumerate(slab_refs):
        block = slab_ref[...]
        cos_polar, azimuth, bond_class = block[0], block[1], block[2:5]
        radial = jnp.sqrt(1.0 - cos_polar * cos_polar)
        strengths = jnp.zeros(bond_class.shape, jnp.float32)
        for class_index in range(NCLASS):
            strengths = jnp.where(bond_class == class_index, exchange_ref[class_index], strengths)
        site = jnp.stack([radial * jnp.cos(azimuth), radial * jnp.sin(azimuth), cos_polar], 0)
        win[:, :, k * slab_rows:(k + 1) * slab_rows, :] = jnp.concatenate([site, strengths], 0)
    width = len(slab_refs) * slab_rows

    def bond(d, a, b):
        return win[3 + d, :, a:b, :]

    def from_window(a, b):
        return win[0:3, :, a:b, :]

    def from_a(a, b):
        return sweep_a[:, :, a - 1:b - 1, :]

    rows_a = width - 2
    sweep_a[:, :, 0:rows_a, :] = relax_update(win[0:3, :, 1:width - 1, :], field_rows(from_window, bond, 0, width))
    rows_b = width - 4
    sweep_b[:, :, 0:rows_b, :] = relax_update(sweep_a[:, :, 1:rows_a - 1, :], field_rows(from_a, bond, 1, width - 2))
    relaxed_ref[...] = sweep_b[:, :, halo - SWEEPS:halo - SWEEPS + slab_rows, :]

    first = halo - CHEB
    n_start = slab_rows + 2 * CHEB
    lanes = win.shape[3]
    depth = win.shape[1]
    probes = start_ref.shape[4]
    for xr in range(n_start):
        w = first + xr
        site = jnp.broadcast_to(win[3:6, :, w:w + 1, :], (3, depth, probes, lanes))
        bonds_b[xr] = site
        bonds_yr[xr] = y_roll(site[1], 1)
        bonds_zr[xr] = z_roll(site[2], 1)
    for xr in range(n_start - 2):
        w = first + 1 + xr
        spins_b[xr] = jnp.broadcast_to(sweep_b[:, :, w - SWEEPS:w - SWEEPS + 1, :], (3, depth, probes, lanes))

    t_refs = (start_ref, t1, t2, t3, last_ref)
    for order in range(CHEB):
        lo = first + order
        n = n_start - 2 * order
        source = t_refs[order]
        target = t_refs[order + 1]
        acc = None
        for i in range(n - 2):
            w = lo + 1 + i
            b = w - first
            up = source[i + 2]
            down = source[i]
            centre = source[i + 1]
            total = bonds_b[b, 0] * up + bonds_b[b - 1, 0] * down
            total = total + bonds_b[b, 1] * y_roll(centre, -1) + bonds_yr[b] * y_roll(centre, 1)
            total = total + bonds_b[b, 2] * z_roll(centre, -1) + bonds_zr[b] * z_roll(centre, 1)
            advanced = cross_product(spins_b[b - 1], total) * -precess_scale
            if order > 0:
                advanced = 2.0 * advanced - t_refs[order - 1][i + 2]
            target[i] = advanced
            if halo <= w < halo + slab_rows:
                squares = advanced * advanced
                part = squares[0] + squares[1]
                part = part[0] + part[1] + part[2]
                part = part[0] + part[1] + part[2] + part[3]
                acc = part if acc is None else acc + part
        sums_ref[order:order + 1, :] = jnp.sum(acc.T, axis=0, keepdims=True)


def run_local(slab_blocks, start, exchange, halo, slab_rows):
    depth, lanes = slab_blocks[0].shape[1], slab_blocks[0].shape[3]
    width = len(slab_blocks) * slab_rows
    n_start, probes = start.shape[0], start.shape[4]
    vec_shape = start.shape[1:]

    def body(*refs):
        local_kernel(halo, slab_rows, *refs)

    sites = n_start * start[0].size
    return pl.pallas_call(
        body,
        out_shape=(
            jax.ShapeDtypeStruct((3, depth, slab_rows, lanes), jnp.float32),
            jax.ShapeDtypeStruct((slab_rows,) + vec_shape, jnp.float32),
            jax.ShapeDtypeStruct((CHEB, probes), jnp.float32),
        ),
        in_specs=[pl.BlockSpec(memory_space=pltpu.VMEM)] * (len(slab_blocks) + 1)
        + [pl.BlockSpec(memory_space=pltpu.SMEM)],
        out_specs=[pl.BlockSpec(memory_space=pltpu.VMEM)] * 3,
        scratch_shapes=[
            pltpu.VMEM((6, depth, width, lanes), jnp.float32),
            pltpu.VMEM((3, depth, width, lanes), jnp.float32),
            pltpu.VMEM((3, depth, width, lanes), jnp.float32),
            pltpu.VMEM((n_start, 3, depth, probes, lanes), jnp.float32),
            pltpu.VMEM((n_start, depth, probes, lanes), jnp.float32),
            pltpu.VMEM((n_start, depth, probes, lanes), jnp.float32),
            pltpu.VMEM((n_start, 3, depth, probes, lanes), jnp.float32),
        ]
        + [pltpu.VMEM((n_start - 2 * k,) + vec_shape, jnp.float32) for k in range(1, CHEB)],
        cost_estimate=pl.CostEstimate(
            flops=30 * sites + 200 * 3 * depth * width * lanes,
            transcendentals=0,
            bytes_accessed=4 * (6 * depth * width * lanes + start.size + start.size // 3),
        ),
    )(*slab_blocks, start, exchange)


def shards(cos_polar, azimuth, bond_class, exchange, probe_wave):
    groups = lax.axis_size("probe")
    slabs = lax.axis_size("space")
    group = lax.axis_index("probe")
    slab = lax.axis_index("space")
    slab_rows = cos_polar.shape[1]
    block_y = cos_polar.shape[2]
    total_x = slab_rows * slabs
    total_y = block_y * groups
    site_count = total_x * total_y * LZ

    local = jnp.concatenate([cos_polar[None], azimuth[None], bond_class.astype(jnp.float32)], 0)

    pieces = [shifted(local, "probe", k) for k in range(groups)]
    rotated = jnp.concatenate(pieces, -1)
    full_y = jnp.roll(rotated, group * block_y, -1) if groups > 1 else rotated

    def wraps(i, k):
        return not 0 <= i + k < slabs

    def far_block(k):
        blocks = []
        for j in range(groups):
            pairs = [
                (((g + j) % groups) * slabs + (i + k) % slabs, g * slabs + i)
                for g in range(groups)
                for i in range(slabs)
                if wraps(i, k)
            ]
            blocks.append(lax.ppermute(local, ("probe", "space"), pairs))
        joined = jnp.concatenate(blocks, -1)
        return jnp.roll(joined, group * block_y, -1) if groups > 1 else joined

    shifts = [k for k in range(-HALO_SLABS, HALO_SLABS + 1) if k != 0]
    far = {k: far_block(k) for k in shifts}
    slab_blocks = []
    for k in range(-HALO_SLABS, HALO_SLABS + 1):
        if k == 0:
            slab_blocks.append(full_y)
            continue
        near = lax.ppermute(full_y, "space", [(i + k, i) for i in range(slabs) if not wraps(i, k)])
        wrapped = (slab + k < 0) | (slab + k >= slabs)
        slab_blocks.append(jnp.where(wrapped, far[k], near))
    halo = HALO_SLABS * slab_rows

    width = slab_rows + 2 * CHEB
    x_coords = (slab * slab_rows - CHEB + jnp.arange(width, dtype=jnp.int32)) % total_x
    y_coords = jnp.arange(total_y, dtype=jnp.int32)
    group_size = probe_wave.shape[0]
    probe_ids = group * group_size + jnp.arange(group_size, dtype=jnp.int32)
    start = make_probes(probe_wave, probe_ids, x_coords, y_coords, total_x, total_y, LZ)
    start = jnp.transpose(start, (4, 1, 2, 3, 0, 5))

    relaxed, last, sums = run_local(slab_blocks, start, exchange, halo, slab_rows)
    relaxed_own = lax.dynamic_slice_in_dim(relaxed, group * block_y, block_y, -1)
    last = jnp.transpose(last, (4, 1, 2, 3, 0, 5)).astype(jnp.bfloat16)
    moment_rows = butterfly_sum(sums, "space") / site_count
    return (relaxed_own, last, moment_rows.T)


def solution(mesh):
    return jax.shard_map(
        shards,
        mesh=mesh,
        in_specs=(
            P(None, "space", "probe"),
            P(None, "space", "probe"),
            P(None, None, "space", "probe"),
            P(),
            P("probe", None),
        ),
        out_specs=(
            P(None, None, "space", "probe"),
            P("probe", None, None, None, "space", None),
            P("probe", None),
        ),
        check_vma=False,
    )
```

```python
import math

import jax
import jax.numpy as jnp
from jax import lax
from jax.experimental import pallas as pl
from jax.experimental.pallas import tpu as pltpu
from jax.sharding import PartitionSpec as P

LZ = 4
SWEEPS = 2
CHEB = 4
HALO_SLABS = 2
NCLASS = 8


relax_rate = 0.15
precess_scale = 1.0 / 6.0


def shifted(array, axis, shift):
    size = lax.axis_size(axis)
    if shift % size == 0:
        return array
    return lax.ppermute(array, axis, [(i, (i - shift) % size) for i in range(size)])


def cross_product(spin_core, vector):
    spin_a, spin_b, spin_c = (spin_core[0], spin_core[1], spin_core[2])
    vec_a = vector[..., 0, :, :, :]
    vec_b = vector[..., 1, :, :, :]
    vec_c = vector[..., 2, :, :, :]
    return jnp.stack(
        [
            spin_b * vec_c - spin_c * vec_b,
            spin_c * vec_a - spin_a * vec_c,
            spin_a * vec_b - spin_b * vec_a,
        ],
        axis=-4,
    )


def rows(array, start, stop):
    return lax.slice_in_dim(array, start, stop, axis=array.ndim - 2)


def neighbour_window(vector, bonds):
    n = vector.shape[-2]
    along_x, along_y, along_z = (bonds[0], bonds[1], bonds[2])
    total = rows(along_x, 1, n - 1) * rows(vector, 2, n) + rows(along_x, 0, n - 2) * rows(vector, 0, n - 2)
    centre = rows(vector, 1, n - 1)
    bond_y = rows(along_y, 1, n - 1)
    total = total + bond_y * jnp.roll(centre, -1, -1) + jnp.roll(bond_y, 1, -1) * jnp.roll(centre, 1, -1)
    bond_z = rows(along_z, 1, n - 1)
    total = total + bond_z * jnp.roll(centre, -1, -3) + jnp.roll(bond_z, 1, -3) * jnp.roll(centre, 1, -3)
    return total


def relax_update(spins, field):
    turned = cross_product(spins, field)
    twice = cross_product(spins, turned)
    moved = spins - relax_rate * twice
    length = jnp.sqrt(jnp.sum(moved * moved, axis=0))
    return moved / length


def make_probes(probe_wave, probe_ids, x_coords, y_coords, total_x, total_y, depth_z):
    wave_x = probe_wave[:, 0][:, None]
    wave_y = probe_wave[:, 1][:, None]
    wave_z = probe_wave[:, 2][:, None]
    phase_x = wave_x * x_coords[None, :] % total_x
    phase_y = wave_y * y_coords[None, :] % total_y
    phase_z = wave_z * jnp.arange(depth_z, dtype=jnp.int32)[None, :] % depth_z
    fraction = (
        phase_z[:, :, None, None].astype(jnp.float32) / depth_z
        + phase_x[:, None, :, None].astype(jnp.float32) / total_x
        + phase_y[:, None, None, :].astype(jnp.float32) / total_y
    )
    angle = 2.0 * math.pi * fraction
    ramp = jnp.sqrt(1.0 + 2.0 * x_coords.astype(jnp.float32) / total_x)[None, None, :, None]
    waves = jnp.stack([jnp.cos(angle) * ramp, jnp.sin(angle) * ramp], 1)
    polar = ((probe_ids % 3)[:, None] == jnp.arange(3, dtype=jnp.int32)[None, :]).astype(
        jnp.float32
    )
    return waves, polar


def butterfly_sum(value, axis):
    size = lax.axis_size(axis)
    if size & (size - 1):
        return lax.psum(value, axis)
    step = 1
    while step < size:
        value = value + lax.ppermute(value, axis, [(i, i ^ step) for i in range(size)])
        step *= 2
    return value


def y_roll(x, shift):
    return pltpu.roll(x, shift % x.shape[-1], x.ndim - 1)


def z_roll(x, shift):
    axis = x.ndim - 3
    n = x.shape[axis]
    s = shift % n
    if s == 0:
        return x
    return jnp.concatenate(
        [lax.slice_in_dim(x, n - s, n, axis=axis), lax.slice_in_dim(x, 0, n - s, axis=axis)], axis
    )


def field_rows(vector, bond, lo, n):
    up = vector(lo + 2, lo + n)
    down = vector(lo, lo + n - 2)
    centre = vector(lo + 1, lo + n - 1)
    total = bond(0, lo + 1, lo + n - 1) * up + bond(0, lo, lo + n - 2) * down
    bond_y = bond(1, lo + 1, lo + n - 1)
    total = total + bond_y * y_roll(centre, -1) + y_roll(bond_y, 1) * y_roll(centre, 1)
    bond_z = bond(2, lo + 1, lo + n - 1)
    total = total + bond_z * z_roll(centre, -1) + z_roll(bond_z, 1) * z_roll(centre, 1)
    return total


def local_kernel(halo, slab_rows, *refs):
    slab_refs = refs[:2 * HALO_SLABS + 1]
    start_ref, polar_ref, exchange_ref, relaxed_ref, last_ref, sums_ref, win, sweep_a, sweep_b, bonds_b, bonds_yr, bonds_zr, spins_b, t1, t2, t3 = refs[2 * HALO_SLABS + 1:]
    for k, slab_ref in enumerate(slab_refs):
        block = slab_ref[...]
        cos_polar, azimuth, bond_class = block[0], block[1], block[2:5]
        radial = jnp.sqrt(1.0 - cos_polar * cos_polar)
        strengths = jnp.zeros(bond_class.shape, jnp.float32)
        for class_index in range(NCLASS):
            strengths = jnp.where(bond_class == class_index, exchange_ref[class_index], strengths)
        site = jnp.stack([radial * jnp.cos(azimuth), radial * jnp.sin(azimuth), cos_polar], 0)
        win[:, :, k * slab_rows:(k + 1) * slab_rows, :] = jnp.concatenate([site, strengths], 0)
    width = len(slab_refs) * slab_rows

    def bond(d, a, b):
        return win[3 + d, :, a:b, :]

    def from_window(a, b):
        return win[0:3, :, a:b, :]

    def from_a(a, b):
        return sweep_a[:, :, a - 1:b - 1, :]

    rows_a = width - 2
    sweep_a[:, :, 0:rows_a, :] = relax_update(win[0:3, :, 1:width - 1, :], field_rows(from_window, bond, 0, width))
    rows_b = width - 4
    sweep_b[:, :, 0:rows_b, :] = relax_update(sweep_a[:, :, 1:rows_a - 1, :], field_rows(from_a, bond, 1, width - 2))
    relaxed_ref[...] = sweep_b[:, :, halo - SWEEPS:halo - SWEEPS + slab_rows, :]

    first = halo - CHEB
    n_start = slab_rows + 2 * CHEB
    lanes = win.shape[3]
    depth = win.shape[1]
    probes = start_ref.shape[3]
    for xr in range(n_start):
        w = first + xr
        site = jnp.broadcast_to(win[3:6, :, w:w + 1, :], (3, depth, probes, lanes))
        bonds_b[xr] = site
        bonds_yr[xr] = y_roll(site[1], 1)
        bonds_zr[xr] = z_roll(site[2], 1)
    for xr in range(n_start - 2):
        w = first + 1 + xr
        spins_b[xr] = jnp.broadcast_to(sweep_b[:, :, w - SWEEPS:w - SWEEPS + 1, :], (3, depth, probes, lanes))

    polar = [polar_ref[j] for j in range(3)]

    def start_row(i):
        wave = start_ref[i]
        return jnp.stack([wave * polar[j] for j in range(3)], 1)

    t_refs = (start_ref, t1, t2, t3, last_ref)
    for order in range(CHEB):
        lo = first + order
        n = n_start - 2 * order
        source = t_refs[order]
        target = t_refs[order + 1]
        acc = None
        for i in range(n - 2):
            w = lo + 1 + i
            b = w - first
            up = source[i + 2]
            down = source[i]
            centre = source[i + 1]
            total = bonds_b[b, 0] * up + bonds_b[b - 1, 0] * down
            total = total + bonds_b[b, 1] * y_roll(centre, -1) + bonds_yr[b] * y_roll(centre, 1)
            total = total + bonds_b[b, 2] * z_roll(centre, -1) + bonds_zr[b] * z_roll(centre, 1)
            if order == 0:
                total = jnp.stack([total * polar[j] for j in range(3)], 1)
                advanced = cross_product(spins_b[b - 1], total) * -precess_scale
            else:
                previous = start_row(i + 2) if order == 1 else t_refs[order - 1][i + 2]
                advanced = cross_product(spins_b[b - 1], total) * (-2.0 * precess_scale) - previous
            target[i] = advanced
            if halo <= w < halo + slab_rows:
                squares = advanced * advanced
                part = squares[0] + squares[1]
                part = part[0] + part[1] + part[2]
                part = part[0] + part[1] + part[2] + part[3]
                acc = part if acc is None else acc + part
        sums_ref[order:order + 1, :] = jnp.sum(acc.T, axis=0, keepdims=True)


def run_local(slab_blocks, start, polar, exchange, halo, slab_rows):
    depth, lanes = slab_blocks[0].shape[1], slab_blocks[0].shape[3]
    width = len(slab_blocks) * slab_rows
    n_start, probes = start.shape[0], start.shape[3]
    vec_shape = (start.shape[1], 3) + start.shape[2:]

    def body(*refs):
        local_kernel(halo, slab_rows, *refs)

    sites = n_start * 3 * start[0].size
    return pl.pallas_call(
        body,
        out_shape=(
            jax.ShapeDtypeStruct((3, depth, slab_rows, lanes), jnp.float32),
            jax.ShapeDtypeStruct((slab_rows,) + vec_shape, jnp.float32),
            jax.ShapeDtypeStruct((CHEB, probes), jnp.float32),
        ),
        in_specs=[pl.BlockSpec(memory_space=pltpu.VMEM)] * (len(slab_blocks) + 2)
        + [pl.BlockSpec(memory_space=pltpu.SMEM)],
        out_specs=[pl.BlockSpec(memory_space=pltpu.VMEM)] * 3,
        scratch_shapes=[
            pltpu.VMEM((6, depth, width, lanes), jnp.float32),
            pltpu.VMEM((3, depth, width, lanes), jnp.float32),
            pltpu.VMEM((3, depth, width, lanes), jnp.float32),
            pltpu.VMEM((n_start, 3, depth, probes, lanes), jnp.float32),
            pltpu.VMEM((n_start, depth, probes, lanes), jnp.float32),
            pltpu.VMEM((n_start, depth, probes, lanes), jnp.float32),
            pltpu.VMEM((n_start, 3, depth, probes, lanes), jnp.float32),
        ]
        + [pltpu.VMEM((n_start - 2 * k,) + vec_shape, jnp.float32) for k in range(1, CHEB)],
        cost_estimate=pl.CostEstimate(
            flops=30 * sites + 200 * 3 * depth * width * lanes,
            transcendentals=0,
            bytes_accessed=4 * (6 * depth * width * lanes + 2 * start.size),
        ),
    )(*slab_blocks, start, polar, exchange)


def shards(cos_polar, azimuth, bond_class, exchange, probe_wave):
    groups = lax.axis_size("probe")
    slabs = lax.axis_size("space")
    group = lax.axis_index("probe")
    slab = lax.axis_index("space")
    slab_rows = cos_polar.shape[1]
    block_y = cos_polar.shape[2]
    total_x = slab_rows * slabs
    total_y = block_y * groups
    site_count = total_x * total_y * LZ

    local = jnp.concatenate([cos_polar[None], azimuth[None], bond_class.astype(jnp.float32)], 0)

    pieces = [shifted(local, "probe", k) for k in range(groups)]
    rotated = jnp.concatenate(pieces, -1)
    full_y = jnp.roll(rotated, group * block_y, -1) if groups > 1 else rotated

    slab_blocks = [shifted(full_y, "space", k) for k in range(-HALO_SLABS, HALO_SLABS + 1)]
    halo = HALO_SLABS * slab_rows

    width = slab_rows + 2 * CHEB
    x_coords = (slab * slab_rows - CHEB + jnp.arange(width, dtype=jnp.int32)) % total_x
    y_coords = jnp.arange(total_y, dtype=jnp.int32)
    group_size = probe_wave.shape[0]
    probe_ids = group * group_size + jnp.arange(group_size, dtype=jnp.int32)
    waves, polar = make_probes(probe_wave, probe_ids, x_coords, y_coords, total_x, total_y, LZ)
    waves = jnp.transpose(waves, (3, 1, 2, 0, 4))
    polar = jnp.broadcast_to(polar.T[:, :, None], (3, group_size, total_y))

    relaxed, last, sums = run_local(slab_blocks, waves, polar, exchange, halo, slab_rows)
    relaxed_own = lax.dynamic_slice_in_dim(relaxed, group * block_y, block_y, -1)
    last = jnp.transpose(last, (4, 1, 2, 3, 0, 5)).astype(jnp.bfloat16)
    moment_rows = butterfly_sum(sums, "space") / site_count
    return (relaxed_own, last, moment_rows.T)


def solution(mesh):
    return jax.shard_map(
        shards,
        mesh=mesh,
        in_specs=(
            P(None, "space", "probe"),
            P(None, "space", "probe"),
            P(None, None, "space", "probe"),
            P(),
            P("probe", None),
        ),
        out_specs=(
            P(None, None, "space", "probe"),
            P("probe", None, None, None, "space", None),
            P("probe", None),
        ),
        check_vma=False,
    )
```

```python
import math

import jax
import jax.numpy as jnp
from jax import lax
from jax.experimental import pallas as pl
from jax.experimental.pallas import tpu as pltpu
from jax.sharding import PartitionSpec as P

LZ = 4
SWEEPS = 2
CHEB = 4
HALO_SLABS = 2
NCLASS = 8


relax_rate = 0.15
precess_scale = 1.0 / 6.0


def shifted(array, axis, shift):
    size = lax.axis_size(axis)
    if shift % size == 0:
        return array
    return lax.ppermute(array, axis, [(i, (i - shift) % size) for i in range(size)])


def cross_product(spin_core, vector):
    spin_a, spin_b, spin_c = (spin_core[0], spin_core[1], spin_core[2])
    vec_a = vector[..., 0, :, :, :]
    vec_b = vector[..., 1, :, :, :]
    vec_c = vector[..., 2, :, :, :]
    return jnp.stack(
        [
            spin_b * vec_c - spin_c * vec_b,
            spin_c * vec_a - spin_a * vec_c,
            spin_a * vec_b - spin_b * vec_a,
        ],
        axis=-4,
    )


def rows(array, start, stop):
    return lax.slice_in_dim(array, start, stop, axis=array.ndim - 2)


def neighbour_window(vector, bonds):
    n = vector.shape[-2]
    along_x, along_y, along_z = (bonds[0], bonds[1], bonds[2])
    total = rows(along_x, 1, n - 1) * rows(vector, 2, n) + rows(along_x, 0, n - 2) * rows(vector, 0, n - 2)
    centre = rows(vector, 1, n - 1)
    bond_y = rows(along_y, 1, n - 1)
    total = total + bond_y * jnp.roll(centre, -1, -1) + jnp.roll(bond_y, 1, -1) * jnp.roll(centre, 1, -1)
    bond_z = rows(along_z, 1, n - 1)
    total = total + bond_z * jnp.roll(centre, -1, -3) + jnp.roll(bond_z, 1, -3) * jnp.roll(centre, 1, -3)
    return total


def relax_update(spins, field):
    turned = cross_product(spins, field)
    twice = cross_product(spins, turned)
    moved = spins - relax_rate * twice
    length = jnp.sqrt(jnp.sum(moved * moved, axis=0))
    return moved / length


def make_probes(probe_wave, probe_ids, x_coords, y_coords, total_x, total_y, depth_z):
    wave_x = probe_wave[:, 0][:, None]
    wave_y = probe_wave[:, 1][:, None]
    wave_z = probe_wave[:, 2][:, None]
    phase_x = wave_x * x_coords[None, :] % total_x
    phase_y = wave_y * y_coords[None, :] % total_y
    phase_z = wave_z * jnp.arange(depth_z, dtype=jnp.int32)[None, :] % depth_z
    fraction = (
        phase_z[:, :, None, None].astype(jnp.float32) / depth_z
        + phase_x[:, None, :, None].astype(jnp.float32) / total_x
        + phase_y[:, None, None, :].astype(jnp.float32) / total_y
    )
    angle = 2.0 * math.pi * fraction
    ramp = jnp.sqrt(1.0 + 2.0 * x_coords.astype(jnp.float32) / total_x)[None, None, :, None]
    waves = jnp.stack([jnp.cos(angle) * ramp, jnp.sin(angle) * ramp], 1)
    polar = ((probe_ids % 3)[:, None] == jnp.arange(3, dtype=jnp.int32)[None, :]).astype(
        jnp.float32
    )
    return waves, polar


def butterfly_sum(value, axis):
    size = lax.axis_size(axis)
    if size & (size - 1):
        return lax.psum(value, axis)
    step = 1
    while step < size:
        value = value + lax.ppermute(value, axis, [(i, i ^ step) for i in range(size)])
        step *= 2
    return value


def y_roll(x, shift):
    return pltpu.roll(x, shift % x.shape[-1], x.ndim - 1)


def z_roll(x, shift):
    axis = x.ndim - 3
    n = x.shape[axis]
    s = shift % n
    if s == 0:
        return x
    return jnp.concatenate(
        [lax.slice_in_dim(x, n - s, n, axis=axis), lax.slice_in_dim(x, 0, n - s, axis=axis)], axis
    )


def field_rows(vector, bond, lo, n):
    up = vector(lo + 2, lo + n)
    down = vector(lo, lo + n - 2)
    centre = vector(lo + 1, lo + n - 1)
    total = bond(0, lo + 1, lo + n - 1) * up + bond(0, lo, lo + n - 2) * down
    bond_y = bond(1, lo + 1, lo + n - 1)
    total = total + bond_y * y_roll(centre, -1) + y_roll(bond_y, 1) * y_roll(centre, 1)
    bond_z = bond(2, lo + 1, lo + n - 1)
    total = total + bond_z * z_roll(centre, -1) + z_roll(bond_z, 1) * z_roll(centre, 1)
    return total


def local_kernel(halo, slab_rows, *refs):
    slab_refs = refs[:2 * HALO_SLABS + 1]
    start_ref, polar_ref, exchange_ref, relaxed_ref, last_ref, sums_ref, win, sweep_a, sweep_b, bonds_b, bonds_yr, bonds_zr, spins_b, t1, t2, t3 = refs[2 * HALO_SLABS + 1:]
    for k, slab_ref in enumerate(slab_refs):
        block = slab_ref[...]
        cos_polar, azimuth, bond_class = block[0], block[1], block[2:5]
        radial = jnp.sqrt(1.0 - cos_polar * cos_polar)
        strengths = jnp.zeros(bond_class.shape, jnp.float32)
        for class_index in range(NCLASS):
            strengths = jnp.where(bond_class == class_index, exchange_ref[class_index], strengths)
        site = jnp.stack([radial * jnp.cos(azimuth), radial * jnp.sin(azimuth), cos_polar], 0)
        win[:, :, k * slab_rows:(k + 1) * slab_rows, :] = jnp.concatenate([site, strengths], 0)
    width = len(slab_refs) * slab_rows

    def bond(d, a, b):
        return win[3 + d, :, a:b, :]

    def from_window(a, b):
        return win[0:3, :, a:b, :]

    def from_a(a, b):
        return sweep_a[:, :, a - 1:b - 1, :]

    rows_a = width - 2
    sweep_a[:, :, 0:rows_a, :] = relax_update(win[0:3, :, 1:width - 1, :], field_rows(from_window, bond, 0, width))
    rows_b = width - 4
    sweep_b[:, :, 0:rows_b, :] = relax_update(sweep_a[:, :, 1:rows_a - 1, :], field_rows(from_a, bond, 1, width - 2))
    relaxed_ref[...] = sweep_b[:, :, halo - SWEEPS:halo - SWEEPS + slab_rows, :]

    first = halo - CHEB
    n_start = slab_rows + 2 * CHEB
    lanes = win.shape[3]
    depth = win.shape[1]
    probes = start_ref.shape[3]
    for xr in range(n_start):
        w = first + xr
        site = jnp.broadcast_to(win[3:6, :, w:w + 1, :], (3, depth, probes, lanes))
        bonds_b[xr] = site
        bonds_yr[xr] = y_roll(site[1], 1)
        bonds_zr[xr] = z_roll(site[2], 1)
    for xr in range(n_start - 2):
        w = first + 1 + xr
        spins_b[xr] = jnp.broadcast_to(sweep_b[:, :, w - SWEEPS:w - SWEEPS + 1, :], (3, depth, probes, lanes))

    sublane = lax.broadcasted_iota(jnp.int32, (probes, lanes), 0)
    local_comp = jnp.zeros((probes, lanes), jnp.int32)
    for p in range(probes):
        local_comp = jnp.where(sublane == p, p % 3, local_comp)
    comp = local_comp + polar_ref[0] % 3
    comp = jnp.where(comp >= 3, comp - 3, comp)
    polar = [jnp.where(comp == j, 1.0, 0.0).astype(jnp.float32) for j in range(3)]

    def start_row(i):
        wave = start_ref[i]
        return jnp.stack([wave * polar[j] for j in range(3)], 1)

    t_refs = (start_ref, t1, t2, t3, last_ref)
    for order in range(CHEB):
        lo = first + order
        n = n_start - 2 * order
        source = t_refs[order]
        target = t_refs[order + 1]
        acc = None
        for i in range(n - 2):
            w = lo + 1 + i
            b = w - first
            up = source[i + 2]
            down = source[i]
            centre = source[i + 1]
            total = bonds_b[b, 0] * up + bonds_b[b - 1, 0] * down
            total = total + bonds_b[b, 1] * y_roll(centre, -1) + bonds_yr[b] * y_roll(centre, 1)
            total = total + bonds_b[b, 2] * z_roll(centre, -1) + bonds_zr[b] * z_roll(centre, 1)
            if order == 0:
                total = jnp.stack([total * polar[j] for j in range(3)], 1)
                advanced = cross_product(spins_b[b - 1], total) * -precess_scale
            else:
                previous = start_row(i + 2) if order == 1 else t_refs[order - 1][i + 2]
                advanced = cross_product(spins_b[b - 1], total) * (-2.0 * precess_scale) - previous
            target[i] = advanced
            if halo <= w < halo + slab_rows:
                squares = advanced * advanced
                part = squares[0] + squares[1]
                part = part[0] + part[1] + part[2]
                part = part[0] + part[1] + part[2] + part[3]
                acc = part if acc is None else acc + part
        sums_ref[order:order + 1, :] = jnp.sum(acc.T, axis=0, keepdims=True)


def run_local(slab_blocks, start, polar, exchange, halo, slab_rows):
    depth, lanes = slab_blocks[0].shape[1], slab_blocks[0].shape[3]
    width = len(slab_blocks) * slab_rows
    n_start, probes = start.shape[0], start.shape[3]
    vec_shape = (start.shape[1], 3) + start.shape[2:]

    def body(*refs):
        local_kernel(halo, slab_rows, *refs)

    sites = n_start * 3 * start[0].size
    return pl.pallas_call(
        body,
        out_shape=(
            jax.ShapeDtypeStruct((3, depth, slab_rows, lanes), jnp.float32),
            jax.ShapeDtypeStruct((slab_rows,) + vec_shape, jnp.float32),
            jax.ShapeDtypeStruct((CHEB, probes), jnp.float32),
        ),
        in_specs=[pl.BlockSpec(memory_space=pltpu.VMEM)] * (len(slab_blocks) + 1)
        + [pl.BlockSpec(memory_space=pltpu.SMEM)] * 2,
        out_specs=[pl.BlockSpec(memory_space=pltpu.VMEM)] * 3,
        scratch_shapes=[
            pltpu.VMEM((6, depth, width, lanes), jnp.float32),
            pltpu.VMEM((3, depth, width, lanes), jnp.float32),
            pltpu.VMEM((3, depth, width, lanes), jnp.float32),
            pltpu.VMEM((n_start, 3, depth, probes, lanes), jnp.float32),
            pltpu.VMEM((n_start, depth, probes, lanes), jnp.float32),
            pltpu.VMEM((n_start, depth, probes, lanes), jnp.float32),
            pltpu.VMEM((n_start, 3, depth, probes, lanes), jnp.float32),
        ]
        + [pltpu.VMEM((n_start - 2 * k,) + vec_shape, jnp.float32) for k in range(1, CHEB)],
        cost_estimate=pl.CostEstimate(
            flops=30 * sites + 200 * 3 * depth * width * lanes,
            transcendentals=0,
            bytes_accessed=4 * (6 * depth * width * lanes + 2 * start.size),
        ),
    )(*slab_blocks, start, polar, exchange)


def shards(cos_polar, azimuth, bond_class, exchange, probe_wave):
    groups = lax.axis_size("probe")
    slabs = lax.axis_size("space")
    group = lax.axis_index("probe")
    slab = lax.axis_index("space")
    slab_rows = cos_polar.shape[1]
    block_y = cos_polar.shape[2]
    total_x = slab_rows * slabs
    total_y = block_y * groups
    site_count = total_x * total_y * LZ

    local = jnp.concatenate([cos_polar[None], azimuth[None], bond_class.astype(jnp.float32)], 0)

    pieces = [shifted(local, "probe", k) for k in range(groups)]
    rotated = jnp.concatenate(pieces, -1)
    full_y = jnp.roll(rotated, group * block_y, -1) if groups > 1 else rotated

    slab_blocks = [shifted(full_y, "space", k) for k in range(-HALO_SLABS, HALO_SLABS + 1)]
    halo = HALO_SLABS * slab_rows

    width = slab_rows + 2 * CHEB
    x_coords = (slab * slab_rows - CHEB + jnp.arange(width, dtype=jnp.int32)) % total_x
    y_coords = jnp.arange(total_y, dtype=jnp.int32)
    group_size = probe_wave.shape[0]
    probe_ids = group * group_size + jnp.arange(group_size, dtype=jnp.int32)
    waves, polar = make_probes(probe_wave, probe_ids, x_coords, y_coords, total_x, total_y, LZ)
    waves = jnp.transpose(waves, (3, 1, 2, 0, 4))
    first_id = (group * group_size).astype(jnp.int32).reshape(1)

    relaxed, last, sums = run_local(slab_blocks, waves, first_id, exchange, halo, slab_rows)
    relaxed_own = lax.dynamic_slice_in_dim(relaxed, group * block_y, block_y, -1)
    last = jnp.transpose(last, (4, 1, 2, 3, 0, 5)).astype(jnp.bfloat16)
    moment_rows = butterfly_sum(sums, "space") / site_count
    return (relaxed_own, last, moment_rows.T)


def solution(mesh):
    return jax.shard_map(
        shards,
        mesh=mesh,
        in_specs=(
            P(None, "space", "probe"),
            P(None, "space", "probe"),
            P(None, None, "space", "probe"),
            P(),
            P("probe", None),
        ),
        out_specs=(
            P(None, None, "space", "probe"),
            P("probe", None, None, None, "space", None),
            P("probe", None),
        ),
        check_vma=False,
    )
```

```python
import math

import jax
import jax.numpy as jnp
from jax import lax
from jax.experimental import pallas as pl
from jax.experimental.pallas import tpu as pltpu
from jax.sharding import PartitionSpec as P

LZ = 4
SWEEPS = 2
CHEB = 4
HALO_SLABS = 2
NCLASS = 8


relax_rate = 0.15
precess_scale = 1.0 / 6.0


def shifted(array, axis, shift):
    size = lax.axis_size(axis)
    if shift % size == 0:
        return array
    return lax.ppermute(array, axis, [(i, (i - shift) % size) for i in range(size)])


def cross_product(spin_core, vector):
    spin_a, spin_b, spin_c = (spin_core[0], spin_core[1], spin_core[2])
    vec_a = vector[..., 0, :, :, :]
    vec_b = vector[..., 1, :, :, :]
    vec_c = vector[..., 2, :, :, :]
    return jnp.stack(
        [
            spin_b * vec_c - spin_c * vec_b,
            spin_c * vec_a - spin_a * vec_c,
            spin_a * vec_b - spin_b * vec_a,
        ],
        axis=-4,
    )


def rows(array, start, stop):
    return lax.slice_in_dim(array, start, stop, axis=array.ndim - 2)


def neighbour_window(vector, bonds):
    n = vector.shape[-2]
    along_x, along_y, along_z = (bonds[0], bonds[1], bonds[2])
    total = rows(along_x, 1, n - 1) * rows(vector, 2, n) + rows(along_x, 0, n - 2) * rows(vector, 0, n - 2)
    centre = rows(vector, 1, n - 1)
    bond_y = rows(along_y, 1, n - 1)
    total = total + bond_y * jnp.roll(centre, -1, -1) + jnp.roll(bond_y, 1, -1) * jnp.roll(centre, 1, -1)
    bond_z = rows(along_z, 1, n - 1)
    total = total + bond_z * jnp.roll(centre, -1, -3) + jnp.roll(bond_z, 1, -3) * jnp.roll(centre, 1, -3)
    return total


def relax_update(spins, field):
    turned = cross_product(spins, field)
    twice = cross_product(spins, turned)
    moved = spins - relax_rate * twice
    length = jnp.sqrt(jnp.sum(moved * moved, axis=0))
    return moved / length


def make_probes(probe_wave, probe_ids, x_coords, y_coords, total_x, total_y, depth_z):
    wave_x = probe_wave[:, 0][:, None]
    wave_y = probe_wave[:, 1][:, None]
    wave_z = probe_wave[:, 2][:, None]
    phase_x = wave_x * x_coords[None, :] % total_x
    phase_y = wave_y * y_coords[None, :] % total_y
    phase_z = wave_z * jnp.arange(depth_z, dtype=jnp.int32)[None, :] % depth_z
    fraction = (
        phase_z[:, :, None, None].astype(jnp.float32) / depth_z
        + phase_x[:, None, :, None].astype(jnp.float32) / total_x
        + phase_y[:, None, None, :].astype(jnp.float32) / total_y
    )
    angle = 2.0 * math.pi * fraction
    ramp = jnp.sqrt(1.0 + 2.0 * x_coords.astype(jnp.float32) / total_x)[None, None, :, None]
    waves = jnp.stack([jnp.cos(angle) * ramp, jnp.sin(angle) * ramp], 1)
    polar = ((probe_ids % 3)[:, None] == jnp.arange(3, dtype=jnp.int32)[None, :]).astype(
        jnp.float32
    )
    return waves, polar


def butterfly_sum(value, axis):
    size = lax.axis_size(axis)
    if size & (size - 1):
        return lax.psum(value, axis)
    step = 1
    while step < size:
        value = value + lax.ppermute(value, axis, [(i, i ^ step) for i in range(size)])
        step *= 2
    return value


def y_roll(x, shift):
    return pltpu.roll(x, shift % x.shape[-1], x.ndim - 1)


def z_roll(x, shift):
    axis = x.ndim - 3
    n = x.shape[axis]
    s = shift % n
    if s == 0:
        return x
    return jnp.concatenate(
        [lax.slice_in_dim(x, n - s, n, axis=axis), lax.slice_in_dim(x, 0, n - s, axis=axis)], axis
    )


def field_rows(vector, bond, lo, n):
    up = vector(lo + 2, lo + n)
    down = vector(lo, lo + n - 2)
    centre = vector(lo + 1, lo + n - 1)
    total = bond(0, lo + 1, lo + n - 1) * up + bond(0, lo, lo + n - 2) * down
    bond_y = bond(1, lo + 1, lo + n - 1)
    total = total + bond_y * y_roll(centre, -1) + y_roll(bond_y, 1) * y_roll(centre, 1)
    bond_z = bond(2, lo + 1, lo + n - 1)
    total = total + bond_z * z_roll(centre, -1) + z_roll(bond_z, 1) * z_roll(centre, 1)
    return total


def local_kernel(halo, slab_rows, *refs):
    slab_refs = refs[:2 * HALO_SLABS + 1]
    start_ref, polar_ref, exchange_ref, relaxed_ref, last_ref, sums_ref, win, sweep_a, sweep_b, bonds_b, bonds_yr, bonds_zr, spins_b, t1, t2, t3 = refs[2 * HALO_SLABS + 1:]
    for k, slab_ref in enumerate(slab_refs):
        block = slab_ref[...]
        cos_polar, azimuth, bond_class = block[0], block[1], block[2:5]
        radial = jnp.sqrt(1.0 - cos_polar * cos_polar)
        strengths = jnp.zeros(bond_class.shape, jnp.float32)
        for class_index in range(NCLASS):
            strengths = jnp.where(bond_class == class_index, exchange_ref[class_index], strengths)
        site = jnp.stack([radial * jnp.cos(azimuth), radial * jnp.sin(azimuth), cos_polar], 0)
        win[:, :, k * slab_rows:(k + 1) * slab_rows, :] = jnp.concatenate([site, strengths], 0)
    width = len(slab_refs) * slab_rows

    def bond(d, a, b):
        return win[3 + d, :, a:b, :]

    def from_window(a, b):
        return win[0:3, :, a:b, :]

    def from_a(a, b):
        return sweep_a[:, :, a - 1:b - 1, :]

    rows_a = width - 2
    sweep_a[:, :, 0:rows_a, :] = relax_update(win[0:3, :, 1:width - 1, :], field_rows(from_window, bond, 0, width))
    rows_b = width - 4
    sweep_b[:, :, 0:rows_b, :] = relax_update(sweep_a[:, :, 1:rows_a - 1, :], field_rows(from_a, bond, 1, width - 2))
    relaxed_ref[...] = sweep_b[:, :, halo - SWEEPS:halo - SWEEPS + slab_rows, :]

    first = halo - CHEB
    n_start = slab_rows + 2 * CHEB
    lanes = win.shape[3]
    depth = win.shape[1]
    probes = start_ref.shape[3]
    for xr in range(n_start):
        w = first + xr
        site = jnp.broadcast_to(win[3:6, :, w:w + 1, :], (3, depth, probes, lanes))
        bonds_b[xr] = site
        bonds_yr[xr] = y_roll(site[1], 1)
        bonds_zr[xr] = z_roll(site[2], 1)
    for xr in range(n_start - 2):
        w = first + 1 + xr
        spins_b[xr] = jnp.broadcast_to(sweep_b[:, :, w - SWEEPS:w - SWEEPS + 1, :], (3, depth, probes, lanes))

    sublane = lax.broadcasted_iota(jnp.int32, (probes, lanes), 0)
    local_comp = jnp.zeros((probes, lanes), jnp.int32)
    for p in range(probes):
        local_comp = jnp.where(sublane == p, p % 3, local_comp)
    comp = local_comp + polar_ref[0] % 3
    comp = jnp.where(comp >= 3, comp - 3, comp)
    polar = [jnp.where(comp == j, 1.0, 0.0).astype(jnp.float32) for j in range(3)]

    def start_row(i):
        wave = start_ref[i]
        return jnp.stack([wave * polar[j] for j in range(3)], 1)

    t_refs = (start_ref, t1, t2, t3, last_ref)
    for order in range(CHEB):
        lo = first + order
        n = n_start - 2 * order
        source = t_refs[order]
        target = t_refs[order + 1]
        acc = None
        for i in range(n - 2):
            w = lo + 1 + i
            b = w - first
            up = source[i + 2]
            down = source[i]
            centre = source[i + 1]
            total = bonds_b[b, 0] * up + bonds_b[b - 1, 0] * down
            total = total + bonds_b[b, 1] * y_roll(centre, -1) + bonds_yr[b] * y_roll(centre, 1)
            total = total + bonds_b[b, 2] * z_roll(centre, -1) + bonds_zr[b] * z_roll(centre, 1)
            if order == 0:
                total = jnp.stack([total * polar[j] for j in range(3)], 1)
                advanced = cross_product(spins_b[b - 1], total) * -precess_scale
            else:
                previous = start_row(i + 2) if order == 1 else t_refs[order - 1][i + 2]
                advanced = cross_product(spins_b[b - 1], total) * (-2.0 * precess_scale) - previous
            target[i] = advanced
            if halo <= w < halo + slab_rows:
                squares = advanced * advanced
                part = squares[0] + squares[1]
                part = part[0] + part[1] + part[2]
                part = part[0] + part[1] + part[2] + part[3]
                acc = part if acc is None else acc + part
        sums_ref[order:order + 1, :] = jnp.sum(acc.T, axis=0, keepdims=True)


def run_local(slab_blocks, start, polar, exchange, halo, slab_rows):
    depth, lanes = slab_blocks[0].shape[1], slab_blocks[0].shape[3]
    width = len(slab_blocks) * slab_rows
    n_start, probes = start.shape[0], start.shape[3]
    vec_shape = (start.shape[1], 3) + start.shape[2:]

    def body(*refs):
        local_kernel(halo, slab_rows, *refs)

    sites = n_start * 3 * start[0].size
    return pl.pallas_call(
        body,
        out_shape=(
            jax.ShapeDtypeStruct((3, depth, slab_rows, lanes), jnp.float32),
            jax.ShapeDtypeStruct((slab_rows,) + vec_shape, jnp.float32),
            jax.ShapeDtypeStruct((CHEB, probes), jnp.float32),
        ),
        in_specs=[pl.BlockSpec(memory_space=pltpu.VMEM)] * (len(slab_blocks) + 1)
        + [pl.BlockSpec(memory_space=pltpu.SMEM)] * 2,
        out_specs=[pl.BlockSpec(memory_space=pltpu.VMEM)] * 3,
        scratch_shapes=[
            pltpu.VMEM((6, depth, width, lanes), jnp.float32),
            pltpu.VMEM((3, depth, width, lanes), jnp.float32),
            pltpu.VMEM((3, depth, width, lanes), jnp.float32),
            pltpu.VMEM((n_start, 3, depth, probes, lanes), jnp.float32),
            pltpu.VMEM((n_start, depth, probes, lanes), jnp.float32),
            pltpu.VMEM((n_start, depth, probes, lanes), jnp.float32),
            pltpu.VMEM((n_start, 3, depth, probes, lanes), jnp.float32),
        ]
        + [pltpu.VMEM((n_start - 2 * k,) + vec_shape, jnp.float32) for k in range(1, CHEB)],
        cost_estimate=pl.CostEstimate(
            flops=30 * sites + 200 * 3 * depth * width * lanes,
            transcendentals=0,
            bytes_accessed=4 * (6 * depth * width * lanes + 2 * start.size),
        ),
    )(*slab_blocks, start, polar, exchange)


def shards(cos_polar, azimuth, bond_class, exchange, probe_wave):
    groups = lax.axis_size("probe")
    slabs = lax.axis_size("space")
    group = lax.axis_index("probe")
    slab = lax.axis_index("space")
    slab_rows = cos_polar.shape[1]
    block_y = cos_polar.shape[2]
    total_x = slab_rows * slabs
    total_y = block_y * groups
    site_count = total_x * total_y * LZ

    local = jnp.concatenate([cos_polar[None], azimuth[None], bond_class.astype(jnp.float32)], 0)

    dense = (slab_rows * block_y) % 128 == 0 and block_y < 128
    packed = local.reshape(local.shape[:2] + (slab_rows * block_y // 128, 128)) if dense else local
    pieces = [shifted(packed, "probe", k).reshape(local.shape) for k in range(groups)]
    rotated = jnp.concatenate(pieces, -1)
    full_y = jnp.roll(rotated, group * block_y, -1) if groups > 1 else rotated

    slab_blocks = [shifted(full_y, "space", k) for k in range(-HALO_SLABS, HALO_SLABS + 1)]
    halo = HALO_SLABS * slab_rows

    width = slab_rows + 2 * CHEB
    x_coords = (slab * slab_rows - CHEB + jnp.arange(width, dtype=jnp.int32)) % total_x
    y_coords = jnp.arange(total_y, dtype=jnp.int32)
    group_size = probe_wave.shape[0]
    probe_ids = group * group_size + jnp.arange(group_size, dtype=jnp.int32)
    waves, polar = make_probes(probe_wave, probe_ids, x_coords, y_coords, total_x, total_y, LZ)
    waves = jnp.transpose(waves, (3, 1, 2, 0, 4))
    first_id = (group * group_size).astype(jnp.int32).reshape(1)

    relaxed, last, sums = run_local(slab_blocks, waves, first_id, exchange, halo, slab_rows)
    relaxed_own = lax.dynamic_slice_in_dim(relaxed, group * block_y, block_y, -1)
    last = jnp.transpose(last, (4, 1, 2, 3, 0, 5)).astype(jnp.bfloat16)
    moment_rows = butterfly_sum(sums, "space") / site_count
    return (relaxed_own, last, moment_rows.T)


def solution(mesh):
    return jax.shard_map(
        shards,
        mesh=mesh,
        in_specs=(
            P(None, "space", "probe"),
            P(None, "space", "probe"),
            P(None, None, "space", "probe"),
            P(),
            P("probe", None),
        ),
        out_specs=(
            P(None, None, "space", "probe"),
            P("probe", None, None, None, "space", None),
            P("probe", None),
        ),
        check_vma=False,
    )
```

```python
import math

import jax
import jax.numpy as jnp
from jax import lax
from jax.experimental import pallas as pl
from jax.experimental.pallas import tpu as pltpu
from jax.sharding import PartitionSpec as P

LZ = 4
SWEEPS = 2
CHEB = 4
HALO_SLABS = 2
NCLASS = 8


relax_rate = 0.15
precess_scale = 1.0 / 6.0


def shifted(array, axis, shift):
    size = lax.axis_size(axis)
    if shift % size == 0:
        return array
    return lax.ppermute(array, axis, [(i, (i - shift) % size) for i in range(size)])


def cross_product(spin_core, vector):
    spin_a, spin_b, spin_c = (spin_core[0], spin_core[1], spin_core[2])
    vec_a = vector[..., 0, :, :, :]
    vec_b = vector[..., 1, :, :, :]
    vec_c = vector[..., 2, :, :, :]
    return jnp.stack(
        [
            spin_b * vec_c - spin_c * vec_b,
            spin_c * vec_a - spin_a * vec_c,
            spin_a * vec_b - spin_b * vec_a,
        ],
        axis=-4,
    )


def rows(array, start, stop):
    return lax.slice_in_dim(array, start, stop, axis=array.ndim - 2)


def neighbour_window(vector, bonds):
    n = vector.shape[-2]
    along_x, along_y, along_z = (bonds[0], bonds[1], bonds[2])
    total = rows(along_x, 1, n - 1) * rows(vector, 2, n) + rows(along_x, 0, n - 2) * rows(vector, 0, n - 2)
    centre = rows(vector, 1, n - 1)
    bond_y = rows(along_y, 1, n - 1)
    total = total + bond_y * jnp.roll(centre, -1, -1) + jnp.roll(bond_y, 1, -1) * jnp.roll(centre, 1, -1)
    bond_z = rows(along_z, 1, n - 1)
    total = total + bond_z * jnp.roll(centre, -1, -3) + jnp.roll(bond_z, 1, -3) * jnp.roll(centre, 1, -3)
    return total


def relax_update(spins, field):
    turned = cross_product(spins, field)
    twice = cross_product(spins, turned)
    moved = spins - relax_rate * twice
    length = jnp.sqrt(jnp.sum(moved * moved, axis=0))
    return moved / length


def make_probes(probe_wave, probe_ids, x_coords, y_coords, total_x, total_y, depth_z):
    wave_x = probe_wave[:, 0][:, None]
    wave_y = probe_wave[:, 1][:, None]
    wave_z = probe_wave[:, 2][:, None]
    phase_x = wave_x * x_coords[None, :] % total_x
    phase_y = wave_y * y_coords[None, :] % total_y
    phase_z = wave_z * jnp.arange(depth_z, dtype=jnp.int32)[None, :] % depth_z
    fraction = (
        phase_z[:, :, None, None].astype(jnp.float32) / depth_z
        + phase_x[:, None, :, None].astype(jnp.float32) / total_x
        + phase_y[:, None, None, :].astype(jnp.float32) / total_y
    )
    angle = 2.0 * math.pi * fraction
    ramp = jnp.sqrt(1.0 + 2.0 * x_coords.astype(jnp.float32) / total_x)[None, None, :, None]
    waves = jnp.stack([jnp.cos(angle) * ramp, jnp.sin(angle) * ramp], 1)
    polar = ((probe_ids % 3)[:, None] == jnp.arange(3, dtype=jnp.int32)[None, :]).astype(
        jnp.float32
    )
    return waves, polar


def butterfly_sum(value, axis):
    size = lax.axis_size(axis)
    if size & (size - 1):
        return lax.psum(value, axis)
    step = 1
    while step < size:
        value = value + lax.ppermute(value, axis, [(i, i ^ step) for i in range(size)])
        step *= 2
    return value


def y_roll(x, shift):
    return pltpu.roll(x, shift % x.shape[-1], x.ndim - 1)


def z_roll(x, shift):
    axis = x.ndim - 3
    n = x.shape[axis]
    s = shift % n
    if s == 0:
        return x
    return jnp.concatenate(
        [lax.slice_in_dim(x, n - s, n, axis=axis), lax.slice_in_dim(x, 0, n - s, axis=axis)], axis
    )


def field_rows(vector, bond, lo, n):
    up = vector(lo + 2, lo + n)
    down = vector(lo, lo + n - 2)
    centre = vector(lo + 1, lo + n - 1)
    total = bond(0, lo + 1, lo + n - 1) * up + bond(0, lo, lo + n - 2) * down
    bond_y = bond(1, lo + 1, lo + n - 1)
    total = total + bond_y * y_roll(centre, -1) + y_roll(bond_y, 1) * y_roll(centre, 1)
    bond_z = bond(2, lo + 1, lo + n - 1)
    total = total + bond_z * z_roll(centre, -1) + z_roll(bond_z, 1) * z_roll(centre, 1)
    return total


def local_kernel(halo, slab_rows, *refs):
    slab_refs = refs[:2 * HALO_SLABS + 1]
    start_ref, polar_ref, exchange_ref, relaxed_ref, last_ref, sums_ref, win, sweep_a, sweep_b, bonds_b, bonds_yr, bonds_zr, spins_b, t1, t2, t3 = refs[2 * HALO_SLABS + 1:]
    for k, slab_ref in enumerate(slab_refs):
        block = slab_ref[...]
        cos_polar, azimuth, bond_class = block[0], block[1], block[2:5]
        radial = jnp.sqrt(1.0 - cos_polar * cos_polar)
        strengths = jnp.zeros(bond_class.shape, jnp.float32)
        for class_index in range(NCLASS):
            strengths = jnp.where(bond_class == class_index, exchange_ref[class_index], strengths)
        site = jnp.stack([radial * jnp.cos(azimuth), radial * jnp.sin(azimuth), cos_polar], 0)
        win[:, :, k * slab_rows:(k + 1) * slab_rows, :] = jnp.concatenate([site, strengths], 0)
    width = len(slab_refs) * slab_rows

    def bond(d, a, b):
        return win[3 + d, :, a:b, :]

    def from_window(a, b):
        return win[0:3, :, a:b, :]

    first = halo - CHEB
    n_start = slab_rows + 2 * CHEB
    base_a = first

    def from_a(a, b):
        return sweep_a[:, :, a - base_a:b - base_a, :]

    sweep_a[:, :, 0:n_start, :] = relax_update(
        win[0:3, :, first:first + n_start, :], field_rows(from_window, bond, first - 1, n_start + 2)
    )
    sweep_b[:, :, 0:n_start - 2, :] = relax_update(
        sweep_a[:, :, 1:n_start - 1, :], field_rows(from_a, bond, first, n_start)
    )
    base_b = first + 1
    relaxed_ref[...] = sweep_b[:, :, halo - base_b:halo - base_b + slab_rows, :]
    lanes = win.shape[3]
    depth = win.shape[1]
    probes = start_ref.shape[3]
    for xr in range(n_start):
        w = first + xr
        site = jnp.broadcast_to(win[3:6, :, w:w + 1, :], (3, depth, probes, lanes))
        bonds_b[xr] = site
        bonds_yr[xr] = y_roll(site[1], 1)
        bonds_zr[xr] = z_roll(site[2], 1)
    for xr in range(n_start - 2):
        w = first + 1 + xr
        spins_b[xr] = jnp.broadcast_to(sweep_b[:, :, w - base_b:w - base_b + 1, :], (3, depth, probes, lanes))

    polar = [polar_ref[j] for j in range(3)]

    def start_row(i):
        wave = start_ref[i]
        return jnp.stack([wave * polar[j] for j in range(3)], 1)

    t_refs = (start_ref, t1, t2, t3, last_ref)
    for order in range(CHEB):
        lo = first + order
        n = n_start - 2 * order
        source = t_refs[order]
        target = t_refs[order + 1]
        acc = None
        for i in range(n - 2):
            w = lo + 1 + i
            b = w - first
            up = source[i + 2]
            down = source[i]
            centre = source[i + 1]
            total = bonds_b[b, 0] * up + bonds_b[b - 1, 0] * down
            total = total + bonds_b[b, 1] * y_roll(centre, -1) + bonds_yr[b] * y_roll(centre, 1)
            total = total + bonds_b[b, 2] * z_roll(centre, -1) + bonds_zr[b] * z_roll(centre, 1)
            if order == 0:
                total = jnp.stack([total * polar[j] for j in range(3)], 1)
                advanced = cross_product(spins_b[b - 1], total) * -precess_scale
            else:
                previous = start_row(i + 2) if order == 1 else t_refs[order - 1][i + 2]
                advanced = cross_product(spins_b[b - 1], total) * (-2.0 * precess_scale) - previous
            target[i] = advanced
            if halo <= w < halo + slab_rows:
                squares = advanced * advanced
                part = squares[0] + squares[1]
                part = part[0] + part[1] + part[2]
                part = part[0] + part[1] + part[2] + part[3]
                acc = part if acc is None else acc + part
        sums_ref[order:order + 1, :] = jnp.sum(acc.T, axis=0, keepdims=True)


def run_local(slab_blocks, start, polar, exchange, halo, slab_rows):
    depth, lanes = slab_blocks[0].shape[1], slab_blocks[0].shape[3]
    width = len(slab_blocks) * slab_rows
    n_start, probes = start.shape[0], start.shape[3]
    vec_shape = (start.shape[1], 3) + start.shape[2:]

    def body(*refs):
        local_kernel(halo, slab_rows, *refs)

    sites = n_start * 3 * start[0].size
    return pl.pallas_call(
        body,
        out_shape=(
            jax.ShapeDtypeStruct((3, depth, slab_rows, lanes), jnp.float32),
            jax.ShapeDtypeStruct((slab_rows,) + vec_shape, jnp.float32),
            jax.ShapeDtypeStruct((CHEB, probes), jnp.float32),
        ),
        in_specs=[pl.BlockSpec(memory_space=pltpu.VMEM)] * (len(slab_blocks) + 2)
        + [pl.BlockSpec(memory_space=pltpu.SMEM)],
        out_specs=[pl.BlockSpec(memory_space=pltpu.VMEM)] * 3,
        scratch_shapes=[
            pltpu.VMEM((6, depth, width, lanes), jnp.float32),
            pltpu.VMEM((3, depth, width, lanes), jnp.float32),
            pltpu.VMEM((3, depth, width, lanes), jnp.float32),
            pltpu.VMEM((n_start, 3, depth, probes, lanes), jnp.float32),
            pltpu.VMEM((n_start, depth, probes, lanes), jnp.float32),
            pltpu.VMEM((n_start, depth, probes, lanes), jnp.float32),
            pltpu.VMEM((n_start, 3, depth, probes, lanes), jnp.float32),
        ]
        + [pltpu.VMEM((n_start - 2 * k,) + vec_shape, jnp.float32) for k in range(1, CHEB)],
        cost_estimate=pl.CostEstimate(
            flops=30 * sites + 200 * 3 * depth * width * lanes,
            transcendentals=0,
            bytes_accessed=4 * (6 * depth * width * lanes + 2 * start.size),
        ),
    )(*slab_blocks, start, polar, exchange)


def shards(cos_polar, azimuth, bond_class, exchange, probe_wave):
    groups = lax.axis_size("probe")
    slabs = lax.axis_size("space")
    group = lax.axis_index("probe")
    slab = lax.axis_index("space")
    slab_rows = cos_polar.shape[1]
    block_y = cos_polar.shape[2]
    total_x = slab_rows * slabs
    total_y = block_y * groups
    site_count = total_x * total_y * LZ

    local = jnp.concatenate([cos_polar[None], azimuth[None], bond_class.astype(jnp.float32)], 0)

    pieces = [shifted(local, "probe", k) for k in range(groups)]
    rotated = jnp.concatenate(pieces, -1)
    full_y = jnp.roll(rotated, group * block_y, -1) if groups > 1 else rotated

    slab_blocks = [shifted(full_y, "space", k) for k in range(-HALO_SLABS, HALO_SLABS + 1)]
    halo = HALO_SLABS * slab_rows

    width = slab_rows + 2 * CHEB
    x_coords = (slab * slab_rows - CHEB + jnp.arange(width, dtype=jnp.int32)) % total_x
    y_coords = jnp.arange(total_y, dtype=jnp.int32)
    group_size = probe_wave.shape[0]
    probe_ids = group * group_size + jnp.arange(group_size, dtype=jnp.int32)
    waves, polar = make_probes(probe_wave, probe_ids, x_coords, y_coords, total_x, total_y, LZ)
    waves = jnp.transpose(waves, (3, 1, 2, 0, 4))
    polar = jnp.broadcast_to(polar.T[:, :, None], (3, group_size, total_y))

    relaxed, last, sums = run_local(slab_blocks, waves, polar, exchange, halo, slab_rows)
    relaxed_own = lax.dynamic_slice_in_dim(relaxed, group * block_y, block_y, -1)
    last = jnp.transpose(last, (4, 1, 2, 3, 0, 5)).astype(jnp.bfloat16)
    moment_rows = butterfly_sum(sums, "space") / site_count
    return (relaxed_own, last, moment_rows.T)


def solution(mesh):
    return jax.shard_map(
        shards,
        mesh=mesh,
        in_specs=(
            P(None, "space", "probe"),
            P(None, "space", "probe"),
            P(None, None, "space", "probe"),
            P(),
            P("probe", None),
        ),
        out_specs=(
            P(None, None, "space", "probe"),
            P("probe", None, None, None, "space", None),
            P("probe", None),
        ),
        check_vma=False,
    )
```

```python
import math

import jax
import jax.numpy as jnp
from jax import lax
from jax.experimental import pallas as pl
from jax.experimental.pallas import tpu as pltpu
from jax.sharding import PartitionSpec as P

LZ = 4
SWEEPS = 2
CHEB = 4
HALO_SLABS = 2
NCLASS = 8


relax_rate = 0.15
precess_scale = 1.0 / 6.0


def shifted(array, axis, shift):
    size = lax.axis_size(axis)
    if shift % size == 0:
        return array
    return lax.ppermute(array, axis, [(i, (i - shift) % size) for i in range(size)])


def cross_product(spin_core, vector):
    spin_a, spin_b, spin_c = (spin_core[0], spin_core[1], spin_core[2])
    vec_a = vector[..., 0, :, :, :]
    vec_b = vector[..., 1, :, :, :]
    vec_c = vector[..., 2, :, :, :]
    return jnp.stack(
        [
            spin_b * vec_c - spin_c * vec_b,
            spin_c * vec_a - spin_a * vec_c,
            spin_a * vec_b - spin_b * vec_a,
        ],
        axis=-4,
    )


def rows(array, start, stop):
    return lax.slice_in_dim(array, start, stop, axis=array.ndim - 2)


def neighbour_window(vector, bonds):
    n = vector.shape[-2]
    along_x, along_y, along_z = (bonds[0], bonds[1], bonds[2])
    total = rows(along_x, 1, n - 1) * rows(vector, 2, n) + rows(along_x, 0, n - 2) * rows(vector, 0, n - 2)
    centre = rows(vector, 1, n - 1)
    bond_y = rows(along_y, 1, n - 1)
    total = total + bond_y * jnp.roll(centre, -1, -1) + jnp.roll(bond_y, 1, -1) * jnp.roll(centre, 1, -1)
    bond_z = rows(along_z, 1, n - 1)
    total = total + bond_z * jnp.roll(centre, -1, -3) + jnp.roll(bond_z, 1, -3) * jnp.roll(centre, 1, -3)
    return total


def relax_update(spins, field):
    turned = cross_product(spins, field)
    twice = cross_product(spins, turned)
    moved = spins - relax_rate * twice
    length = jnp.sqrt(jnp.sum(moved * moved, axis=0))
    return moved / length


def make_probes(probe_wave, probe_ids, x_coords, y_coords, total_x, total_y, depth_z):
    wave_x = probe_wave[:, 0][:, None]
    wave_y = probe_wave[:, 1][:, None]
    wave_z = probe_wave[:, 2][:, None]
    phase_x = wave_x * x_coords[None, :] % total_x
    phase_y = wave_y * y_coords[None, :] % total_y
    phase_z = wave_z * jnp.arange(depth_z, dtype=jnp.int32)[None, :] % depth_z
    fraction = (
        phase_z[:, :, None, None].astype(jnp.float32) / depth_z
        + phase_x[:, None, :, None].astype(jnp.float32) / total_x
        + phase_y[:, None, None, :].astype(jnp.float32) / total_y
    )
    angle = 2.0 * math.pi * fraction
    ramp = jnp.sqrt(1.0 + 2.0 * x_coords.astype(jnp.float32) / total_x)[None, None, :, None]
    waves = jnp.stack([jnp.cos(angle) * ramp, jnp.sin(angle) * ramp], 1)
    polar = ((probe_ids % 3)[:, None] == jnp.arange(3, dtype=jnp.int32)[None, :]).astype(
        jnp.float32
    )
    return waves, polar


def butterfly_sum(value, axis):
    size = lax.axis_size(axis)
    if size & (size - 1):
        return lax.psum(value, axis)
    step = 1
    while step < size:
        value = value + lax.ppermute(value, axis, [(i, i ^ step) for i in range(size)])
        step *= 2
    return value


def y_roll(x, shift):
    return pltpu.roll(x, shift % x.shape[-1], x.ndim - 1)


def z_roll(x, shift):
    axis = x.ndim - 3
    n = x.shape[axis]
    s = shift % n
    if s == 0:
        return x
    return jnp.concatenate(
        [lax.slice_in_dim(x, n - s, n, axis=axis), lax.slice_in_dim(x, 0, n - s, axis=axis)], axis
    )


def field_rows(vector, bond, lo, n):
    up = vector(lo + 2, lo + n)
    down = vector(lo, lo + n - 2)
    centre = vector(lo + 1, lo + n - 1)
    total = bond(0, lo + 1, lo + n - 1) * up + bond(0, lo, lo + n - 2) * down
    bond_y = bond(1, lo + 1, lo + n - 1)
    total = total + bond_y * y_roll(centre, -1) + y_roll(bond_y, 1) * y_roll(centre, 1)
    bond_z = bond(2, lo + 1, lo + n - 1)
    total = total + bond_z * z_roll(centre, -1) + z_roll(bond_z, 1) * z_roll(centre, 1)
    return total


def local_kernel(halo, slab_rows, *refs):
    slab_refs = refs[:2 * HALO_SLABS + 1]
    start_ref, polar_ref, exchange_ref, relaxed_ref, last_ref, sums_ref, win, sweep_a, sweep_b, bonds_b, bonds_yr, bonds_zr, spins_b, t1, t2, t3 = refs[2 * HALO_SLABS + 1:]
    for k, slab_ref in enumerate(slab_refs):
        block = slab_ref[...]
        cos_polar, azimuth, bond_class = block[0], block[1], block[2:5]
        radial = jnp.sqrt(1.0 - cos_polar * cos_polar)
        strengths = jnp.zeros(bond_class.shape, jnp.float32)
        for class_index in range(NCLASS):
            strengths = jnp.where(bond_class == class_index, exchange_ref[class_index], strengths)
        site = jnp.stack([radial * jnp.cos(azimuth), radial * jnp.sin(azimuth), cos_polar], 0)
        win[:, :, k * slab_rows:(k + 1) * slab_rows, :] = jnp.concatenate([site, strengths], 0)
    width = len(slab_refs) * slab_rows

    def bond(d, a, b):
        return win[3 + d, :, a:b, :]

    def from_window(a, b):
        return win[0:3, :, a:b, :]

    first = halo - CHEB
    n_start = slab_rows + 2 * CHEB
    base_a = first

    def from_a(a, b):
        return sweep_a[:, :, a - base_a:b - base_a, :]

    sweep_a[:, :, 0:n_start, :] = relax_update(
        win[0:3, :, first:first + n_start, :], field_rows(from_window, bond, first - 1, n_start + 2)
    )
    sweep_b[:, :, 0:n_start - 2, :] = relax_update(
        sweep_a[:, :, 1:n_start - 1, :], field_rows(from_a, bond, first, n_start)
    )
    base_b = first + 1
    relaxed_ref[...] = sweep_b[:, :, halo - base_b:halo - base_b + slab_rows, :]
    lanes = win.shape[3]
    depth = win.shape[1]
    probes = start_ref.shape[3]
    for xr in range(n_start):
        w = first + xr
        site = jnp.broadcast_to(win[3:6, :, w:w + 1, :], (3, depth, probes, lanes))
        bonds_b[xr] = site
        bonds_yr[xr] = y_roll(site[1], 1)
        bonds_zr[xr] = z_roll(site[2], 1)
    for xr in range(n_start - 2):
        w = first + 1 + xr
        spins_b[xr] = jnp.broadcast_to(sweep_b[:, :, w - base_b:w - base_b + 1, :], (3, depth, probes, lanes))

    polar = [polar_ref[j] for j in range(3)]

    def start_row(i):
        wave = start_ref[i]
        return jnp.stack([wave * polar[j] for j in range(3)], 1)

    t_refs = (start_ref, t1, t2, t3, last_ref)
    for order in range(CHEB):
        lo = first + order
        n = n_start - 2 * order
        source = t_refs[order]
        target = t_refs[order + 1]
        acc = None
        for i in range(n - 2):
            w = lo + 1 + i
            b = w - first
            up = source[i + 2]
            down = source[i]
            centre = source[i + 1]
            total = bonds_b[b, 0] * up + bonds_b[b - 1, 0] * down
            total = total + bonds_b[b, 1] * y_roll(centre, -1) + bonds_yr[b] * y_roll(centre, 1)
            total = total + bonds_b[b, 2] * z_roll(centre, -1) + bonds_zr[b] * z_roll(centre, 1)
            if order == 0:
                spin = spins_b[b - 1]
                turn = (
                    spin[1] * polar[2] - spin[2] * polar[1],
                    spin[2] * polar[0] - spin[0] * polar[2],
                    spin[0] * polar[1] - spin[1] * polar[0],
                )
                advanced = jnp.stack([total * turn[j] for j in range(3)], 1) * -precess_scale
            else:
                previous = start_row(i + 2) if order == 1 else t_refs[order - 1][i + 2]
                advanced = cross_product(spins_b[b - 1], total) * (-2.0 * precess_scale) - previous
            target[i] = advanced.astype(target.dtype)
            if halo <= w < halo + slab_rows:
                squares = advanced * advanced
                part = squares[0] + squares[1]
                part = part[0] + part[1] + part[2]
                part = part[0] + part[1] + part[2] + part[3]
                acc = part if acc is None else acc + part
        sums_ref[order:order + 1, :] = jnp.sum(acc.T, axis=0, keepdims=True)


def run_local(slab_blocks, start, polar, exchange, halo, slab_rows):
    depth, lanes = slab_blocks[0].shape[1], slab_blocks[0].shape[3]
    width = len(slab_blocks) * slab_rows
    n_start, probes = start.shape[0], start.shape[3]
    vec_shape = (start.shape[1], 3) + start.shape[2:]

    def body(*refs):
        local_kernel(halo, slab_rows, *refs)

    sites = n_start * 3 * start[0].size
    return pl.pallas_call(
        body,
        out_shape=(
            jax.ShapeDtypeStruct((3, depth, slab_rows, lanes), jnp.float32),
            jax.ShapeDtypeStruct((slab_rows,) + vec_shape, jnp.bfloat16),
            jax.ShapeDtypeStruct((CHEB, probes), jnp.float32),
        ),
        in_specs=[pl.BlockSpec(memory_space=pltpu.VMEM)] * (len(slab_blocks) + 2)
        + [pl.BlockSpec(memory_space=pltpu.SMEM)],
        out_specs=[pl.BlockSpec(memory_space=pltpu.VMEM)] * 3,
        scratch_shapes=[
            pltpu.VMEM((6, depth, width, lanes), jnp.float32),
            pltpu.VMEM((3, depth, width, lanes), jnp.float32),
            pltpu.VMEM((3, depth, width, lanes), jnp.float32),
            pltpu.VMEM((n_start, 3, depth, probes, lanes), jnp.float32),
            pltpu.VMEM((n_start, depth, probes, lanes), jnp.float32),
            pltpu.VMEM((n_start, depth, probes, lanes), jnp.float32),
            pltpu.VMEM((n_start, 3, depth, probes, lanes), jnp.float32),
        ]
        + [pltpu.VMEM((n_start - 2 * k,) + vec_shape, jnp.float32) for k in range(1, CHEB)],
        cost_estimate=pl.CostEstimate(
            flops=30 * sites + 200 * 3 * depth * width * lanes,
            transcendentals=0,
            bytes_accessed=4 * (6 * depth * width * lanes + 2 * start.size),
        ),
    )(*slab_blocks, start, polar, exchange)


def shards(cos_polar, azimuth, bond_class, exchange, probe_wave):
    groups = lax.axis_size("probe")
    slabs = lax.axis_size("space")
    group = lax.axis_index("probe")
    slab = lax.axis_index("space")
    slab_rows = cos_polar.shape[1]
    block_y = cos_polar.shape[2]
    total_x = slab_rows * slabs
    total_y = block_y * groups
    site_count = total_x * total_y * LZ

    local = jnp.concatenate([cos_polar[None], azimuth[None], bond_class.astype(jnp.float32)], 0)

    pieces = [shifted(local, "probe", k) for k in range(groups)]
    rotated = jnp.concatenate(pieces, -1)
    full_y = jnp.roll(rotated, group * block_y, -1) if groups > 1 else rotated

    slab_blocks = [shifted(full_y, "space", k) for k in range(-HALO_SLABS, HALO_SLABS + 1)]
    halo = HALO_SLABS * slab_rows

    width = slab_rows + 2 * CHEB
    x_coords = (slab * slab_rows - CHEB + jnp.arange(width, dtype=jnp.int32)) % total_x
    y_coords = jnp.arange(total_y, dtype=jnp.int32)
    group_size = probe_wave.shape[0]
    probe_ids = group * group_size + jnp.arange(group_size, dtype=jnp.int32)
    waves, polar = make_probes(probe_wave, probe_ids, x_coords, y_coords, total_x, total_y, LZ)
    waves = jnp.transpose(waves, (3, 1, 2, 0, 4))
    polar = jnp.broadcast_to(polar.T[:, :, None], (3, group_size, total_y))

    relaxed, last, sums = run_local(slab_blocks, waves, polar, exchange, halo, slab_rows)
    relaxed_own = lax.dynamic_slice_in_dim(relaxed, group * block_y, block_y, -1)
    last = jnp.transpose(last, (4, 1, 2, 3, 0, 5))
    moment_rows = butterfly_sum(sums, "space") / site_count
    return (relaxed_own, last, moment_rows.T)


def solution(mesh):
    return jax.shard_map(
        shards,
        mesh=mesh,
        in_specs=(
            P(None, "space", "probe"),
            P(None, "space", "probe"),
            P(None, None, "space", "probe"),
            P(),
            P("probe", None),
        ),
        out_specs=(
            P(None, None, "space", "probe"),
            P("probe", None, None, None, "space", None),
            P("probe", None),
        ),
        check_vma=False,
    )
```

```python
import math

import jax
import jax.numpy as jnp
from jax import lax
from jax.experimental import pallas as pl
from jax.experimental.pallas import tpu as pltpu
from jax.sharding import PartitionSpec as P

LZ = 4
SWEEPS = 2
CHEB = 4
HALO_SLABS = 2
NCLASS = 8


relax_rate = 0.15
precess_scale = 1.0 / 6.0


def shifted(array, axis, shift):
    size = lax.axis_size(axis)
    if shift % size == 0:
        return array
    return lax.ppermute(array, axis, [(i, (i - shift) % size) for i in range(size)])


def cross_product(spin_core, vector):
    spin_a, spin_b, spin_c = (spin_core[0], spin_core[1], spin_core[2])
    vec_a = vector[..., 0, :, :, :]
    vec_b = vector[..., 1, :, :, :]
    vec_c = vector[..., 2, :, :, :]
    return jnp.stack(
        [
            spin_b * vec_c - spin_c * vec_b,
            spin_c * vec_a - spin_a * vec_c,
            spin_a * vec_b - spin_b * vec_a,
        ],
        axis=-4,
    )


def rows(array, start, stop):
    return lax.slice_in_dim(array, start, stop, axis=array.ndim - 2)


def neighbour_window(vector, bonds):
    n = vector.shape[-2]
    along_x, along_y, along_z = (bonds[0], bonds[1], bonds[2])
    total = rows(along_x, 1, n - 1) * rows(vector, 2, n) + rows(along_x, 0, n - 2) * rows(vector, 0, n - 2)
    centre = rows(vector, 1, n - 1)
    bond_y = rows(along_y, 1, n - 1)
    total = total + bond_y * jnp.roll(centre, -1, -1) + jnp.roll(bond_y, 1, -1) * jnp.roll(centre, 1, -1)
    bond_z = rows(along_z, 1, n - 1)
    total = total + bond_z * jnp.roll(centre, -1, -3) + jnp.roll(bond_z, 1, -3) * jnp.roll(centre, 1, -3)
    return total


def relax_update(spins, field):
    turned = cross_product(spins, field)
    twice = cross_product(spins, turned)
    moved = spins - relax_rate * twice
    length = jnp.sqrt(jnp.sum(moved * moved, axis=0))
    return moved / length


def make_probes(probe_wave, probe_ids, x_coords, y_coords, total_x, total_y, depth_z):
    wave_x = probe_wave[:, 0][:, None]
    wave_y = probe_wave[:, 1][:, None]
    wave_z = probe_wave[:, 2][:, None]
    phase_x = wave_x * x_coords[None, :] % total_x
    phase_y = wave_y * y_coords[None, :] % total_y
    phase_z = wave_z * jnp.arange(depth_z, dtype=jnp.int32)[None, :] % depth_z
    fraction = (
        phase_z[:, :, None, None].astype(jnp.float32) / depth_z
        + phase_x[:, None, :, None].astype(jnp.float32) / total_x
        + phase_y[:, None, None, :].astype(jnp.float32) / total_y
    )
    angle = 2.0 * math.pi * fraction
    ramp = jnp.sqrt(1.0 + 2.0 * x_coords.astype(jnp.float32) / total_x)[None, None, :, None]
    waves = jnp.stack([jnp.cos(angle) * ramp, jnp.sin(angle) * ramp], 1)
    polar = ((probe_ids % 3)[:, None] == jnp.arange(3, dtype=jnp.int32)[None, :]).astype(
        jnp.float32
    )
    return waves, polar


def butterfly_sum(value, axis):
    size = lax.axis_size(axis)
    if size & (size - 1):
        return lax.psum(value, axis)
    step = 1
    while step < size:
        value = value + lax.ppermute(value, axis, [(i, i ^ step) for i in range(size)])
        step *= 2
    return value


def y_roll(x, shift):
    return pltpu.roll(x, shift % x.shape[-1], x.ndim - 1)


def z_roll(x, shift):
    axis = x.ndim - 3
    n = x.shape[axis]
    s = shift % n
    if s == 0:
        return x
    return jnp.concatenate(
        [lax.slice_in_dim(x, n - s, n, axis=axis), lax.slice_in_dim(x, 0, n - s, axis=axis)], axis
    )


def field_rows(vector, bond, lo, n):
    up = vector(lo + 2, lo + n)
    down = vector(lo, lo + n - 2)
    centre = vector(lo + 1, lo + n - 1)
    total = bond(0, lo + 1, lo + n - 1) * up + bond(0, lo, lo + n - 2) * down
    bond_y = bond(1, lo + 1, lo + n - 1)
    total = total + bond_y * y_roll(centre, -1) + y_roll(bond_y, 1) * y_roll(centre, 1)
    bond_z = bond(2, lo + 1, lo + n - 1)
    total = total + bond_z * z_roll(centre, -1) + z_roll(bond_z, 1) * z_roll(centre, 1)
    return total


def local_kernel(halo, slab_rows, *refs):
    slab_refs = refs[:2 * HALO_SLABS + 1]
    start_ref, polar_ref, exchange_ref, relaxed_ref, last_ref, sums_ref, win, sweep_a, sweep_b, bonds_b, bonds_yr, bonds_zr, spins_b, t1, t2, t3 = refs[2 * HALO_SLABS + 1:]
    for k, slab_ref in enumerate(slab_refs):
        block = slab_ref[...]
        cos_polar, azimuth, bond_class = block[0], block[1], block[2:5]
        radial = jnp.sqrt(1.0 - cos_polar * cos_polar)
        strengths = jnp.zeros(bond_class.shape, jnp.float32)
        for class_index in range(NCLASS):
            strengths = jnp.where(bond_class == class_index, exchange_ref[class_index], strengths)
        site = jnp.stack([radial * jnp.cos(azimuth), radial * jnp.sin(azimuth), cos_polar], 0)
        win[:, :, k * slab_rows:(k + 1) * slab_rows, :] = jnp.concatenate([site, strengths], 0)
    width = len(slab_refs) * slab_rows

    def bond(d, a, b):
        return win[3 + d, :, a:b, :]

    def from_window(a, b):
        return win[0:3, :, a:b, :]

    first = halo - CHEB
    n_start = slab_rows + 2 * CHEB
    base_a = first

    def from_a(a, b):
        return sweep_a[:, :, a - base_a:b - base_a, :]

    sweep_a[:, :, 0:n_start, :] = relax_update(
        win[0:3, :, first:first + n_start, :], field_rows(from_window, bond, first - 1, n_start + 2)
    )
    sweep_b[:, :, 0:n_start - 2, :] = relax_update(
        sweep_a[:, :, 1:n_start - 1, :], field_rows(from_a, bond, first, n_start)
    )
    base_b = first + 1
    relaxed_ref[...] = sweep_b[:, :, halo - base_b:halo - base_b + slab_rows, :]
    lanes = win.shape[3]
    depth = win.shape[1]
    probes = start_ref.shape[3]
    for xr in range(n_start):
        w = first + xr
        site = jnp.broadcast_to(win[3:6, :, w:w + 1, :], (3, depth, probes, lanes))
        bonds_b[xr] = site
        bonds_yr[xr] = y_roll(site[1], 1)
        bonds_zr[xr] = z_roll(site[2], 1)
    for xr in range(n_start - 2):
        w = first + 1 + xr
        spins_b[xr] = jnp.broadcast_to(sweep_b[:, :, w - base_b:w - base_b + 1, :], (3, depth, probes, lanes))

    sublane = lax.broadcasted_iota(jnp.int32, (probes, lanes), 0)
    local_comp = jnp.zeros((probes, lanes), jnp.int32)
    for p in range(probes):
        local_comp = jnp.where(sublane == p, p % 3, local_comp)
    comp = local_comp + polar_ref[0] % 3
    comp = jnp.where(comp >= 3, comp - 3, comp)
    polar = [jnp.where(comp == j, 1.0, 0.0).astype(jnp.float32) for j in range(3)]

    def start_row(i):
        wave = start_ref[i]
        return jnp.stack([wave * polar[j] for j in range(3)], 1)

    t_refs = (start_ref, t1, t2, t3, last_ref)
    for order in range(CHEB):
        lo = first + order
        n = n_start - 2 * order
        source = t_refs[order]
        target = t_refs[order + 1]
        acc = None
        for i in range(n - 2):
            w = lo + 1 + i
            b = w - first
            up = source[i + 2]
            down = source[i]
            centre = source[i + 1]
            total = bonds_b[b, 0] * up + bonds_b[b - 1, 0] * down
            total = total + bonds_b[b, 1] * y_roll(centre, -1) + bonds_yr[b] * y_roll(centre, 1)
            total = total + bonds_b[b, 2] * z_roll(centre, -1) + bonds_zr[b] * z_roll(centre, 1)
            if order == 0:
                spin = spins_b[b - 1]
                turn = (
                    spin[1] * polar[2] - spin[2] * polar[1],
                    spin[2] * polar[0] - spin[0] * polar[2],
                    spin[0] * polar[1] - spin[1] * polar[0],
                )
                advanced = jnp.stack([total * turn[j] for j in range(3)], 1) * -precess_scale
            else:
                previous = start_row(i + 2) if order == 1 else t_refs[order - 1][i + 2]
                advanced = cross_product(spins_b[b - 1], total) * (-2.0 * precess_scale) - previous
            target[i] = advanced.astype(target.dtype)
            if halo <= w < halo + slab_rows:
                squares = advanced * advanced
                part = squares[0] + squares[1]
                part = part[0] + part[1] + part[2]
                part = part[0] + part[1] + part[2] + part[3]
                acc = part if acc is None else acc + part
        sums_ref[order:order + 1, :] = jnp.sum(acc.T, axis=0, keepdims=True)


def run_local(slab_blocks, start, polar, exchange, halo, slab_rows):
    depth, lanes = slab_blocks[0].shape[1], slab_blocks[0].shape[3]
    width = len(slab_blocks) * slab_rows
    n_start, probes = start.shape[0], start.shape[3]
    vec_shape = (start.shape[1], 3) + start.shape[2:]

    def body(*refs):
        local_kernel(halo, slab_rows, *refs)

    sites = n_start * 3 * start[0].size
    return pl.pallas_call(
        body,
        out_shape=(
            jax.ShapeDtypeStruct((3, depth, slab_rows, lanes), jnp.float32),
            jax.ShapeDtypeStruct((slab_rows,) + vec_shape, jnp.bfloat16),
            jax.ShapeDtypeStruct((CHEB, probes), jnp.float32),
        ),
        in_specs=[pl.BlockSpec(memory_space=pltpu.VMEM)] * (len(slab_blocks) + 1)
        + [pl.BlockSpec(memory_space=pltpu.SMEM)] * 2,
        out_specs=[pl.BlockSpec(memory_space=pltpu.VMEM)] * 3,
        scratch_shapes=[
            pltpu.VMEM((6, depth, width, lanes), jnp.float32),
            pltpu.VMEM((3, depth, width, lanes), jnp.float32),
            pltpu.VMEM((3, depth, width, lanes), jnp.float32),
            pltpu.VMEM((n_start, 3, depth, probes, lanes), jnp.float32),
            pltpu.VMEM((n_start, depth, probes, lanes), jnp.float32),
            pltpu.VMEM((n_start, depth, probes, lanes), jnp.float32),
            pltpu.VMEM((n_start, 3, depth, probes, lanes), jnp.float32),
        ]
        + [pltpu.VMEM((n_start - 2 * k,) + vec_shape, jnp.float32) for k in range(1, CHEB)],
        cost_estimate=pl.CostEstimate(
            flops=30 * sites + 200 * 3 * depth * width * lanes,
            transcendentals=0,
            bytes_accessed=4 * (6 * depth * width * lanes + 2 * start.size),
        ),
    )(*slab_blocks, start, polar, exchange)


def shards(cos_polar, azimuth, bond_class, exchange, probe_wave):
    groups = lax.axis_size("probe")
    slabs = lax.axis_size("space")
    group = lax.axis_index("probe")
    slab = lax.axis_index("space")
    slab_rows = cos_polar.shape[1]
    block_y = cos_polar.shape[2]
    total_x = slab_rows * slabs
    total_y = block_y * groups
    site_count = total_x * total_y * LZ

    local = jnp.concatenate([cos_polar[None], azimuth[None], bond_class.astype(jnp.float32)], 0)

    pieces = [shifted(local, "probe", k) for k in range(groups)]
    rotated = jnp.concatenate(pieces, -1)
    full_y = jnp.roll(rotated, group * block_y, -1) if groups > 1 else rotated

    slab_blocks = [shifted(full_y, "space", k) for k in range(-HALO_SLABS, HALO_SLABS + 1)]
    halo = HALO_SLABS * slab_rows

    width = slab_rows + 2 * CHEB
    x_coords = (slab * slab_rows - CHEB + jnp.arange(width, dtype=jnp.int32)) % total_x
    y_coords = jnp.arange(total_y, dtype=jnp.int32)
    group_size = probe_wave.shape[0]
    probe_ids = group * group_size + jnp.arange(group_size, dtype=jnp.int32)
    waves, polar = make_probes(probe_wave, probe_ids, x_coords, y_coords, total_x, total_y, LZ)
    waves = jnp.transpose(waves, (3, 1, 2, 0, 4))
    first_id = (group * group_size).astype(jnp.int32).reshape(1)

    relaxed, last, sums = run_local(slab_blocks, waves, first_id, exchange, halo, slab_rows)
    relaxed_own = lax.dynamic_slice_in_dim(relaxed, group * block_y, block_y, -1)
    last = jnp.transpose(last, (4, 1, 2, 3, 0, 5))
    moment_rows = butterfly_sum(sums, "space") / site_count
    return (relaxed_own, last, moment_rows.T)


def solution(mesh):
    return jax.shard_map(
        shards,
        mesh=mesh,
        in_specs=(
            P(None, "space", "probe"),
            P(None, "space", "probe"),
            P(None, None, "space", "probe"),
            P(),
            P("probe", None),
        ),
        out_specs=(
            P(None, None, "space", "probe"),
            P("probe", None, None, None, "space", None),
            P("probe", None),
        ),
        check_vma=False,
    )
```

```python
import math

import jax
import jax.numpy as jnp
from jax import lax
from jax.experimental import pallas as pl
from jax.experimental.pallas import tpu as pltpu
from jax.sharding import PartitionSpec as P

LZ = 4
SWEEPS = 2
CHEB = 4
HALO_SLABS = 2
NCLASS = 8


relax_rate = 0.15
precess_scale = 1.0 / 6.0


def shifted(array, axis, shift):
    size = lax.axis_size(axis)
    if shift % size == 0:
        return array
    return lax.ppermute(array, axis, [(i, (i - shift) % size) for i in range(size)])


def cross_product(spin_core, vector):
    spin_a, spin_b, spin_c = (spin_core[0], spin_core[1], spin_core[2])
    vec_a = vector[..., 0, :, :, :]
    vec_b = vector[..., 1, :, :, :]
    vec_c = vector[..., 2, :, :, :]
    return jnp.stack(
        [
            spin_b * vec_c - spin_c * vec_b,
            spin_c * vec_a - spin_a * vec_c,
            spin_a * vec_b - spin_b * vec_a,
        ],
        axis=-4,
    )


def rows(array, start, stop):
    return lax.slice_in_dim(array, start, stop, axis=array.ndim - 2)


def neighbour_window(vector, bonds):
    n = vector.shape[-2]
    along_x, along_y, along_z = (bonds[0], bonds[1], bonds[2])
    total = rows(along_x, 1, n - 1) * rows(vector, 2, n) + rows(along_x, 0, n - 2) * rows(vector, 0, n - 2)
    centre = rows(vector, 1, n - 1)
    bond_y = rows(along_y, 1, n - 1)
    total = total + bond_y * jnp.roll(centre, -1, -1) + jnp.roll(bond_y, 1, -1) * jnp.roll(centre, 1, -1)
    bond_z = rows(along_z, 1, n - 1)
    total = total + bond_z * jnp.roll(centre, -1, -3) + jnp.roll(bond_z, 1, -3) * jnp.roll(centre, 1, -3)
    return total


def relax_update(spins, field):
    turned = cross_product(spins, field)
    twice = cross_product(spins, turned)
    moved = spins - relax_rate * twice
    length = jnp.sqrt(jnp.sum(moved * moved, axis=0))
    return moved / length


def make_probes(probe_wave, probe_ids, x_coords, y_coords, total_x, total_y, depth_z):
    wave_x = probe_wave[:, 0][:, None]
    wave_y = probe_wave[:, 1][:, None]
    wave_z = probe_wave[:, 2][:, None]
    phase_x = wave_x * x_coords[None, :] % total_x
    phase_y = wave_y * y_coords[None, :] % total_y
    phase_z = wave_z * jnp.arange(depth_z, dtype=jnp.int32)[None, :] % depth_z
    fraction = (
        phase_z[:, :, None, None].astype(jnp.float32) / depth_z
        + phase_x[:, None, :, None].astype(jnp.float32) / total_x
        + phase_y[:, None, None, :].astype(jnp.float32) / total_y
    )
    angle = 2.0 * math.pi * fraction
    ramp = jnp.sqrt(1.0 + 2.0 * x_coords.astype(jnp.float32) / total_x)[None, None, :, None]
    waves = jnp.stack([jnp.cos(angle) * ramp, jnp.sin(angle) * ramp], 1)
    polar = ((probe_ids % 3)[:, None] == jnp.arange(3, dtype=jnp.int32)[None, :]).astype(
        jnp.float32
    )
    return waves, polar


def butterfly_sum(value, axis):
    size = lax.axis_size(axis)
    if size & (size - 1):
        return lax.psum(value, axis)
    step = 1
    while step < size:
        value = value + lax.ppermute(value, axis, [(i, i ^ step) for i in range(size)])
        step *= 2
    return value


def y_roll(x, shift):
    return pltpu.roll(x, shift % x.shape[-1], x.ndim - 1)


def z_roll(x, shift):
    axis = x.ndim - 3
    n = x.shape[axis]
    s = shift % n
    if s == 0:
        return x
    return jnp.concatenate(
        [lax.slice_in_dim(x, n - s, n, axis=axis), lax.slice_in_dim(x, 0, n - s, axis=axis)], axis
    )


def field_rows(vector, bond, lo, n):
    up = vector(lo + 2, lo + n)
    down = vector(lo, lo + n - 2)
    centre = vector(lo + 1, lo + n - 1)
    total = bond(0, lo + 1, lo + n - 1) * up + bond(0, lo, lo + n - 2) * down
    bond_y = bond(1, lo + 1, lo + n - 1)
    total = total + bond_y * y_roll(centre, -1) + y_roll(bond_y, 1) * y_roll(centre, 1)
    bond_z = bond(2, lo + 1, lo + n - 1)
    total = total + bond_z * z_roll(centre, -1) + z_roll(bond_z, 1) * z_roll(centre, 1)
    return total


def local_kernel(halo, slab_rows, *refs):
    slab_refs = refs[:2 * HALO_SLABS + 1]
    start_ref, polar_ref, exchange_ref, relaxed_ref, last_ref, sums_ref, win, sweep_a, sweep_b, bonds_b, bonds_yr, bonds_zr, spins_b, t1, t2, t3 = refs[2 * HALO_SLABS + 1:]
    for k, slab_ref in enumerate(slab_refs):
        block = slab_ref[...]
        cos_polar, azimuth, bond_class = block[0], block[1], block[2:5]
        radial = jnp.sqrt(1.0 - cos_polar * cos_polar)
        strengths = jnp.zeros(bond_class.shape, jnp.float32)
        for class_index in range(NCLASS):
            strengths = jnp.where(bond_class == class_index, exchange_ref[class_index], strengths)
        site = jnp.stack([radial * jnp.cos(azimuth), radial * jnp.sin(azimuth), cos_polar], 0)
        win[:, :, k * slab_rows:(k + 1) * slab_rows, :] = jnp.concatenate([site, strengths], 0)
    width = len(slab_refs) * slab_rows

    def bond(d, a, b):
        return win[3 + d, :, a:b, :]

    def from_window(a, b):
        return win[0:3, :, a:b, :]

    first = halo - CHEB
    n_start = slab_rows + 2 * CHEB
    base_a = first

    def from_a(a, b):
        return sweep_a[:, :, a - base_a:b - base_a, :]

    sweep_a[:, :, 0:n_start, :] = relax_update(
        win[0:3, :, first:first + n_start, :], field_rows(from_window, bond, first - 1, n_start + 2)
    )
    sweep_b[:, :, 0:n_start - 2, :] = relax_update(
        sweep_a[:, :, 1:n_start - 1, :], field_rows(from_a, bond, first, n_start)
    )
    base_b = first + 1
    relaxed_ref[...] = sweep_b[:, :, halo - base_b:halo - base_b + slab_rows, :]
    lanes = win.shape[3]
    depth = win.shape[1]
    probes = start_ref.shape[3]
    for xr in range(n_start):
        w = first + xr
        site = jnp.broadcast_to(win[3:6, :, w:w + 1, :], (3, depth, probes, lanes))
        bonds_b[xr] = site
        bonds_yr[xr] = y_roll(site[1], 1)
        bonds_zr[xr] = z_roll(site[2], 1)
    for xr in range(n_start - 2):
        w = first + 1 + xr
        spins_b[xr] = jnp.broadcast_to(sweep_b[:, :, w - base_b:w - base_b + 1, :], (3, depth, probes, lanes))

    sublane = lax.broadcasted_iota(jnp.int32, (probes, lanes), 0)
    polar = []
    for j in range(3):
        factor = jnp.zeros((probes, lanes), jnp.float32)
        for p in range(probes):
            factor = jnp.where(sublane == p, polar_ref[j, p], factor)
        polar.append(factor)

    def start_row(i):
        wave = start_ref[i]
        return jnp.stack([wave * polar[j] for j in range(3)], 1)

    t_refs = (start_ref, t1, t2, t3, last_ref)
    for order in range(CHEB):
        lo = first + order
        n = n_start - 2 * order
        source = t_refs[order]
        target = t_refs[order + 1]
        acc = None
        for i in range(n - 2):
            w = lo + 1 + i
            b = w - first
            up = source[i + 2]
            down = source[i]
            centre = source[i + 1]
            total = bonds_b[b, 0] * up + bonds_b[b - 1, 0] * down
            total = total + bonds_b[b, 1] * y_roll(centre, -1) + bonds_yr[b] * y_roll(centre, 1)
            total = total + bonds_b[b, 2] * z_roll(centre, -1) + bonds_zr[b] * z_roll(centre, 1)
            if order == 0:
                spin = spins_b[b - 1]
                turn = (
                    spin[1] * polar[2] - spin[2] * polar[1],
                    spin[2] * polar[0] - spin[0] * polar[2],
                    spin[0] * polar[1] - spin[1] * polar[0],
                )
                advanced = jnp.stack([total * turn[j] for j in range(3)], 1) * -precess_scale
            else:
                previous = start_row(i + 2) if order == 1 else t_refs[order - 1][i + 2]
                advanced = cross_product(spins_b[b - 1], total) * (-2.0 * precess_scale) - previous
            target[i] = advanced.astype(target.dtype)
            if halo <= w < halo + slab_rows:
                squares = advanced * advanced
                part = squares[0] + squares[1]
                part = part[0] + part[1] + part[2]
                part = part[0] + part[1] + part[2] + part[3]
                acc = part if acc is None else acc + part
        sums_ref[order:order + 1, :] = jnp.sum(acc.T, axis=0, keepdims=True)


def run_local(slab_blocks, start, polar, exchange, halo, slab_rows):
    depth, lanes = slab_blocks[0].shape[1], slab_blocks[0].shape[3]
    width = len(slab_blocks) * slab_rows
    n_start, probes = start.shape[0], start.shape[3]
    vec_shape = (start.shape[1], 3) + start.shape[2:]

    def body(*refs):
        local_kernel(halo, slab_rows, *refs)

    sites = n_start * 3 * start[0].size
    return pl.pallas_call(
        body,
        out_shape=(
            jax.ShapeDtypeStruct((3, depth, slab_rows, lanes), jnp.float32),
            jax.ShapeDtypeStruct((slab_rows,) + vec_shape, jnp.bfloat16),
            jax.ShapeDtypeStruct((CHEB, probes), jnp.float32),
        ),
        in_specs=[pl.BlockSpec(memory_space=pltpu.VMEM)] * (len(slab_blocks) + 1)
        + [pl.BlockSpec(memory_space=pltpu.SMEM)] * 2,
        out_specs=[pl.BlockSpec(memory_space=pltpu.VMEM)] * 3,
        scratch_shapes=[
            pltpu.VMEM((6, depth, width, lanes), jnp.float32),
            pltpu.VMEM((3, depth, width, lanes), jnp.float32),
            pltpu.VMEM((3, depth, width, lanes), jnp.float32),
            pltpu.VMEM((n_start, 3, depth, probes, lanes), jnp.float32),
            pltpu.VMEM((n_start, depth, probes, lanes), jnp.float32),
            pltpu.VMEM((n_start, depth, probes, lanes), jnp.float32),
            pltpu.VMEM((n_start, 3, depth, probes, lanes), jnp.float32),
        ]
        + [pltpu.VMEM((n_start - 2 * k,) + vec_shape, jnp.float32) for k in range(1, CHEB)],
        cost_estimate=pl.CostEstimate(
            flops=30 * sites + 200 * 3 * depth * width * lanes,
            transcendentals=0,
            bytes_accessed=4 * (6 * depth * width * lanes + 2 * start.size),
        ),
    )(*slab_blocks, start, polar, exchange)


def shards(cos_polar, azimuth, bond_class, exchange, probe_wave):
    groups = lax.axis_size("probe")
    slabs = lax.axis_size("space")
    group = lax.axis_index("probe")
    slab = lax.axis_index("space")
    slab_rows = cos_polar.shape[1]
    block_y = cos_polar.shape[2]
    total_x = slab_rows * slabs
    total_y = block_y * groups
    site_count = total_x * total_y * LZ

    local = jnp.concatenate([cos_polar[None], azimuth[None], bond_class.astype(jnp.float32)], 0)

    pieces = [shifted(local, "probe", k) for k in range(groups)]
    rotated = jnp.concatenate(pieces, -1)
    full_y = jnp.roll(rotated, group * block_y, -1) if groups > 1 else rotated

    slab_blocks = [shifted(full_y, "space", k) for k in range(-HALO_SLABS, HALO_SLABS + 1)]
    halo = HALO_SLABS * slab_rows

    width = slab_rows + 2 * CHEB
    x_coords = (slab * slab_rows - CHEB + jnp.arange(width, dtype=jnp.int32)) % total_x
    y_coords = jnp.arange(total_y, dtype=jnp.int32)
    group_size = probe_wave.shape[0]
    probe_ids = group * group_size + jnp.arange(group_size, dtype=jnp.int32)
    waves, polar = make_probes(probe_wave, probe_ids, x_coords, y_coords, total_x, total_y, LZ)
    waves = jnp.transpose(waves, (3, 1, 2, 0, 4))
    polar = polar.T

    relaxed, last, sums = run_local(slab_blocks, waves, polar, exchange, halo, slab_rows)
    relaxed_own = lax.dynamic_slice_in_dim(relaxed, group * block_y, block_y, -1)
    last = jnp.transpose(last, (4, 1, 2, 3, 0, 5))
    moment_rows = butterfly_sum(sums, "space") / site_count
    return (relaxed_own, last, moment_rows.T)


def solution(mesh):
    return jax.shard_map(
        shards,
        mesh=mesh,
        in_specs=(
            P(None, "space", "probe"),
            P(None, "space", "probe"),
            P(None, None, "space", "probe"),
            P(),
            P("probe", None),
        ),
        out_specs=(
            P(None, None, "space", "probe"),
            P("probe", None, None, None, "space", None),
            P("probe", None),
        ),
        check_vma=False,
    )
```

```python
import math

import jax
import jax.numpy as jnp
from jax import lax
from jax.experimental import pallas as pl
from jax.experimental.pallas import tpu as pltpu
from jax.sharding import PartitionSpec as P

LZ = 4
SWEEPS = 2
CHEB = 4
HALO_SLABS = 2
NCLASS = 8


relax_rate = 0.15
precess_scale = 1.0 / 6.0


def shifted(array, axis, shift):
    size = lax.axis_size(axis)
    if shift % size == 0:
        return array
    return lax.ppermute(array, axis, [(i, (i - shift) % size) for i in range(size)])


def cross_product(spin_core, vector):
    spin_a, spin_b, spin_c = (spin_core[0], spin_core[1], spin_core[2])
    vec_a = vector[..., 0, :, :, :]
    vec_b = vector[..., 1, :, :, :]
    vec_c = vector[..., 2, :, :, :]
    return jnp.stack(
        [
            spin_b * vec_c - spin_c * vec_b,
            spin_c * vec_a - spin_a * vec_c,
            spin_a * vec_b - spin_b * vec_a,
        ],
        axis=-4,
    )


def rows(array, start, stop):
    return lax.slice_in_dim(array, start, stop, axis=array.ndim - 2)


def neighbour_window(vector, bonds):
    n = vector.shape[-2]
    along_x, along_y, along_z = (bonds[0], bonds[1], bonds[2])
    total = rows(along_x, 1, n - 1) * rows(vector, 2, n) + rows(along_x, 0, n - 2) * rows(vector, 0, n - 2)
    centre = rows(vector, 1, n - 1)
    bond_y = rows(along_y, 1, n - 1)
    total = total + bond_y * jnp.roll(centre, -1, -1) + jnp.roll(bond_y, 1, -1) * jnp.roll(centre, 1, -1)
    bond_z = rows(along_z, 1, n - 1)
    total = total + bond_z * jnp.roll(centre, -1, -3) + jnp.roll(bond_z, 1, -3) * jnp.roll(centre, 1, -3)
    return total


def relax_update(spins, field):
    turned = cross_product(spins, field)
    twice = cross_product(spins, turned)
    moved = spins - relax_rate * twice
    length = jnp.sqrt(jnp.sum(moved * moved, axis=0))
    return moved / length


def make_probes(probe_wave, probe_ids, x_coords, y_coords, total_x, total_y, depth_z):
    wave_x = probe_wave[:, 0][:, None]
    wave_y = probe_wave[:, 1][:, None]
    wave_z = probe_wave[:, 2][:, None]
    phase_x = wave_x * x_coords[None, :] % total_x
    phase_y = wave_y * y_coords[None, :] % total_y
    phase_z = wave_z * jnp.arange(depth_z, dtype=jnp.int32)[None, :] % depth_z
    fraction = (
        phase_z[:, :, None, None].astype(jnp.float32) / depth_z
        + phase_x[:, None, :, None].astype(jnp.float32) / total_x
        + phase_y[:, None, None, :].astype(jnp.float32) / total_y
    )
    angle = 2.0 * math.pi * fraction
    ramp = jnp.sqrt(1.0 + 2.0 * x_coords.astype(jnp.float32) / total_x)[None, None, :, None]
    waves = jnp.stack([jnp.cos(angle) * ramp, jnp.sin(angle) * ramp], 1)
    polar = ((probe_ids % 3)[:, None] == jnp.arange(3, dtype=jnp.int32)[None, :]).astype(
        jnp.float32
    )
    return waves, polar


def butterfly_sum(value, axis):
    size = lax.axis_size(axis)
    if size & (size - 1):
        return lax.psum(value, axis)
    step = 1
    while step < size:
        value = value + lax.ppermute(value, axis, [(i, i ^ step) for i in range(size)])
        step *= 2
    return value


def y_roll(x, shift):
    return pltpu.roll(x, shift % x.shape[-1], x.ndim - 1)


def z_roll(x, shift):
    axis = x.ndim - 3
    n = x.shape[axis]
    s = shift % n
    if s == 0:
        return x
    return jnp.concatenate(
        [lax.slice_in_dim(x, n - s, n, axis=axis), lax.slice_in_dim(x, 0, n - s, axis=axis)], axis
    )


def field_rows(vector, bond, lo, n):
    up = vector(lo + 2, lo + n)
    down = vector(lo, lo + n - 2)
    centre = vector(lo + 1, lo + n - 1)
    total = bond(0, lo + 1, lo + n - 1) * up + bond(0, lo, lo + n - 2) * down
    bond_y = bond(1, lo + 1, lo + n - 1)
    total = total + bond_y * y_roll(centre, -1) + y_roll(bond_y, 1) * y_roll(centre, 1)
    bond_z = bond(2, lo + 1, lo + n - 1)
    total = total + bond_z * z_roll(centre, -1) + z_roll(bond_z, 1) * z_roll(centre, 1)
    return total


def local_kernel(halo, slab_rows, *refs):
    slab_refs = refs[:2 * HALO_SLABS + 1]
    start_ref, polar_ref, exchange_ref, relaxed_ref, last_ref, sums_ref, win, sweep_a, sweep_b, bonds_b, bonds_yr, bonds_zr, spins_b, t1, t2, t3, late_buf, late_sem = refs[2 * HALO_SLABS + 1:]
    late_copy = pltpu.make_async_copy(slab_refs[-1], late_buf, late_sem)
    late_copy.start()
    for k, slab_ref in enumerate(slab_refs):
        if k == len(slab_refs) - 1:
            late_copy.wait()
            block = late_buf[...]
        else:
            block = slab_ref[...]
        cos_polar, azimuth, bond_class = block[0], block[1], block[2:5]
        radial = jnp.sqrt(1.0 - cos_polar * cos_polar)
        strengths = jnp.zeros(bond_class.shape, jnp.float32)
        for class_index in range(NCLASS):
            strengths = jnp.where(bond_class == class_index, exchange_ref[class_index], strengths)
        site = jnp.stack([radial * jnp.cos(azimuth), radial * jnp.sin(azimuth), cos_polar], 0)
        win[:, :, k * slab_rows:(k + 1) * slab_rows, :] = jnp.concatenate([site, strengths], 0)
    width = len(slab_refs) * slab_rows

    def bond(d, a, b):
        return win[3 + d, :, a:b, :]

    def from_window(a, b):
        return win[0:3, :, a:b, :]

    first = halo - CHEB
    n_start = slab_rows + 2 * CHEB
    base_a = first

    def from_a(a, b):
        return sweep_a[:, :, a - base_a:b - base_a, :]

    sweep_a[:, :, 0:n_start, :] = relax_update(
        win[0:3, :, first:first + n_start, :], field_rows(from_window, bond, first - 1, n_start + 2)
    )
    sweep_b[:, :, 0:n_start - 2, :] = relax_update(
        sweep_a[:, :, 1:n_start - 1, :], field_rows(from_a, bond, first, n_start)
    )
    base_b = first + 1
    relaxed_ref[...] = sweep_b[:, :, halo - base_b:halo - base_b + slab_rows, :]
    lanes = win.shape[3]
    depth = win.shape[1]
    probes = start_ref.shape[3]
    for xr in range(n_start):
        w = first + xr
        site = jnp.broadcast_to(win[3:6, :, w:w + 1, :], (3, depth, probes, lanes))
        bonds_b[xr] = site
        bonds_yr[xr] = y_roll(site[1], 1)
        bonds_zr[xr] = z_roll(site[2], 1)
    for xr in range(n_start - 2):
        w = first + 1 + xr
        spins_b[xr] = jnp.broadcast_to(sweep_b[:, :, w - base_b:w - base_b + 1, :], (3, depth, probes, lanes))

    sublane = lax.broadcasted_iota(jnp.int32, (probes, lanes), 0)
    polar = []
    for j in range(3):
        factor = jnp.zeros((probes, lanes), jnp.float32)
        for p in range(probes):
            factor = jnp.where(sublane == p, polar_ref[j, p], factor)
        polar.append(factor)

    def start_row(i):
        wave = start_ref[i]
        return jnp.stack([wave * polar[j] for j in range(3)], 1)

    t_refs = (start_ref, t1, t2, t3, last_ref)
    for order in range(CHEB):
        lo = first + order
        n = n_start - 2 * order
        source = t_refs[order]
        target = t_refs[order + 1]
        acc = None
        for i in range(n - 2):
            w = lo + 1 + i
            b = w - first
            up = source[i + 2]
            down = source[i]
            centre = source[i + 1]
            total = bonds_b[b, 0] * up + bonds_b[b - 1, 0] * down
            total = total + bonds_b[b, 1] * y_roll(centre, -1) + bonds_yr[b] * y_roll(centre, 1)
            total = total + bonds_b[b, 2] * z_roll(centre, -1) + bonds_zr[b] * z_roll(centre, 1)
            if order == 0:
                spin = spins_b[b - 1]
                turn = (
                    spin[1] * polar[2] - spin[2] * polar[1],
                    spin[2] * polar[0] - spin[0] * polar[2],
                    spin[0] * polar[1] - spin[1] * polar[0],
                )
                advanced = jnp.stack([total * turn[j] for j in range(3)], 1) * -precess_scale
            else:
                previous = start_row(i + 2) if order == 1 else t_refs[order - 1][i + 2]
                advanced = cross_product(spins_b[b - 1], total) * (-2.0 * precess_scale) - previous
            target[i] = advanced.astype(target.dtype)
            if halo <= w < halo + slab_rows:
                squares = advanced * advanced
                part = squares[0] + squares[1]
                part = part[0] + part[1] + part[2]
                part = part[0] + part[1] + part[2] + part[3]
                acc = part if acc is None else acc + part
        sums_ref[order:order + 1, :] = jnp.sum(acc.T, axis=0, keepdims=True)


def run_local(slab_blocks, start, polar, exchange, halo, slab_rows):
    depth, lanes = slab_blocks[0].shape[1], slab_blocks[0].shape[3]
    width = len(slab_blocks) * slab_rows
    n_start, probes = start.shape[0], start.shape[3]
    vec_shape = (start.shape[1], 3) + start.shape[2:]

    def body(*refs):
        local_kernel(halo, slab_rows, *refs)

    sites = n_start * 3 * start[0].size
    return pl.pallas_call(
        body,
        out_shape=(
            jax.ShapeDtypeStruct((3, depth, slab_rows, lanes), jnp.float32),
            jax.ShapeDtypeStruct((slab_rows,) + vec_shape, jnp.bfloat16),
            jax.ShapeDtypeStruct((CHEB, probes), jnp.float32),
        ),
        in_specs=[pl.BlockSpec(memory_space=pltpu.VMEM)] * (len(slab_blocks) - 1)
        + [pl.BlockSpec(memory_space=pl.ANY), pl.BlockSpec(memory_space=pltpu.VMEM)]
        + [pl.BlockSpec(memory_space=pltpu.SMEM)] * 2,
        out_specs=[pl.BlockSpec(memory_space=pltpu.VMEM)] * 3,
        scratch_shapes=[
            pltpu.VMEM((6, depth, width, lanes), jnp.float32),
            pltpu.VMEM((3, depth, width, lanes), jnp.float32),
            pltpu.VMEM((3, depth, width, lanes), jnp.float32),
            pltpu.VMEM((n_start, 3, depth, probes, lanes), jnp.float32),
            pltpu.VMEM((n_start, depth, probes, lanes), jnp.float32),
            pltpu.VMEM((n_start, depth, probes, lanes), jnp.float32),
            pltpu.VMEM((n_start, 3, depth, probes, lanes), jnp.float32),
        ]
        + [pltpu.VMEM((n_start - 2 * k,) + vec_shape, jnp.float32) for k in range(1, CHEB)]
        + [pltpu.VMEM(slab_blocks[-1].shape, jnp.float32), pltpu.SemaphoreType.DMA(())],
        cost_estimate=pl.CostEstimate(
            flops=30 * sites + 200 * 3 * depth * width * lanes,
            transcendentals=0,
            bytes_accessed=4 * (6 * depth * width * lanes + 2 * start.size),
        ),
    )(*slab_blocks, start, polar, exchange)


def shards(cos_polar, azimuth, bond_class, exchange, probe_wave):
    groups = lax.axis_size("probe")
    slabs = lax.axis_size("space")
    group = lax.axis_index("probe")
    slab = lax.axis_index("space")
    slab_rows = cos_polar.shape[1]
    block_y = cos_polar.shape[2]
    total_x = slab_rows * slabs
    total_y = block_y * groups
    site_count = total_x * total_y * LZ

    local = jnp.concatenate([cos_polar[None], azimuth[None], bond_class.astype(jnp.float32)], 0)

    pieces = [shifted(local, "probe", k) for k in range(groups)]
    rotated = jnp.concatenate(pieces, -1)
    full_y = jnp.roll(rotated, group * block_y, -1) if groups > 1 else rotated

    slab_blocks = [shifted(full_y, "space", k) for k in range(-HALO_SLABS, HALO_SLABS + 1)]
    halo = HALO_SLABS * slab_rows

    width = slab_rows + 2 * CHEB
    x_coords = (slab * slab_rows - CHEB + jnp.arange(width, dtype=jnp.int32)) % total_x
    y_coords = jnp.arange(total_y, dtype=jnp.int32)
    group_size = probe_wave.shape[0]
    probe_ids = group * group_size + jnp.arange(group_size, dtype=jnp.int32)
    waves, polar = make_probes(probe_wave, probe_ids, x_coords, y_coords, total_x, total_y, LZ)
    waves = jnp.transpose(waves, (3, 1, 2, 0, 4))
    polar = polar.T

    relaxed, last, sums = run_local(slab_blocks, waves, polar, exchange, halo, slab_rows)
    relaxed_own = lax.dynamic_slice_in_dim(relaxed, group * block_y, block_y, -1)
    last = jnp.transpose(last, (4, 1, 2, 3, 0, 5))
    moment_rows = butterfly_sum(sums, "space") / site_count
    return (relaxed_own, last, moment_rows.T)


def solution(mesh):
    return jax.shard_map(
        shards,
        mesh=mesh,
        in_specs=(
            P(None, "space", "probe"),
            P(None, "space", "probe"),
            P(None, None, "space", "probe"),
            P(),
            P("probe", None),
        ),
        out_specs=(
            P(None, None, "space", "probe"),
            P("probe", None, None, None, "space", None),
            P("probe", None),
        ),
        check_vma=False,
    )
```

```python
import math

import jax
import jax.numpy as jnp
from jax import lax
from jax.experimental import pallas as pl
from jax.experimental.pallas import tpu as pltpu
from jax.sharding import PartitionSpec as P

LZ = 4
SWEEPS = 2
CHEB = 4
HALO_SLABS = 2
NCLASS = 8


relax_rate = 0.15
precess_scale = 1.0 / 6.0


def shifted(array, axis, shift):
    size = lax.axis_size(axis)
    if shift % size == 0:
        return array
    return lax.ppermute(array, axis, [(i, (i - shift) % size) for i in range(size)])


def cross_product(spin_core, vector):
    spin_a, spin_b, spin_c = (spin_core[0], spin_core[1], spin_core[2])
    vec_a = vector[..., 0, :, :, :]
    vec_b = vector[..., 1, :, :, :]
    vec_c = vector[..., 2, :, :, :]
    return jnp.stack(
        [
            spin_b * vec_c - spin_c * vec_b,
            spin_c * vec_a - spin_a * vec_c,
            spin_a * vec_b - spin_b * vec_a,
        ],
        axis=-4,
    )


def rows(array, start, stop):
    return lax.slice_in_dim(array, start, stop, axis=array.ndim - 2)


def neighbour_window(vector, bonds):
    n = vector.shape[-2]
    along_x, along_y, along_z = (bonds[0], bonds[1], bonds[2])
    total = rows(along_x, 1, n - 1) * rows(vector, 2, n) + rows(along_x, 0, n - 2) * rows(vector, 0, n - 2)
    centre = rows(vector, 1, n - 1)
    bond_y = rows(along_y, 1, n - 1)
    total = total + bond_y * jnp.roll(centre, -1, -1) + jnp.roll(bond_y, 1, -1) * jnp.roll(centre, 1, -1)
    bond_z = rows(along_z, 1, n - 1)
    total = total + bond_z * jnp.roll(centre, -1, -3) + jnp.roll(bond_z, 1, -3) * jnp.roll(centre, 1, -3)
    return total


def relax_update(spins, field):
    turned = cross_product(spins, field)
    twice = cross_product(spins, turned)
    moved = spins - relax_rate * twice
    length = jnp.sqrt(jnp.sum(moved * moved, axis=0))
    return moved / length


def make_probes(probe_wave, probe_ids, x_coords, y_coords, total_x, total_y, depth_z):
    wave_x = probe_wave[:, 0][:, None]
    wave_y = probe_wave[:, 1][:, None]
    wave_z = probe_wave[:, 2][:, None]
    phase_x = wave_x * x_coords[None, :] % total_x
    phase_y = wave_y * y_coords[None, :] % total_y
    phase_z = wave_z * jnp.arange(depth_z, dtype=jnp.int32)[None, :] % depth_z
    fraction = (
        phase_z[:, :, None, None].astype(jnp.float32) / depth_z
        + phase_x[:, None, :, None].astype(jnp.float32) / total_x
        + phase_y[:, None, None, :].astype(jnp.float32) / total_y
    )
    angle = 2.0 * math.pi * fraction
    ramp = jnp.sqrt(1.0 + 2.0 * x_coords.astype(jnp.float32) / total_x)[None, None, :, None]
    waves = jnp.stack([jnp.cos(angle) * ramp, jnp.sin(angle) * ramp], 1)
    polar = ((probe_ids % 3)[:, None] == jnp.arange(3, dtype=jnp.int32)[None, :]).astype(
        jnp.float32
    )
    return waves, polar


def butterfly_sum(value, axis):
    size = lax.axis_size(axis)
    if size & (size - 1):
        return lax.psum(value, axis)
    step = 1
    while step < size:
        value = value + lax.ppermute(value, axis, [(i, i ^ step) for i in range(size)])
        step *= 2
    return value


def y_roll(x, shift):
    return pltpu.roll(x, shift % x.shape[-1], x.ndim - 1)


def z_roll(x, shift):
    axis = x.ndim - 3
    n = x.shape[axis]
    s = shift % n
    if s == 0:
        return x
    return jnp.concatenate(
        [lax.slice_in_dim(x, n - s, n, axis=axis), lax.slice_in_dim(x, 0, n - s, axis=axis)], axis
    )


def field_rows(vector, bond, lo, n):
    up = vector(lo + 2, lo + n)
    down = vector(lo, lo + n - 2)
    centre = vector(lo + 1, lo + n - 1)
    total = bond(0, lo + 1, lo + n - 1) * up + bond(0, lo, lo + n - 2) * down
    bond_y = bond(1, lo + 1, lo + n - 1)
    total = total + bond_y * y_roll(centre, -1) + y_roll(bond_y, 1) * y_roll(centre, 1)
    bond_z = bond(2, lo + 1, lo + n - 1)
    total = total + bond_z * z_roll(centre, -1) + z_roll(bond_z, 1) * z_roll(centre, 1)
    return total


def local_kernel(halo, slab_rows, *refs):
    slab_refs = refs[:2 * HALO_SLABS + 1]
    start_ref, polar_ref, exchange_ref, relaxed_ref, last_ref, sums_ref, win, sweep_a, sweep_b, bonds_b, bonds_yr, bonds_zr, spins_b, t1, t2, t3 = refs[2 * HALO_SLABS + 1:]
    for k, slab_ref in enumerate(slab_refs):
        block = slab_ref[...]
        cos_polar, azimuth, bond_class = block[0], block[1], block[2:5]
        radial = jnp.sqrt(1.0 - cos_polar * cos_polar)
        strengths = jnp.zeros(bond_class.shape, jnp.float32)
        for class_index in range(NCLASS):
            strengths = jnp.where(bond_class == class_index, exchange_ref[class_index], strengths)
        site = jnp.stack([radial * jnp.cos(azimuth), radial * jnp.sin(azimuth), cos_polar], 0)
        win[:, :, k * slab_rows:(k + 1) * slab_rows, :] = jnp.concatenate([site, strengths], 0)
    width = len(slab_refs) * slab_rows

    def bond(d, a, b):
        return win[3 + d, :, a:b, :]

    def from_window(a, b):
        return win[0:3, :, a:b, :]

    first = halo - CHEB
    n_start = slab_rows + 2 * CHEB
    base_a = first

    def from_a(a, b):
        return sweep_a[:, :, a - base_a:b - base_a, :]

    sweep_a[:, :, 0:n_start, :] = relax_update(
        win[0:3, :, first:first + n_start, :], field_rows(from_window, bond, first - 1, n_start + 2)
    )
    sweep_b[:, :, 0:n_start - 2, :] = relax_update(
        sweep_a[:, :, 1:n_start - 1, :], field_rows(from_a, bond, first, n_start)
    )
    base_b = first + 1
    relaxed_ref[...] = sweep_b[:, :, halo - base_b:halo - base_b + slab_rows, :]
    lanes = win.shape[3]
    depth = win.shape[1]
    probes = start_ref.shape[3]
    for xr in range(n_start):
        w = first + xr
        site = jnp.broadcast_to(win[3:6, :, w:w + 1, :], (3, depth, probes, lanes))
        bonds_b[xr] = site
        bonds_yr[xr] = y_roll(site[1], 1)
        bonds_zr[xr] = z_roll(site[2], 1)
    for xr in range(n_start - 2):
        w = first + 1 + xr
        spins_b[xr] = jnp.broadcast_to(sweep_b[:, :, w - base_b:w - base_b + 1, :] * (-2.0 * precess_scale), (3, depth, probes, lanes))

    polar = [polar_ref[j] for j in range(3)]

    def start_row(i):
        wave = start_ref[i]
        return jnp.stack([wave * polar[j] for j in range(3)], 1)

    t_refs = (start_ref, t1, t2, t3, last_ref)
    for order in range(CHEB):
        lo = first + order
        n = n_start - 2 * order
        source = t_refs[order]
        target = t_refs[order + 1]
        acc = None
        for i in range(n - 2):
            w = lo + 1 + i
            b = w - first
            up = source[i + 2]
            down = source[i]
            centre = source[i + 1]
            total = bonds_b[b, 0] * up + bonds_b[b - 1, 0] * down
            total = total + bonds_b[b, 1] * y_roll(centre, -1) + bonds_yr[b] * y_roll(centre, 1)
            total = total + bonds_b[b, 2] * z_roll(centre, -1) + bonds_zr[b] * z_roll(centre, 1)
            if order == 0:
                spin = spins_b[b - 1]
                turn = (
                    spin[1] * polar[2] - spin[2] * polar[1],
                    spin[2] * polar[0] - spin[0] * polar[2],
                    spin[0] * polar[1] - spin[1] * polar[0],
                )
                advanced = jnp.stack([total * turn[j] for j in range(3)], 1) * 0.5
            else:
                previous = start_row(i + 2) if order == 1 else t_refs[order - 1][i + 2]
                advanced = cross_product(spins_b[b - 1], total) - previous
            target[i] = advanced.astype(target.dtype)
            if halo <= w < halo + slab_rows:
                squares = advanced * advanced
                part = squares[0] + squares[1]
                part = part[0] + part[1] + part[2]
                part = part[0] + part[1] + part[2] + part[3]
                acc = part if acc is None else acc + part
        sums_ref[order:order + 1, :] = jnp.sum(acc.T, axis=0, keepdims=True)


def run_local(slab_blocks, start, polar, exchange, halo, slab_rows):
    depth, lanes = slab_blocks[0].shape[1], slab_blocks[0].shape[3]
    width = len(slab_blocks) * slab_rows
    n_start, probes = start.shape[0], start.shape[3]
    vec_shape = (start.shape[1], 3) + start.shape[2:]

    def body(*refs):
        local_kernel(halo, slab_rows, *refs)

    sites = n_start * 3 * start[0].size
    return pl.pallas_call(
        body,
        out_shape=(
            jax.ShapeDtypeStruct((3, depth, slab_rows, lanes), jnp.float32),
            jax.ShapeDtypeStruct((slab_rows,) + vec_shape, jnp.bfloat16),
            jax.ShapeDtypeStruct((CHEB, probes), jnp.float32),
        ),
        in_specs=[pl.BlockSpec(memory_space=pltpu.VMEM)] * (len(slab_blocks) + 2)
        + [pl.BlockSpec(memory_space=pltpu.SMEM)],
        out_specs=[pl.BlockSpec(memory_space=pltpu.VMEM)] * 3,
        scratch_shapes=[
            pltpu.VMEM((6, depth, width, lanes), jnp.float32),
            pltpu.VMEM((3, depth, width, lanes), jnp.float32),
            pltpu.VMEM((3, depth, width, lanes), jnp.float32),
            pltpu.VMEM((n_start, 3, depth, probes, lanes), jnp.float32),
            pltpu.VMEM((n_start, depth, probes, lanes), jnp.float32),
            pltpu.VMEM((n_start, depth, probes, lanes), jnp.float32),
            pltpu.VMEM((n_start, 3, depth, probes, lanes), jnp.float32),
        ]
        + [pltpu.VMEM((n_start - 2 * k,) + vec_shape, jnp.float32) for k in range(1, CHEB)],
        cost_estimate=pl.CostEstimate(
            flops=30 * sites + 200 * 3 * depth * width * lanes,
            transcendentals=0,
            bytes_accessed=4 * (6 * depth * width * lanes + 2 * start.size),
        ),
    )(*slab_blocks, start, polar, exchange)


def shards(cos_polar, azimuth, bond_class, exchange, probe_wave):
    groups = lax.axis_size("probe")
    slabs = lax.axis_size("space")
    group = lax.axis_index("probe")
    slab = lax.axis_index("space")
    slab_rows = cos_polar.shape[1]
    block_y = cos_polar.shape[2]
    total_x = slab_rows * slabs
    total_y = block_y * groups
    site_count = total_x * total_y * LZ

    local = jnp.concatenate([cos_polar[None], azimuth[None], bond_class.astype(jnp.float32)], 0)

    pieces = [shifted(local, "probe", k) for k in range(groups)]
    rotated = jnp.concatenate(pieces, -1)
    full_y = jnp.roll(rotated, group * block_y, -1) if groups > 1 else rotated

    slab_blocks = [shifted(full_y, "space", k) for k in range(-HALO_SLABS, HALO_SLABS + 1)]
    halo = HALO_SLABS * slab_rows

    width = slab_rows + 2 * CHEB
    x_coords = (slab * slab_rows - CHEB + jnp.arange(width, dtype=jnp.int32)) % total_x
    y_coords = jnp.arange(total_y, dtype=jnp.int32)
    group_size = probe_wave.shape[0]
    probe_ids = group * group_size + jnp.arange(group_size, dtype=jnp.int32)
    waves, polar = make_probes(probe_wave, probe_ids, x_coords, y_coords, total_x, total_y, LZ)
    waves = jnp.transpose(waves, (3, 1, 2, 0, 4))
    polar = jnp.broadcast_to(polar.T[:, :, None], (3, group_size, total_y))

    relaxed, last, sums = run_local(slab_blocks, waves, polar, exchange, halo, slab_rows)
    relaxed_own = lax.dynamic_slice_in_dim(relaxed, group * block_y, block_y, -1)
    last = jnp.transpose(last, (4, 1, 2, 3, 0, 5))
    moment_rows = butterfly_sum(sums, "space") / site_count
    return (relaxed_own, last, moment_rows.T)


def solution(mesh):
    return jax.shard_map(
        shards,
        mesh=mesh,
        in_specs=(
            P(None, "space", "probe"),
            P(None, "space", "probe"),
            P(None, None, "space", "probe"),
            P(),
            P("probe", None),
        ),
        out_specs=(
            P(None, None, "space", "probe"),
            P("probe", None, None, None, "space", None),
            P("probe", None),
        ),
        check_vma=False,
    )
```
